32 devices in a mesh: leaf: 8 (over z, y), case: 4 (over x, core).
Axes of the slice: x: 2, y: 2, z: 4, core: 2. Of those that a mesh axis runs over, the one named last changes fastest.
Arguments:
- features: bfloat16 [8, 16384, 128], P('case', 'leaf'), may hold values from -6 to 6
- cotangent: bfloat16 [8, 16384, 128], P('case', 'leaf'), may hold values from -6 to 6
- kernel_blocks: bfloat16 [128, 12, 128, 128], P('leaf'), may hold values from -0.15625 to 0.15625
- near_pairs: int32 [128, 12], P('leaf'), may hold values from 0 to 127, as said below
- leaf_basis: bfloat16 [64, 16384], P(None, 'leaf'), may hold values from -0.125 to 0.125
- w_near: bfloat16 [128, 128], replicated, may hold values from -0.5 to 0.5
- w_far: bfloat16 [128, 128], replicated, may hold values from -0.5 to 0.5
- translations: float32 [3, 64, 64], replicated, may hold values from -0.75 to 0.75
Outputs:
- output: bfloat16 [8, 16384, 128], P('case', 'leaf')
- grad_features: bfloat16 [8, 16384, 128], P('case', 'leaf')
- grad_near: float32 [128, 128], replicated
- grad_far: float32 [128, 128], replicated
The draws below stay inside these ranges and needn't reach their ends.
Inputs may be any that keep to these rules, and one draw needn't show every extreme that they name: `near_pairs`: A target block held by one index of leaf names blocks of that index, or blocks at most 8 places beyond its first or last block; on every index both of these farthest blocks occur where they exist; 0 and 127 both occur.
All inputs are finite; a program needn't handle non-finite values.
Results may differ from the reference program's by a relative error of at most 0.0085.
Values may be sent and summed in bfloat16 or wider, within the bound.
No kernel may reach another device: no remote copies, remote signals or barrier semaphores. Data moves between devices by JAX's collectives and lax.ppermute only.
A program may use at most 128 MiB of HBM per device.

```python
import jax
import jax.numpy as jnp
from jax import lax

C = 128
R = 64
B = 128
K = 12
P_DEV = 2048
NB = 16
POINTS = 16384
NBLK = 128
CASES = 8
LEVELS = 3
N_LEAF = 8


def draw_near_pairs(key, part):
    half_reach = NB // 2
    row_ids = jnp.arange(NBLK, dtype=jnp.int32)
    owner_start = row_ids // NB * NB
    offsets = jax.random.randint(key, (NBLK, K), -half_reach, NB + half_reach, dtype=jnp.int32)
    column_ids = jnp.arange(K, dtype=jnp.int32)[None, :]
    first_row = (row_ids % NB == 0)[:, None]
    last_row = (row_ids % NB == NB - 1)[:, None]
    offsets = jnp.where(first_row & (column_ids == 1), -half_reach, offsets)
    offsets = jnp.where(last_row & (column_ids == 2), NB + half_reach - 1, offsets)
    source = owner_start[:, None] + offsets
    outside = (source < 0) | (source >= NBLK)
    source = jnp.where(outside, owner_start[:, None] + jnp.mod(offsets, NB), source)
    source = source.at[0, 0].set(0)
    source = source.at[NBLK - 1, 0].set(NBLK - 1)
    return source.astype(jnp.int32)


def levels(own_key, shape, shards, smallest, largest):
    def one(dim, shards_of):
        draws = jax.random.uniform(jax.random.fold_in(jax.random.fold_in(own_key, 6), dim), (shards_of,), jnp.float32, smallest / len(shards), largest / len(shards))
        return jnp.repeat(jnp.exp(draws), shape[dim] // shards_of).reshape((-1,) + (1,) * (len(shape) - dim - 1))

    loudness = one(*shards[0])
    for cut in shards[1:]:
        loudness = loudness * one(*cut)
    return loudness


def centred(stream_key, dims, spread, bound, cuts=(), kind=jnp.bfloat16):
    factor_of = levels(stream_key, dims, cuts, -0.22, 0.18) if cuts else 1.0
    array = jax.random.normal(stream_key, dims, jnp.float32) * spread * factor_of
    return jnp.minimum(jnp.maximum(array, -bound), bound).astype(kind)


def setup_inputs(seed: int = 0) -> dict:
    keys = jax.random.split(jax.random.key(seed), 9)
    features = centred(keys[0], (CASES, POINTS, C), 1.0, 6.0, ((0, 4), (1, 8)))
    cotangent = centred(keys[1], (CASES, POINTS, C), 1.0, 6.0, ((0, 4), (1, 8)))
    kernel_blocks = centred(keys[2], (NBLK, K, B, B), (B * K) ** -0.5, 0.15625, ((0, 8),))
    near_pairs = draw_near_pairs(jax.random.fold_in(keys[8], 71), 0)
    leaf_basis = centred(keys[4], (R, POINTS), P_DEV ** -0.5, 0.125, ((1, 8),))
    w_near = centred(keys[5], (C, C), C ** -0.5, 0.5)
    w_far = centred(keys[6], (C, C), C ** -0.5, 0.5)
    translations = centred(keys[7], (LEVELS, R, R), R ** -0.5, 0.75, (), jnp.float32)
    return dict(features=features, cotangent=cotangent, kernel_blocks=kernel_blocks, near_pairs=near_pairs, leaf_basis=leaf_basis, w_near=w_near, w_far=w_far, translations=translations)


def tree_terms(leaf_values, translations, flipped):
    leaf_count = leaf_values.shape[0]
    summed = jnp.zeros(leaf_values.shape, jnp.float32)
    for height in range(LEVELS):
        stride = 2 ** height
        groups = leaf_values.reshape((leaf_count // stride, stride) + leaf_values.shape[1:]).sum(axis=1)
        swapped = groups.reshape((leaf_count // (2 * stride), 2) + groups.shape[1:])[:, ::-1]
        swapped = swapped.reshape(groups.shape)
        sibling = jnp.repeat(swapped, stride, axis=0)
        matrix = translations[height].T if flipped else translations[height]
        summed = summed + jnp.einsum('rs,lasc->larc', matrix, sibling, precision=lax.Precision.HIGHEST)
    return summed

def reference(features, cotangent, kernel_blocks, near_pairs, leaf_basis, w_near, w_far, translations):
    hp = lax.Precision.HIGHEST
    block_view = features.reshape(CASES, NBLK, B, C)
    pair_groups = near_pairs.reshape(N_LEAF, NB, K)
    kernel_groups = kernel_blocks.reshape(N_LEAF, NB, K, B, B)

    def near_group(items):
        indices, kernels = items
        picked = block_view[:, indices].astype(jnp.float32)
        return jnp.einsum('bkij,abkjc->abic', kernels.astype(jnp.float32), picked, precision=hp)
    near_sum = lax.map(near_group, (pair_groups, kernel_groups))
    near_bf = near_sum.transpose(1, 0, 2, 3, 4).reshape(CASES, POINTS, C).astype(jnp.bfloat16)
    basis_view = leaf_basis.astype(jnp.float32).reshape(R, N_LEAF, P_DEV)
    feature_view = features.astype(jnp.float32).reshape(CASES, N_LEAF, P_DEV, C)
    summary = jnp.einsum('rlp,alpc->larc', basis_view, feature_view, precision=hp)
    expansion = tree_terms(summary, translations, False)
    exp_bf = expansion.astype(jnp.bfloat16)
    far_coeff = jnp.einsum('larc,cd->lard', exp_bf.astype(jnp.float32), w_far.astype(jnp.float32), precision=hp).astype(jnp.bfloat16)
    far_field = jnp.einsum('rlp,lard->alpd', basis_view, far_coeff.astype(jnp.float32), precision=hp).reshape(CASES, POINTS, C)
    mixed = jnp.einsum('apc,cd->apd', near_bf.astype(jnp.float32), w_near.astype(jnp.float32), precision=hp) + far_field
    output = jax.nn.gelu(mixed).astype(jnp.bfloat16)
    _, pullback = jax.vjp(jax.nn.gelu, mixed)
    slope = pullback(cotangent.astype(jnp.float32))[0].astype(jnp.bfloat16)
    slope_view = slope.astype(jnp.float32).reshape(CASES, N_LEAF, P_DEV, C)
    projected = jnp.einsum('rlp,alpc->larc', basis_view, slope_view, precision=hp).astype(jnp.bfloat16)
    back_coeff = jnp.einsum('larc,dc->lard', projected.astype(jnp.float32), w_far.astype(jnp.float32), precision=hp)
    back_exp = tree_terms(back_coeff, translations, True)
    back_far = jnp.einsum('rlp,larc->alpc', basis_view, back_exp.astype(jnp.bfloat16).astype(jnp.float32), precision=hp).reshape(CASES, POINTS, C)
    back_near = jnp.einsum('apc,dc->apd', slope.astype(jnp.float32), w_near.astype(jnp.float32), precision=hp).astype(jnp.bfloat16)
    back_view = back_near.reshape(CASES, N_LEAF, NB, B, C).transpose(1, 0, 2, 3, 4)

    def scatter_group(landed, items):
        indices, kernels, back_blocks = items
        contrib = jnp.einsum('bkij,abic->bkajc', kernels.astype(jnp.float32), back_blocks.astype(jnp.float32), precision=hp)
        landed = landed.at[indices.reshape(-1)].add(contrib.reshape(NB * K, CASES, B, C))
        return (landed, None)
    landed, _ = lax.scan(scatter_group, jnp.zeros((NBLK, CASES, B, C), jnp.float32), (pair_groups, kernel_groups, back_view))
    back_near_sum = landed.transpose(1, 0, 2, 3).reshape(CASES, POINTS, C)
    grad_features = (back_near_sum + back_far).astype(jnp.bfloat16)
    scale = 1.0 / jnp.sqrt(jnp.float32(CASES * POINTS))
    grad_near = jnp.einsum('apc,apd->cd', near_bf.astype(jnp.float32), slope.astype(jnp.float32), precision=hp) * scale
    grad_far = jnp.einsum('larc,lard->cd', exp_bf.astype(jnp.float32), projected.astype(jnp.float32), precision=hp) * scale
    return (output, grad_features, grad_near, grad_far)
```

```python
import functools
import math

import jax
import jax.numpy as jnp
from jax import lax
from jax.experimental import pallas as pl
from jax.experimental.pallas import tpu as pltpu
from jax.sharding import PartitionSpec as P

HALO = 8
TB = 4


def partner(shard, axis, apart):
    return lax.ppermute(shard, axis, [(i, i ^ 1 << apart) for i in range(lax.axis_size(axis))])


def shifted(value, axis, steps):
    count = lax.axis_size(axis)
    leading, last = (max(0, -steps), min(count, count - steps))
    return lax.ppermute(value, axis, [(source, source + steps) for source in range(leading, last)])


def apply_level(matrix, sibling, flipped):
    if flipped:
        return jnp.einsum("sr,asc->arc", matrix, sibling, precision=lax.Precision.HIGHEST)
    return jnp.einsum("rs,asc->arc", matrix, sibling, precision=lax.Precision.HIGHEST)


def expand(own_value, translations, flipped, rider=None):
    depth_count = lax.axis_size("leaf").bit_length() - 1
    summed = jnp.zeros(own_value.shape, jnp.float32)
    node_value = own_value
    rows = own_value.shape[0] * own_value.shape[1]
    for height in range(depth_count):
        if rider is None:
            sibling = partner(node_value, "leaf", height)
        else:
            packed = jnp.concatenate(
                [node_value.reshape(rows, own_value.shape[2]), rider], axis=0
            )
            got = partner(packed, "leaf", height)
            sibling = got[:rows].reshape(own_value.shape)
            rider = rider + got[rows:]
        summed = summed + apply_level(translations[height], sibling, flipped)
        node_value = node_value + sibling
    return summed, rider


def near_fwd_kernel(cases, pairs, rows, ids_ref, kb_ref, ext_ref, out_ref):
    g = pl.program_id(0)
    for tb in range(TB):
        t = g * TB + tb
        lhs = jnp.concatenate([kb_ref[tb, k] for k in range(pairs)], axis=1)
        parts = []
        for k in range(pairs):
            start = pl.multiple_of(ids_ref[t * pairs + k] * rows, rows)
            parts.append(
                jnp.concatenate([ext_ref[c, pl.ds(start, rows), :] for c in range(cases)], axis=1)
            )
        rhs = jnp.concatenate(parts, axis=0)
        acc = jnp.dot(lhs, rhs, preferred_element_type=jnp.float32)
        width = acc.shape[1] // cases
        for c in range(cases):
            out_ref[c, pl.ds(tb * rows, rows), :] = acc[:, c * width : (c + 1) * width].astype(
                out_ref.dtype
            )


def near_forward(ids, kernel_blocks, extended):
    cases, span_points, width = extended.shape
    blocks_here, pairs, rows, _ = kernel_blocks.shape
    steps = blocks_here // TB
    flops = 2 * blocks_here * pairs * rows * rows * cases * width
    return pl.pallas_call(
        functools.partial(near_fwd_kernel, cases, pairs, rows),
        out_shape=jax.ShapeDtypeStruct((cases, blocks_here * rows, width), jnp.bfloat16),
        grid_spec=pltpu.PrefetchScalarGridSpec(
            num_scalar_prefetch=1,
            grid=(steps,),
            in_specs=[
                pl.BlockSpec((TB, pairs, rows, rows), lambda g, ids: (g, 0, 0, 0)),
                pl.BlockSpec((cases, span_points, width), lambda g, ids: (0, 0, 0)),
            ],
            out_specs=pl.BlockSpec((cases, TB * rows, width), lambda g, ids: (0, g, 0)),
        ),
        compiler_params=pltpu.CompilerParams(dimension_semantics=("arbitrary",)),
        cost_estimate=pl.CostEstimate(
            flops=flops,
            transcendentals=0,
            bytes_accessed=kernel_blocks.size * 2 + extended.size * 2 + cases * blocks_here * rows * width * 2,
        ),
    )(ids, kernel_blocks, extended)


def near_bwd_kernel(cases, pairs, rows, steps, ids_ref, kb_ref, back_ref, mid_ref, lo_ref, hi_ref, acc_ref):
    g = pl.program_id(0)

    @pl.when(g == 0)
    def _():
        acc_ref[...] = jnp.zeros(acc_ref.shape, acc_ref.dtype)

    width = back_ref.shape[2]
    for tb in range(TB):
        t = g * TB + tb
        lhs = jnp.concatenate([kb_ref[tb, k] for k in range(pairs)], axis=1)
        rhs = jnp.concatenate(
            [back_ref[c, pl.ds(tb * rows, rows), :] for c in range(cases)], axis=1
        )
        res = lax.dot_general(
            lhs, rhs, (((0,), (0,)), ((), ())), preferred_element_type=jnp.float32
        )
        for k in range(pairs):
            start = pl.multiple_of(ids_ref[t * pairs + k] * rows, rows)
            piece = res[k * rows : (k + 1) * rows]
            for c in range(cases):
                acc_ref[c, pl.ds(start, rows), :] += piece[:, c * width : (c + 1) * width]

    @pl.when(g == steps - 1)
    def _():
        halo_points = lo_ref.shape[1]
        mid_points = mid_ref.shape[1]
        lo_ref[...] = acc_ref[:, :halo_points, :].astype(lo_ref.dtype)
        mid_ref[...] = acc_ref[:, halo_points : halo_points + mid_points, :]
        hi_ref[...] = acc_ref[:, halo_points + mid_points :, :].astype(hi_ref.dtype)


def near_backward(ids, kernel_blocks, back_near, halo_points):
    cases, points_here, width = back_near.shape
    blocks_here, pairs, rows, _ = kernel_blocks.shape
    steps = blocks_here // TB
    span_points = points_here + 2 * halo_points
    flops = 2 * blocks_here * pairs * rows * rows * cases * width
    return pl.pallas_call(
        functools.partial(near_bwd_kernel, cases, pairs, rows, steps),
        out_shape=(
            jax.ShapeDtypeStruct((cases, points_here, width), jnp.float32),
            jax.ShapeDtypeStruct((cases, halo_points, width), jnp.bfloat16),
            jax.ShapeDtypeStruct((cases, halo_points, width), jnp.bfloat16),
        ),
        grid_spec=pltpu.PrefetchScalarGridSpec(
            num_scalar_prefetch=1,
            grid=(steps,),
            in_specs=[
                pl.BlockSpec((TB, pairs, rows, rows), lambda g, ids: (g, 0, 0, 0)),
                pl.BlockSpec((cases, TB * rows, width), lambda g, ids: (0, g, 0)),
            ],
            out_specs=[
                pl.BlockSpec((cases, points_here, width), lambda g, ids: (0, 0, 0)),
                pl.BlockSpec((cases, halo_points, width), lambda g, ids: (0, 0, 0)),
                pl.BlockSpec((cases, halo_points, width), lambda g, ids: (0, 0, 0)),
            ],
            scratch_shapes=[pltpu.VMEM((cases, span_points, width), jnp.float32)],
        ),
        compiler_params=pltpu.CompilerParams(
            dimension_semantics=("arbitrary",), vmem_limit_bytes=60 * 1024 * 1024
        ),
        cost_estimate=pl.CostEstimate(
            flops=flops,
            transcendentals=0,
            bytes_accessed=kernel_blocks.size * 2 + back_near.size * 2 + cases * span_points * width * 4,
        ),
    )(ids, kernel_blocks, back_near)


def on_device(
    features, cotangent, kernel_blocks, near_pairs, leaf_basis, w_near, w_far, translations
):
    cases_here, points_here, width = features.shape
    blocks_here, pair_count, block_rows = (
        kernel_blocks.shape[0],
        kernel_blocks.shape[1],
        kernel_blocks.shape[2],
    )
    halo_points = HALO * block_rows
    span_blocks = blocks_here + 2 * HALO
    position = lax.axis_index("leaf")

    head = features[:, :halo_points]
    tail = features[:, points_here - halo_points :]
    from_prev = shifted(tail, "leaf", 1)
    from_next = shifted(head, "leaf", -1)
    extended = jnp.concatenate([from_prev, features, from_next], axis=1)
    local_ids = jnp.clip(
        near_pairs - (position * blocks_here - HALO), 0, span_blocks - 1
    ).reshape(-1).astype(jnp.int32)

    near_bf = near_forward(local_ids, kernel_blocks, extended)

    summary = jnp.einsum("rp,apc->arc", leaf_basis, features, preferred_element_type=jnp.float32)
    expansion, _ = expand(summary, translations, False)
    exp_bf = expansion.astype(jnp.bfloat16)
    far_coeff = jnp.einsum("arc,cd->ard", exp_bf, w_far, preferred_element_type=jnp.float32).astype(
        jnp.bfloat16
    )
    far_field = jnp.einsum("rp,ard->apd", leaf_basis, far_coeff, preferred_element_type=jnp.float32)
    mixed = (
        jnp.einsum("apc,cd->apd", near_bf, w_near, preferred_element_type=jnp.float32) + far_field
    )
    output = jax.nn.gelu(mixed).astype(jnp.bfloat16)
    _, pullback = jax.vjp(jax.nn.gelu, mixed)
    slope = pullback(cotangent.astype(jnp.float32))[0].astype(jnp.bfloat16)
    projected = jnp.einsum(
        "rp,apc->arc", leaf_basis, slope, preferred_element_type=jnp.float32
    ).astype(jnp.bfloat16)
    back_near = jnp.einsum("apc,dc->apd", slope, w_near, preferred_element_type=jnp.float32).astype(
        jnp.bfloat16
    )

    mid, lo, hi = near_backward(local_ids, kernel_blocks, back_near, halo_points)

    scale = 1.0 / math.sqrt(
        cases_here * lax.axis_size("case") * points_here * lax.axis_size("leaf")
    )
    near_term = (
        jnp.einsum("apc,apd->cd", near_bf, slope, preferred_element_type=jnp.float32) * scale
    )
    far_term = (
        jnp.einsum("arc,ard->cd", exp_bf, projected, preferred_element_type=jnp.float32) * scale
    )
    grads = jnp.concatenate([near_term, far_term], axis=0)

    back_coeff = jnp.einsum("arc,dc->ard", projected, w_far, preferred_element_type=jnp.float32)
    back_exp, grads = expand(back_coeff, translations, True, rider=grads)
    back_far = jnp.einsum(
        "rp,arc->apc", leaf_basis, back_exp.astype(jnp.bfloat16), preferred_element_type=jnp.float32
    )

    case_depth = lax.axis_size("case").bit_length() - 1
    for height in range(case_depth):
        grads = grads + partner(grads, "case", height)

    got_prev = shifted(hi, "leaf", 1).astype(jnp.float32)
    got_next = shifted(lo, "leaf", -1).astype(jnp.float32)
    near_back = jnp.concatenate(
        [
            mid[:, :halo_points] + got_prev,
            mid[:, halo_points : points_here - halo_points],
            mid[:, points_here - halo_points :] + got_next,
        ],
        axis=1,
    )
    grad_features = (near_back + back_far).astype(jnp.bfloat16)
    grad_near = grads[:width]
    grad_far = grads[width:]
    return (output, grad_features, grad_near, grad_far)


def solution(mesh):
    return jax.shard_map(
        on_device,
        mesh=mesh,
        in_specs=(
            P("case", "leaf", None),
            P("case", "leaf", None),
            P("leaf", None, None, None),
            P("leaf", None),
            P(None, "leaf"),
            P(),
            P(),
            P(),
        ),
        out_specs=(P("case", "leaf", None), P("case", "leaf", None), P(), P()),
        check_vma=False,
    )
```

```python
import functools
import math

import jax
import jax.numpy as jnp
from jax import lax
from jax.experimental import pallas as pl
from jax.experimental.pallas import tpu as pltpu
from jax.sharding import PartitionSpec as P

HALO = 8
TB = 4


def partner(shard, axis, apart):
    return lax.ppermute(shard, axis, [(i, i ^ 1 << apart) for i in range(lax.axis_size(axis))])


def shifted(value, axis, steps):
    count = lax.axis_size(axis)
    leading, last = (max(0, -steps), min(count, count - steps))
    return lax.ppermute(value, axis, [(source, source + steps) for source in range(leading, last)])


def apply_level(matrix, sibling, flipped):
    if flipped:
        return jnp.einsum("sr,asc->arc", matrix, sibling, precision=lax.Precision.HIGHEST)
    return jnp.einsum("rs,asc->arc", matrix, sibling, precision=lax.Precision.HIGHEST)


def expand(own_value, translations, flipped, rider=None):
    depth_count = lax.axis_size("leaf").bit_length() - 1
    summed = jnp.zeros(own_value.shape, jnp.float32)
    node_value = own_value
    rows = own_value.shape[0] * own_value.shape[1]
    for height in range(depth_count):
        if rider is None:
            sibling = partner(node_value, "leaf", height)
        else:
            packed = jnp.concatenate(
                [node_value.reshape(rows, own_value.shape[2]), rider], axis=0
            )
            got = partner(packed, "leaf", height)
            sibling = got[:rows].reshape(own_value.shape)
            rider = rider + got[rows:]
        summed = summed + apply_level(translations[height], sibling, flipped)
        node_value = node_value + sibling
    return summed, rider


def near_fwd_kernel(cases, pairs, rows, ids_ref, kb_ref, ext_ref, out_ref):
    g = pl.program_id(0)
    for tb in range(TB):
        t = g * TB + tb
        lhs = jnp.concatenate([kb_ref[tb, k] for k in range(pairs)], axis=1)
        parts = []
        for k in range(pairs):
            start = pl.multiple_of(ids_ref[t * pairs + k] * rows, rows)
            parts.append(
                jnp.concatenate([ext_ref[c, pl.ds(start, rows), :] for c in range(cases)], axis=1)
            )
        rhs = jnp.concatenate(parts, axis=0)
        acc = jnp.dot(lhs, rhs, preferred_element_type=jnp.float32)
        width = acc.shape[1] // cases
        for c in range(cases):
            out_ref[c, pl.ds(tb * rows, rows), :] = acc[:, c * width : (c + 1) * width].astype(
                out_ref.dtype
            )


def near_forward(ids, kernel_blocks, extended):
    cases, span_points, width = extended.shape
    blocks_here, pairs, rows, _ = kernel_blocks.shape
    steps = blocks_here // TB
    flops = 2 * blocks_here * pairs * rows * rows * cases * width
    return pl.pallas_call(
        functools.partial(near_fwd_kernel, cases, pairs, rows),
        out_shape=jax.ShapeDtypeStruct((cases, blocks_here * rows, width), jnp.bfloat16),
        grid_spec=pltpu.PrefetchScalarGridSpec(
            num_scalar_prefetch=1,
            grid=(steps,),
            in_specs=[
                pl.BlockSpec((TB, pairs, rows, rows), lambda g, ids: (g, 0, 0, 0)),
                pl.BlockSpec((cases, span_points, width), lambda g, ids: (0, 0, 0)),
            ],
            out_specs=pl.BlockSpec((cases, TB * rows, width), lambda g, ids: (0, g, 0)),
        ),
        compiler_params=pltpu.CompilerParams(dimension_semantics=("arbitrary",)),
        cost_estimate=pl.CostEstimate(
            flops=flops,
            transcendentals=0,
            bytes_accessed=kernel_blocks.size * 2 + extended.size * 2 + cases * blocks_here * rows * width * 2,
        ),
    )(ids, kernel_blocks, extended)


def near_bwd_kernel(cases, pairs, rows, steps, ids_ref, kb_ref, back_ref, mid_ref, lo_ref, hi_ref, acc_ref):
    g = pl.program_id(0)

    @pl.when(g == 0)
    def _():
        acc_ref[...] = jnp.zeros(acc_ref.shape, acc_ref.dtype)

    width = back_ref.shape[2]
    for tb in range(TB):
        t = g * TB + tb
        lhs = jnp.concatenate([kb_ref[tb, k] for k in range(pairs)], axis=1)
        rhs = jnp.concatenate(
            [back_ref[c, pl.ds(tb * rows, rows), :] for c in range(cases)], axis=1
        )
        res = lax.dot_general(
            lhs, rhs, (((0,), (0,)), ((), ())), preferred_element_type=jnp.float32
        )
        for k in range(pairs):
            start = pl.multiple_of(ids_ref[t * pairs + k] * rows, rows)
            piece = res[k * rows : (k + 1) * rows]
            for c in range(cases):
                acc_ref[c, pl.ds(start, rows), :] += piece[:, c * width : (c + 1) * width]

    @pl.when(g == steps - 1)
    def _():
        halo_points = lo_ref.shape[1]
        mid_points = mid_ref.shape[1]
        lo_ref[...] = acc_ref[:, :halo_points, :].astype(lo_ref.dtype)
        mid_ref[...] = acc_ref[:, halo_points : halo_points + mid_points, :]
        hi_ref[...] = acc_ref[:, halo_points + mid_points :, :].astype(hi_ref.dtype)


def near_backward(ids, kernel_blocks, back_near, halo_points):
    cases, points_here, width = back_near.shape
    blocks_here, pairs, rows, _ = kernel_blocks.shape
    steps = blocks_here // TB
    span_points = points_here + 2 * halo_points
    flops = 2 * blocks_here * pairs * rows * rows * cases * width
    return pl.pallas_call(
        functools.partial(near_bwd_kernel, cases, pairs, rows, steps),
        out_shape=(
            jax.ShapeDtypeStruct((cases, points_here, width), jnp.float32),
            jax.ShapeDtypeStruct((cases, halo_points, width), jnp.bfloat16),
            jax.ShapeDtypeStruct((cases, halo_points, width), jnp.bfloat16),
        ),
        grid_spec=pltpu.PrefetchScalarGridSpec(
            num_scalar_prefetch=1,
            grid=(steps,),
            in_specs=[
                pl.BlockSpec((TB, pairs, rows, rows), lambda g, ids: (g, 0, 0, 0)),
                pl.BlockSpec((cases, TB * rows, width), lambda g, ids: (0, g, 0)),
            ],
            out_specs=[
                pl.BlockSpec((cases, points_here, width), lambda g, ids: (0, 0, 0)),
                pl.BlockSpec((cases, halo_points, width), lambda g, ids: (0, 0, 0)),
                pl.BlockSpec((cases, halo_points, width), lambda g, ids: (0, 0, 0)),
            ],
            scratch_shapes=[pltpu.VMEM((cases, span_points, width), jnp.float32)],
        ),
        compiler_params=pltpu.CompilerParams(
            dimension_semantics=("arbitrary",), vmem_limit_bytes=60 * 1024 * 1024
        ),
        cost_estimate=pl.CostEstimate(
            flops=flops,
            transcendentals=0,
            bytes_accessed=kernel_blocks.size * 2 + back_near.size * 2 + cases * span_points * width * 4,
        ),
    )(ids, kernel_blocks, back_near)


def on_device(
    features, cotangent, kernel_blocks, near_pairs, leaf_basis, w_near, w_far, translations
):
    cases_here, points_here, width = features.shape
    blocks_here, pair_count, block_rows = (
        kernel_blocks.shape[0],
        kernel_blocks.shape[1],
        kernel_blocks.shape[2],
    )
    halo_points = HALO * block_rows
    span_blocks = blocks_here + 2 * HALO
    position = lax.axis_index("leaf")

    head = features[:, :halo_points]
    tail = features[:, points_here - halo_points :]
    from_prev = shifted(tail, "leaf", 1)
    from_next = shifted(head, "leaf", -1)
    extended = jnp.concatenate([from_prev, features, from_next], axis=1)
    local_ids = jnp.clip(
        near_pairs - (position * blocks_here - HALO), 0, span_blocks - 1
    ).reshape(-1).astype(jnp.int32)

    near_bf = near_forward(local_ids, kernel_blocks, extended)

    summary = jnp.einsum("rp,apc->arc", leaf_basis, features, preferred_element_type=jnp.float32)
    expansion, _ = expand(summary, translations, False)
    exp_bf = expansion.astype(jnp.bfloat16)
    far_coeff = jnp.einsum("arc,cd->ard", exp_bf, w_far, preferred_element_type=jnp.float32).astype(
        jnp.bfloat16
    )
    far_field = jnp.einsum("rp,ard->apd", leaf_basis, far_coeff, preferred_element_type=jnp.float32)
    mixed = (
        jnp.einsum("apc,cd->apd", near_bf, w_near, preferred_element_type=jnp.float32) + far_field
    )
    output = jax.nn.gelu(mixed).astype(jnp.bfloat16)
    _, pullback = jax.vjp(jax.nn.gelu, mixed)
    slope = pullback(cotangent.astype(jnp.float32))[0].astype(jnp.bfloat16)
    projected = jnp.einsum(
        "rp,apc->arc", leaf_basis, slope, preferred_element_type=jnp.float32
    ).astype(jnp.bfloat16)
    back_near = jnp.einsum("apc,dc->apd", slope, w_near, preferred_element_type=jnp.float32).astype(
        jnp.bfloat16
    )

    mid, lo, hi = near_backward(local_ids, kernel_blocks, back_near, halo_points)

    scale = 1.0 / math.sqrt(
        cases_here * lax.axis_size("case") * points_here * lax.axis_size("leaf")
    )
    near_term = (
        jnp.einsum("apc,apd->cd", near_bf, slope, preferred_element_type=jnp.float32) * scale
    )
    far_term = (
        jnp.einsum("arc,ard->cd", exp_bf, projected, preferred_element_type=jnp.float32) * scale
    )
    grads = jnp.concatenate([near_term, far_term], axis=0)

    case_depth = lax.axis_size("case").bit_length() - 1
    for height in range(case_depth):
        grads = grads + partner(grads, "case", height)
    leaf_depth = lax.axis_size("leaf").bit_length() - 1
    for height in range(leaf_depth):
        grads = grads + partner(grads, "leaf", height)

    back_coeff = jnp.einsum("arc,dc->ard", projected, w_far, preferred_element_type=jnp.float32)
    back_exp, _ = expand(back_coeff, translations, True)
    back_far = jnp.einsum(
        "rp,arc->apc", leaf_basis, back_exp.astype(jnp.bfloat16), preferred_element_type=jnp.float32
    )

    got_prev = shifted(hi, "leaf", 1).astype(jnp.float32)
    got_next = shifted(lo, "leaf", -1).astype(jnp.float32)
    near_back = jnp.concatenate(
        [
            mid[:, :halo_points] + got_prev,
            mid[:, halo_points : points_here - halo_points],
            mid[:, points_here - halo_points :] + got_next,
        ],
        axis=1,
    )
    grad_features = (near_back + back_far).astype(jnp.bfloat16)
    grad_near = grads[:width]
    grad_far = grads[width:]
    return (output, grad_features, grad_near, grad_far)


def solution(mesh):
    return jax.shard_map(
        on_device,
        mesh=mesh,
        in_specs=(
            P("case", "leaf", None),
            P("case", "leaf", None),
            P("leaf", None, None, None),
            P("leaf", None),
            P(None, "leaf"),
            P(),
            P(),
            P(),
        ),
        out_specs=(P("case", "leaf", None), P("case", "leaf", None), P(), P()),
        check_vma=False,
    )
```

```python
import functools
import math

import jax
import jax.numpy as jnp
from jax import lax
from jax.experimental import pallas as pl
from jax.experimental.pallas import tpu as pltpu
from jax.sharding import PartitionSpec as P

HALO = 8
TB = 4


def partner(shard, axis, apart):
    return lax.ppermute(shard, axis, [(i, i ^ 1 << apart) for i in range(lax.axis_size(axis))])


def shifted(value, axis, steps):
    count = lax.axis_size(axis)
    leading, last = (max(0, -steps), min(count, count - steps))
    return lax.ppermute(value, axis, [(source, source + steps) for source in range(leading, last)])


def split3(x):
    hi = lax.reduce_precision(x, exponent_bits=8, mantissa_bits=7)
    rest = x - hi
    mid = lax.reduce_precision(rest, exponent_bits=8, mantissa_bits=7)
    lo = rest - mid
    return jnp.concatenate(
        [hi.astype(jnp.bfloat16), mid.astype(jnp.bfloat16), lo.astype(jnp.bfloat16)], axis=0
    )


def join3(parts):
    n = parts.shape[0] // 3
    return (parts[:n].astype(jnp.float32) + parts[n : 2 * n].astype(jnp.float32)) + parts[
        2 * n :
    ].astype(jnp.float32)


def neighbour_exchange(down_payload, up_payload, rider):
    parts = split3(rider)
    n = down_payload.shape[0]
    got_next = shifted(jnp.concatenate([down_payload, parts], axis=0), "leaf", -1)
    got_prev = shifted(jnp.concatenate([up_payload, parts], axis=0), "leaf", 1)
    even = lax.axis_index("leaf") % 2 == 0
    sib = join3(jnp.where(even, got_next[n:], got_prev[n:]))
    return got_next[:n], got_prev[:n], sib, join3(parts)


def apply_level(matrix, sibling, flipped):
    if flipped:
        return jnp.einsum("sr,asc->arc", matrix, sibling, precision=lax.Precision.HIGHEST)
    return jnp.einsum("rs,asc->arc", matrix, sibling, precision=lax.Precision.HIGHEST)


def expand(own_value, translations, flipped, sibling0, rider=None):
    depth_count = lax.axis_size("leaf").bit_length() - 1
    summed = apply_level(translations[0], sibling0, flipped)
    node_value = own_value + sibling0
    rows = own_value.shape[0] * own_value.shape[1]
    for height in range(1, depth_count):
        if rider is None:
            sibling = partner(node_value, "leaf", height)
        else:
            packed = jnp.concatenate(
                [node_value.reshape(rows, own_value.shape[2]), rider], axis=0
            )
            got = partner(packed, "leaf", height)
            sibling = got[:rows].reshape(own_value.shape)
            rider = rider + got[rows:]
        summed = summed + apply_level(translations[height], sibling, flipped)
        node_value = node_value + sibling
    return summed, rider


def near_fwd_kernel(cases, pairs, rows, ids_ref, kb_ref, ext_ref, out_ref):
    g = pl.program_id(0)
    for tb in range(TB):
        t = g * TB + tb
        lhs = jnp.concatenate([kb_ref[tb, k] for k in range(pairs)], axis=1)
        parts = []
        for k in range(pairs):
            start = pl.multiple_of(ids_ref[t * pairs + k] * rows, rows)
            parts.append(
                jnp.concatenate([ext_ref[c, pl.ds(start, rows), :] for c in range(cases)], axis=1)
            )
        rhs = jnp.concatenate(parts, axis=0)
        acc = jnp.dot(lhs, rhs, preferred_element_type=jnp.float32)
        width = acc.shape[1] // cases
        for c in range(cases):
            out_ref[c, pl.ds(tb * rows, rows), :] = acc[:, c * width : (c + 1) * width].astype(
                out_ref.dtype
            )


def near_forward(ids, kernel_blocks, extended):
    cases, span_points, width = extended.shape
    blocks_here, pairs, rows, _ = kernel_blocks.shape
    steps = blocks_here // TB
    flops = 2 * blocks_here * pairs * rows * rows * cases * width
    return pl.pallas_call(
        functools.partial(near_fwd_kernel, cases, pairs, rows),
        out_shape=jax.ShapeDtypeStruct((cases, blocks_here * rows, width), jnp.bfloat16),
        grid_spec=pltpu.PrefetchScalarGridSpec(
            num_scalar_prefetch=1,
            grid=(steps,),
            in_specs=[
                pl.BlockSpec((TB, pairs, rows, rows), lambda g, ids: (g, 0, 0, 0)),
                pl.BlockSpec((cases, span_points, width), lambda g, ids: (0, 0, 0)),
            ],
            out_specs=pl.BlockSpec((cases, TB * rows, width), lambda g, ids: (0, g, 0)),
        ),
        compiler_params=pltpu.CompilerParams(dimension_semantics=("arbitrary",)),
        cost_estimate=pl.CostEstimate(
            flops=flops,
            transcendentals=0,
            bytes_accessed=kernel_blocks.size * 2 + extended.size * 2 + cases * blocks_here * rows * width * 2,
        ),
    )(ids, kernel_blocks, extended)


def near_bwd_kernel(cases, pairs, rows, steps, ids_ref, kb_ref, back_ref, mid_ref, lo_ref, hi_ref, acc_ref):
    g = pl.program_id(0)

    @pl.when(g == 0)
    def _():
        acc_ref[...] = jnp.zeros(acc_ref.shape, acc_ref.dtype)

    width = back_ref.shape[2]
    for tb in range(TB):
        t = g * TB + tb
        lhs = jnp.concatenate([kb_ref[tb, k] for k in range(pairs)], axis=1)
        rhs = jnp.concatenate(
            [back_ref[c, pl.ds(tb * rows, rows), :] for c in range(cases)], axis=1
        )
        res = lax.dot_general(
            lhs, rhs, (((0,), (0,)), ((), ())), preferred_element_type=jnp.float32
        )
        for k in range(pairs):
            start = pl.multiple_of(ids_ref[t * pairs + k] * rows, rows)
            piece = res[k * rows : (k + 1) * rows]
            for c in range(cases):
                acc_ref[c, pl.ds(start, rows), :] += piece[:, c * width : (c + 1) * width]

    @pl.when(g == steps - 1)
    def _():
        halo_points = lo_ref.shape[1]
        mid_points = mid_ref.shape[1]
        lo_ref[...] = acc_ref[:, :halo_points, :].astype(lo_ref.dtype)
        mid_ref[...] = acc_ref[:, halo_points : halo_points + mid_points, :]
        hi_ref[...] = acc_ref[:, halo_points + mid_points :, :].astype(hi_ref.dtype)


def near_backward(ids, kernel_blocks, back_near, halo_points):
    cases, points_here, width = back_near.shape
    blocks_here, pairs, rows, _ = kernel_blocks.shape
    steps = blocks_here // TB
    span_points = points_here + 2 * halo_points
    flops = 2 * blocks_here * pairs * rows * rows * cases * width
    return pl.pallas_call(
        functools.partial(near_bwd_kernel, cases, pairs, rows, steps),
        out_shape=(
            jax.ShapeDtypeStruct((cases, points_here, width), jnp.float32),
            jax.ShapeDtypeStruct((cases, halo_points, width), jnp.bfloat16),
            jax.ShapeDtypeStruct((cases, halo_points, width), jnp.bfloat16),
        ),
        grid_spec=pltpu.PrefetchScalarGridSpec(
            num_scalar_prefetch=1,
            grid=(steps,),
            in_specs=[
                pl.BlockSpec((TB, pairs, rows, rows), lambda g, ids: (g, 0, 0, 0)),
                pl.BlockSpec((cases, TB * rows, width), lambda g, ids: (0, g, 0)),
            ],
            out_specs=[
                pl.BlockSpec((cases, points_here, width), lambda g, ids: (0, 0, 0)),
                pl.BlockSpec((cases, halo_points, width), lambda g, ids: (0, 0, 0)),
                pl.BlockSpec((cases, halo_points, width), lambda g, ids: (0, 0, 0)),
            ],
            scratch_shapes=[pltpu.VMEM((cases, span_points, width), jnp.float32)],
        ),
        compiler_params=pltpu.CompilerParams(
            dimension_semantics=("arbitrary",), vmem_limit_bytes=60 * 1024 * 1024
        ),
        cost_estimate=pl.CostEstimate(
            flops=flops,
            transcendentals=0,
            bytes_accessed=kernel_blocks.size * 2 + back_near.size * 2 + cases * span_points * width * 4,
        ),
    )(ids, kernel_blocks, back_near)


def on_device(
    features, cotangent, kernel_blocks, near_pairs, leaf_basis, w_near, w_far, translations
):
    cases_here, points_here, width = features.shape
    blocks_here, pair_count, block_rows = (
        kernel_blocks.shape[0],
        kernel_blocks.shape[1],
        kernel_blocks.shape[2],
    )
    halo_points = HALO * block_rows
    span_blocks = blocks_here + 2 * HALO
    position = lax.axis_index("leaf")

    summary = jnp.einsum("rp,apc->arc", leaf_basis, features, preferred_element_type=jnp.float32)
    summary_rows = summary.reshape(cases_here * summary.shape[1], width)
    head = features[:, :halo_points].reshape(cases_here * halo_points, width)
    tail = features[:, points_here - halo_points :].reshape(cases_here * halo_points, width)
    from_next, from_prev, sib_rows, _ = neighbour_exchange(head, tail, summary_rows)
    from_prev = from_prev.reshape(cases_here, halo_points, width)
    from_next = from_next.reshape(cases_here, halo_points, width)
    extended = jnp.concatenate([from_prev, features, from_next], axis=1)
    local_ids = jnp.clip(
        near_pairs - (position * blocks_here - HALO), 0, span_blocks - 1
    ).reshape(-1).astype(jnp.int32)

    near_bf = near_forward(local_ids, kernel_blocks, extended)

    expansion, _ = expand(summary, translations, False, sib_rows.reshape(summary.shape))
    exp_bf = expansion.astype(jnp.bfloat16)
    far_coeff = jnp.einsum("arc,cd->ard", exp_bf, w_far, preferred_element_type=jnp.float32).astype(
        jnp.bfloat16
    )
    far_field = jnp.einsum("rp,ard->apd", leaf_basis, far_coeff, preferred_element_type=jnp.float32)
    mixed = (
        jnp.einsum("apc,cd->apd", near_bf, w_near, preferred_element_type=jnp.float32) + far_field
    )
    output = jax.nn.gelu(mixed).astype(jnp.bfloat16)
    _, pullback = jax.vjp(jax.nn.gelu, mixed)
    slope = pullback(cotangent.astype(jnp.float32))[0].astype(jnp.bfloat16)
    projected = jnp.einsum(
        "rp,apc->arc", leaf_basis, slope, preferred_element_type=jnp.float32
    ).astype(jnp.bfloat16)
    back_near = jnp.einsum("apc,dc->apd", slope, w_near, preferred_element_type=jnp.float32).astype(
        jnp.bfloat16
    )

    mid, lo, hi = near_backward(local_ids, kernel_blocks, back_near, halo_points)

    scale = 1.0 / math.sqrt(
        cases_here * lax.axis_size("case") * points_here * lax.axis_size("leaf")
    )
    near_term = (
        jnp.einsum("apc,apd->cd", near_bf, slope, preferred_element_type=jnp.float32) * scale
    )
    far_term = (
        jnp.einsum("arc,ard->cd", exp_bf, projected, preferred_element_type=jnp.float32) * scale
    )
    grads = jnp.concatenate([near_term, far_term], axis=0)
    case_depth = lax.axis_size("case").bit_length() - 1
    for height in range(case_depth):
        grads = grads + partner(grads, "case", height)

    back_coeff = jnp.einsum("arc,dc->ard", projected, w_far, preferred_element_type=jnp.float32)
    coeff_rows = back_coeff.reshape(cases_here * back_coeff.shape[1], width)
    rider = jnp.concatenate([coeff_rows, grads], axis=0)
    got_next, got_prev, sib, own = neighbour_exchange(
        lo.reshape(cases_here * halo_points, width),
        hi.reshape(cases_here * halo_points, width),
        rider,
    )
    coeff_count = coeff_rows.shape[0]
    grads = own[coeff_count:] + sib[coeff_count:]
    back_exp, grads = expand(
        back_coeff, translations, True, sib[:coeff_count].reshape(back_coeff.shape), rider=grads
    )
    back_far = jnp.einsum(
        "rp,arc->apc", leaf_basis, back_exp.astype(jnp.bfloat16), preferred_element_type=jnp.float32
    )

    got_prev = got_prev.reshape(cases_here, halo_points, width).astype(jnp.float32)
    got_next = got_next.reshape(cases_here, halo_points, width).astype(jnp.float32)
    near_back = jnp.concatenate(
        [
            mid[:, :halo_points] + got_prev,
            mid[:, halo_points : points_here - halo_points],
            mid[:, points_here - halo_points :] + got_next,
        ],
        axis=1,
    )
    grad_features = (near_back + back_far).astype(jnp.bfloat16)
    grad_near = grads[:width]
    grad_far = grads[width:]
    return (output, grad_features, grad_near, grad_far)


def solution(mesh):
    return jax.shard_map(
        on_device,
        mesh=mesh,
        in_specs=(
            P("case", "leaf", None),
            P("case", "leaf", None),
            P("leaf", None, None, None),
            P("leaf", None),
            P(None, "leaf"),
            P(),
            P(),
            P(),
        ),
        out_specs=(P("case", "leaf", None), P("case", "leaf", None), P(), P()),
        check_vma=False,
    )
```

```python
import functools
import math

import jax
import jax.numpy as jnp
from jax import lax
from jax.experimental import pallas as pl
from jax.experimental.pallas import tpu as pltpu
from jax.sharding import PartitionSpec as P

HALO = 8
TB = 4


def partner(shard, axis, apart):
    return lax.ppermute(shard, axis, [(i, i ^ 1 << apart) for i in range(lax.axis_size(axis))])


def shifted(value, axis, steps):
    count = lax.axis_size(axis)
    leading, last = (max(0, -steps), min(count, count - steps))
    return lax.ppermute(value, axis, [(source, source + steps) for source in range(leading, last)])


def apply_level(matrix, sibling, flipped):
    if flipped:
        return jnp.einsum("sr,asc->arc", matrix, sibling, precision=lax.Precision.HIGHEST)
    return jnp.einsum("rs,asc->arc", matrix, sibling, precision=lax.Precision.HIGHEST)


def expand(own_value, translations, flipped, rider=None, cover=None):
    depth_count = lax.axis_size("leaf").bit_length() - 1
    summed = jnp.zeros(own_value.shape, jnp.float32)
    node_value = own_value
    rows = own_value.shape[0] * own_value.shape[1]
    for height in range(depth_count):
        if rider is None:
            sibling = partner(node_value, "leaf", height)
        else:
            packed = jnp.concatenate(
                [node_value.reshape(rows, own_value.shape[2]), rider], axis=0
            )
            got = partner(packed, "leaf", height)
            if cover is not None and height < 2:
                got, cover = lax.optimization_barrier((got, cover))
            sibling = got[:rows].reshape(own_value.shape)
            rider = rider + got[rows:]
        summed = summed + apply_level(translations[height], sibling, flipped)
        node_value = node_value + sibling
    if cover is None:
        return summed, rider
    return summed, rider, cover


def near_fwd_kernel(cases, pairs, rows, ids_ref, kb_ref, ext_ref, out_ref):
    g = pl.program_id(0)
    for tb in range(TB):
        t = g * TB + tb
        lhs = jnp.concatenate([kb_ref[tb, k] for k in range(pairs)], axis=1)
        parts = []
        for k in range(pairs):
            start = pl.multiple_of(ids_ref[t * pairs + k] * rows, rows)
            parts.append(
                jnp.concatenate([ext_ref[c, pl.ds(start, rows), :] for c in range(cases)], axis=1)
            )
        rhs = jnp.concatenate(parts, axis=0)
        acc = jnp.dot(lhs, rhs, preferred_element_type=jnp.float32)
        width = acc.shape[1] // cases
        for c in range(cases):
            out_ref[c, pl.ds(tb * rows, rows), :] = acc[:, c * width : (c + 1) * width].astype(
                out_ref.dtype
            )


def near_forward(ids, kernel_blocks, extended):
    cases, span_points, width = extended.shape
    blocks_here, pairs, rows, _ = kernel_blocks.shape
    steps = blocks_here // TB
    flops = 2 * blocks_here * pairs * rows * rows * cases * width
    return pl.pallas_call(
        functools.partial(near_fwd_kernel, cases, pairs, rows),
        out_shape=jax.ShapeDtypeStruct((cases, blocks_here * rows, width), jnp.bfloat16),
        grid_spec=pltpu.PrefetchScalarGridSpec(
            num_scalar_prefetch=1,
            grid=(steps,),
            in_specs=[
                pl.BlockSpec((TB, pairs, rows, rows), lambda g, ids: (g, 0, 0, 0)),
                pl.BlockSpec((cases, span_points, width), lambda g, ids: (0, 0, 0)),
            ],
            out_specs=pl.BlockSpec((cases, TB * rows, width), lambda g, ids: (0, g, 0)),
        ),
        compiler_params=pltpu.CompilerParams(dimension_semantics=("arbitrary",)),
        cost_estimate=pl.CostEstimate(
            flops=flops,
            transcendentals=0,
            bytes_accessed=kernel_blocks.size * 2 + extended.size * 2 + cases * blocks_here * rows * width * 2,
        ),
    )(ids, kernel_blocks, extended)


def near_bwd_kernel(cases, pairs, rows, steps, ids_ref, kb_ref, back_ref, mid_ref, lo_ref, hi_ref, acc_ref):
    g = pl.program_id(0)

    @pl.when(g == 0)
    def _():
        acc_ref[...] = jnp.zeros(acc_ref.shape, acc_ref.dtype)

    width = back_ref.shape[2]
    for tb in range(TB):
        t = g * TB + tb
        lhs = jnp.concatenate([kb_ref[tb, k] for k in range(pairs)], axis=1)
        rhs = jnp.concatenate(
            [back_ref[c, pl.ds(tb * rows, rows), :] for c in range(cases)], axis=1
        )
        res = lax.dot_general(
            lhs, rhs, (((0,), (0,)), ((), ())), preferred_element_type=jnp.float32
        )
        for k in range(pairs):
            start = pl.multiple_of(ids_ref[t * pairs + k] * rows, rows)
            piece = res[k * rows : (k + 1) * rows]
            for c in range(cases):
                acc_ref[c, pl.ds(start, rows), :] += piece[:, c * width : (c + 1) * width]

    @pl.when(g == steps - 1)
    def _():
        halo_points = lo_ref.shape[1]
        mid_points = mid_ref.shape[1]
        lo_ref[...] = acc_ref[:, :halo_points, :].astype(lo_ref.dtype)
        mid_ref[...] = acc_ref[:, halo_points : halo_points + mid_points, :]
        hi_ref[...] = acc_ref[:, halo_points + mid_points :, :].astype(hi_ref.dtype)


def near_backward(ids, kernel_blocks, back_near, halo_points):
    cases, points_here, width = back_near.shape
    blocks_here, pairs, rows, _ = kernel_blocks.shape
    steps = blocks_here // TB
    span_points = points_here + 2 * halo_points
    flops = 2 * blocks_here * pairs * rows * rows * cases * width
    return pl.pallas_call(
        functools.partial(near_bwd_kernel, cases, pairs, rows, steps),
        out_shape=(
            jax.ShapeDtypeStruct((cases, points_here, width), jnp.float32),
            jax.ShapeDtypeStruct((cases, halo_points, width), jnp.bfloat16),
            jax.ShapeDtypeStruct((cases, halo_points, width), jnp.bfloat16),
        ),
        grid_spec=pltpu.PrefetchScalarGridSpec(
            num_scalar_prefetch=1,
            grid=(steps,),
            in_specs=[
                pl.BlockSpec((TB, pairs, rows, rows), lambda g, ids: (g, 0, 0, 0)),
                pl.BlockSpec((cases, TB * rows, width), lambda g, ids: (0, g, 0)),
            ],
            out_specs=[
                pl.BlockSpec((cases, points_here, width), lambda g, ids: (0, 0, 0)),
                pl.BlockSpec((cases, halo_points, width), lambda g, ids: (0, 0, 0)),
                pl.BlockSpec((cases, halo_points, width), lambda g, ids: (0, 0, 0)),
            ],
            scratch_shapes=[pltpu.VMEM((cases, span_points, width), jnp.float32)],
        ),
        compiler_params=pltpu.CompilerParams(
            dimension_semantics=("arbitrary",), vmem_limit_bytes=60 * 1024 * 1024
        ),
        cost_estimate=pl.CostEstimate(
            flops=flops,
            transcendentals=0,
            bytes_accessed=kernel_blocks.size * 2 + back_near.size * 2 + cases * span_points * width * 4,
        ),
    )(ids, kernel_blocks, back_near)


def on_device(
    features, cotangent, kernel_blocks, near_pairs, leaf_basis, w_near, w_far, translations
):
    cases_here, points_here, width = features.shape
    blocks_here, pair_count, block_rows = (
        kernel_blocks.shape[0],
        kernel_blocks.shape[1],
        kernel_blocks.shape[2],
    )
    halo_points = HALO * block_rows
    span_blocks = blocks_here + 2 * HALO
    position = lax.axis_index("leaf")

    head = features[:, :halo_points]
    tail = features[:, points_here - halo_points :]
    from_prev = shifted(tail, "leaf", 1)
    from_next = shifted(head, "leaf", -1)
    extended = jnp.concatenate([from_prev, features, from_next], axis=1)
    local_ids = jnp.clip(
        near_pairs - (position * blocks_here - HALO), 0, span_blocks - 1
    ).reshape(-1).astype(jnp.int32)

    near_bf = near_forward(local_ids, kernel_blocks, extended)

    summary = jnp.einsum("rp,apc->arc", leaf_basis, features, preferred_element_type=jnp.float32)
    expansion, _ = expand(summary, translations, False)
    exp_bf = expansion.astype(jnp.bfloat16)
    far_coeff = jnp.einsum("arc,cd->ard", exp_bf, w_far, preferred_element_type=jnp.float32).astype(
        jnp.bfloat16
    )
    far_field = jnp.einsum("rp,ard->apd", leaf_basis, far_coeff, preferred_element_type=jnp.float32)
    mixed = (
        jnp.einsum("apc,cd->apd", near_bf, w_near, preferred_element_type=jnp.float32) + far_field
    )
    output = jax.nn.gelu(mixed).astype(jnp.bfloat16)
    _, pullback = jax.vjp(jax.nn.gelu, mixed)
    slope = pullback(cotangent.astype(jnp.float32))[0].astype(jnp.bfloat16)
    projected = jnp.einsum(
        "rp,apc->arc", leaf_basis, slope, preferred_element_type=jnp.float32
    ).astype(jnp.bfloat16)
    back_near = jnp.einsum("apc,dc->apd", slope, w_near, preferred_element_type=jnp.float32).astype(
        jnp.bfloat16
    )

    mid, lo, hi = near_backward(local_ids, kernel_blocks, back_near, halo_points)

    scale = 1.0 / math.sqrt(
        cases_here * lax.axis_size("case") * points_here * lax.axis_size("leaf")
    )
    near_term = (
        jnp.einsum("apc,apd->cd", near_bf, slope, preferred_element_type=jnp.float32) * scale
    )
    far_term = (
        jnp.einsum("arc,ard->cd", exp_bf, projected, preferred_element_type=jnp.float32) * scale
    )
    grads = jnp.concatenate([near_term, far_term], axis=0)

    back_coeff = jnp.einsum("arc,dc->ard", projected, w_far, preferred_element_type=jnp.float32)
    back_exp, grads, (mid, lo, hi) = expand(
        back_coeff, translations, True, rider=grads, cover=(mid, lo, hi)
    )
    back_far = jnp.einsum(
        "rp,arc->apc", leaf_basis, back_exp.astype(jnp.bfloat16), preferred_element_type=jnp.float32
    )

    case_depth = lax.axis_size("case").bit_length() - 1
    for height in range(case_depth):
        grads = grads + partner(grads, "case", height)

    got_prev = shifted(hi, "leaf", 1).astype(jnp.float32)
    got_next = shifted(lo, "leaf", -1).astype(jnp.float32)
    near_back = jnp.concatenate(
        [
            mid[:, :halo_points] + got_prev,
            mid[:, halo_points : points_here - halo_points],
            mid[:, points_here - halo_points :] + got_next,
        ],
        axis=1,
    )
    grad_features = (near_back + back_far).astype(jnp.bfloat16)
    grad_near = grads[:width]
    grad_far = grads[width:]
    return (output, grad_features, grad_near, grad_far)


def solution(mesh):
    return jax.shard_map(
        on_device,
        mesh=mesh,
        in_specs=(
            P("case", "leaf", None),
            P("case", "leaf", None),
            P("leaf", None, None, None),
            P("leaf", None),
            P(None, "leaf"),
            P(),
            P(),
            P(),
        ),
        out_specs=(P("case", "leaf", None), P("case", "leaf", None), P(), P()),
        check_vma=False,
    )
```

```python
import functools
import math

import jax
import jax.numpy as jnp
from jax import lax
from jax.experimental import pallas as pl
from jax.experimental.pallas import tpu as pltpu
from jax.sharding import PartitionSpec as P

HALO = 8
TB = 4


def partner(shard, axis, apart):
    return lax.ppermute(shard, axis, [(i, i ^ 1 << apart) for i in range(lax.axis_size(axis))])


def shifted(value, axis, steps):
    count = lax.axis_size(axis)
    leading, last = (max(0, -steps), min(count, count - steps))
    return lax.ppermute(value, axis, [(source, source + steps) for source in range(leading, last)])


def apply_level(matrix, sibling, flipped):
    if flipped:
        return jnp.einsum("sr,asc->arc", matrix, sibling, precision=lax.Precision.HIGHEST)
    return jnp.einsum("rs,asc->arc", matrix, sibling, precision=lax.Precision.HIGHEST)


def expand(own_value, translations, flipped, rider=None, cover=None):
    depth_count = lax.axis_size("leaf").bit_length() - 1
    summed = jnp.zeros(own_value.shape, jnp.float32)
    node_value = own_value
    rows = own_value.shape[0] * own_value.shape[1]
    for height in range(depth_count):
        if rider is None:
            sibling = partner(node_value, "leaf", height)
        else:
            packed = jnp.concatenate(
                [node_value.reshape(rows, own_value.shape[2]), rider], axis=0
            )
            got = partner(packed, "leaf", height)
            if cover is not None and height < 2:
                got, cover = lax.optimization_barrier((got, cover))
            sibling = got[:rows].reshape(own_value.shape)
            rider = rider + got[rows:]
        summed = summed + apply_level(translations[height], sibling, flipped)
        node_value = node_value + sibling
    if cover is None:
        return summed, rider
    return summed, rider, cover


def near_fwd_kernel(cases, pairs, rows, ids_ref, kb_ref, ext_ref, out_ref):
    g = pl.program_id(0)
    for tb in range(TB):
        t = g * TB + tb
        lhs = jnp.concatenate([kb_ref[tb, k] for k in range(pairs)], axis=1)
        parts = []
        for k in range(pairs):
            start = pl.multiple_of(ids_ref[t * pairs + k] * rows, rows)
            parts.append(
                jnp.concatenate([ext_ref[c, pl.ds(start, rows), :] for c in range(cases)], axis=1)
            )
        rhs = jnp.concatenate(parts, axis=0)
        acc = jnp.dot(lhs, rhs, preferred_element_type=jnp.float32)
        width = acc.shape[1] // cases
        for c in range(cases):
            out_ref[c, pl.ds(tb * rows, rows), :] = acc[:, c * width : (c + 1) * width].astype(
                out_ref.dtype
            )


def near_forward(ids, kernel_blocks, extended):
    cases, span_points, width = extended.shape
    blocks_here, pairs, rows, _ = kernel_blocks.shape
    steps = blocks_here // TB
    flops = 2 * blocks_here * pairs * rows * rows * cases * width
    return pl.pallas_call(
        functools.partial(near_fwd_kernel, cases, pairs, rows),
        out_shape=jax.ShapeDtypeStruct((cases, blocks_here * rows, width), jnp.bfloat16),
        grid_spec=pltpu.PrefetchScalarGridSpec(
            num_scalar_prefetch=1,
            grid=(steps,),
            in_specs=[
                pl.BlockSpec((TB, pairs, rows, rows), lambda g, ids: (g, 0, 0, 0)),
                pl.BlockSpec((cases, span_points, width), lambda g, ids: (0, 0, 0)),
            ],
            out_specs=pl.BlockSpec((cases, TB * rows, width), lambda g, ids: (0, g, 0)),
        ),
        compiler_params=pltpu.CompilerParams(dimension_semantics=("arbitrary",)),
        cost_estimate=pl.CostEstimate(
            flops=flops,
            transcendentals=0,
            bytes_accessed=kernel_blocks.size * 2 + extended.size * 2 + cases * blocks_here * rows * width * 2,
        ),
    )(ids, kernel_blocks, extended)


def near_bwd_kernel(cases, pairs, rows, steps, ids_ref, kb_ref, back_ref, mid_ref, lo_ref, hi_ref, acc_ref):
    g = pl.program_id(0)

    @pl.when(g == 0)
    def _():
        acc_ref[...] = jnp.zeros(acc_ref.shape, acc_ref.dtype)

    width = back_ref.shape[2]
    for tb in range(TB):
        t = g * TB + tb
        lhs = jnp.concatenate([kb_ref[tb, k] for k in range(pairs)], axis=1)
        rhs = jnp.concatenate(
            [back_ref[c, pl.ds(tb * rows, rows), :] for c in range(cases)], axis=1
        )
        res = lax.dot_general(
            lhs, rhs, (((0,), (0,)), ((), ())), preferred_element_type=jnp.float32
        )
        for k in range(pairs):
            start = pl.multiple_of(ids_ref[t * pairs + k] * rows, rows)
            piece = res[k * rows : (k + 1) * rows]
            for c in range(cases):
                acc_ref[c, pl.ds(start, rows), :] += piece[:, c * width : (c + 1) * width]

    @pl.when(g == steps - 1)
    def _():
        halo_points = lo_ref.shape[1]
        mid_points = mid_ref.shape[1]
        lo_ref[...] = acc_ref[:, :halo_points, :].astype(lo_ref.dtype)
        mid_ref[...] = acc_ref[:, halo_points : halo_points + mid_points, :]
        hi_ref[...] = acc_ref[:, halo_points + mid_points :, :].astype(hi_ref.dtype)


def near_backward(ids, kernel_blocks, back_near, halo_points):
    cases, points_here, width = back_near.shape
    blocks_here, pairs, rows, _ = kernel_blocks.shape
    steps = blocks_here // TB
    span_points = points_here + 2 * halo_points
    flops = 2 * blocks_here * pairs * rows * rows * cases * width
    return pl.pallas_call(
        functools.partial(near_bwd_kernel, cases, pairs, rows, steps),
        out_shape=(
            jax.ShapeDtypeStruct((cases, points_here, width), jnp.float32),
            jax.ShapeDtypeStruct((cases, halo_points, width), jnp.bfloat16),
            jax.ShapeDtypeStruct((cases, halo_points, width), jnp.bfloat16),
        ),
        grid_spec=pltpu.PrefetchScalarGridSpec(
            num_scalar_prefetch=1,
            grid=(steps,),
            in_specs=[
                pl.BlockSpec((TB, pairs, rows, rows), lambda g, ids: (g, 0, 0, 0)),
                pl.BlockSpec((cases, TB * rows, width), lambda g, ids: (0, g, 0)),
            ],
            out_specs=[
                pl.BlockSpec((cases, points_here, width), lambda g, ids: (0, 0, 0)),
                pl.BlockSpec((cases, halo_points, width), lambda g, ids: (0, 0, 0)),
                pl.BlockSpec((cases, halo_points, width), lambda g, ids: (0, 0, 0)),
            ],
            scratch_shapes=[pltpu.VMEM((cases, span_points, width), jnp.float32)],
        ),
        compiler_params=pltpu.CompilerParams(
            dimension_semantics=("arbitrary",), vmem_limit_bytes=60 * 1024 * 1024
        ),
        cost_estimate=pl.CostEstimate(
            flops=flops,
            transcendentals=0,
            bytes_accessed=kernel_blocks.size * 2 + back_near.size * 2 + cases * span_points * width * 4,
        ),
    )(ids, kernel_blocks, back_near)


def on_device(
    features, cotangent, kernel_blocks, near_pairs, leaf_basis, w_near, w_far, translations
):
    cases_here, points_here, width = features.shape
    blocks_here, pair_count, block_rows = (
        kernel_blocks.shape[0],
        kernel_blocks.shape[1],
        kernel_blocks.shape[2],
    )
    halo_points = HALO * block_rows
    span_blocks = blocks_here + 2 * HALO
    position = lax.axis_index("leaf")

    head = features[:, :halo_points]
    tail = features[:, points_here - halo_points :]
    from_prev = shifted(tail, "leaf", 1)
    from_next = shifted(head, "leaf", -1)
    summary = jnp.einsum("rp,apc->arc", leaf_basis, features, preferred_element_type=jnp.float32)
    summary, from_prev, from_next = lax.optimization_barrier((summary, from_prev, from_next))
    extended = jnp.concatenate([from_prev, features, from_next], axis=1)
    local_ids = jnp.clip(
        near_pairs - (position * blocks_here - HALO), 0, span_blocks - 1
    ).reshape(-1).astype(jnp.int32)

    near_bf = near_forward(local_ids, kernel_blocks, extended)

    expansion, _ = expand(summary, translations, False)
    exp_bf = expansion.astype(jnp.bfloat16)
    far_coeff = jnp.einsum("arc,cd->ard", exp_bf, w_far, preferred_element_type=jnp.float32).astype(
        jnp.bfloat16
    )
    far_field = jnp.einsum("rp,ard->apd", leaf_basis, far_coeff, preferred_element_type=jnp.float32)
    mixed = (
        jnp.einsum("apc,cd->apd", near_bf, w_near, preferred_element_type=jnp.float32) + far_field
    )
    output = jax.nn.gelu(mixed).astype(jnp.bfloat16)
    _, pullback = jax.vjp(jax.nn.gelu, mixed)
    slope = pullback(cotangent.astype(jnp.float32))[0].astype(jnp.bfloat16)
    projected = jnp.einsum(
        "rp,apc->arc", leaf_basis, slope, preferred_element_type=jnp.float32
    ).astype(jnp.bfloat16)
    back_near = jnp.einsum("apc,dc->apd", slope, w_near, preferred_element_type=jnp.float32).astype(
        jnp.bfloat16
    )

    mid, lo, hi = near_backward(local_ids, kernel_blocks, back_near, halo_points)

    scale = 1.0 / math.sqrt(
        cases_here * lax.axis_size("case") * points_here * lax.axis_size("leaf")
    )
    near_term = (
        jnp.einsum("apc,apd->cd", near_bf, slope, preferred_element_type=jnp.float32) * scale
    )
    far_term = (
        jnp.einsum("arc,ard->cd", exp_bf, projected, preferred_element_type=jnp.float32) * scale
    )
    grads = jnp.concatenate([near_term, far_term], axis=0)

    back_coeff = jnp.einsum("arc,dc->ard", projected, w_far, preferred_element_type=jnp.float32)
    back_exp, grads, (mid, lo, hi) = expand(
        back_coeff, translations, True, rider=grads, cover=(mid, lo, hi)
    )
    back_far = jnp.einsum(
        "rp,arc->apc", leaf_basis, back_exp.astype(jnp.bfloat16), preferred_element_type=jnp.float32
    )

    case_depth = lax.axis_size("case").bit_length() - 1
    for height in range(case_depth):
        grads = grads + partner(grads, "case", height)

    got_prev = shifted(hi, "leaf", 1).astype(jnp.float32)
    got_next = shifted(lo, "leaf", -1).astype(jnp.float32)
    near_back = jnp.concatenate(
        [
            mid[:, :halo_points] + got_prev,
            mid[:, halo_points : points_here - halo_points],
            mid[:, points_here - halo_points :] + got_next,
        ],
        axis=1,
    )
    grad_features = (near_back + back_far).astype(jnp.bfloat16)
    grad_near = grads[:width]
    grad_far = grads[width:]
    return (output, grad_features, grad_near, grad_far)


def solution(mesh):
    return jax.shard_map(
        on_device,
        mesh=mesh,
        in_specs=(
            P("case", "leaf", None),
            P("case", "leaf", None),
            P("leaf", None, None, None),
            P("leaf", None),
            P(None, "leaf"),
            P(),
            P(),
            P(),
        ),
        out_specs=(P("case", "leaf", None), P("case", "leaf", None), P(), P()),
        check_vma=False,
    )
```

```python
import functools
import math

import jax
import jax.numpy as jnp
from jax import lax
from jax.experimental import pallas as pl
from jax.experimental.pallas import tpu as pltpu
from jax.sharding import PartitionSpec as P

HALO = 8
TB = 4


def partner(shard, axis, apart):
    return lax.ppermute(shard, axis, [(i, i ^ 1 << apart) for i in range(lax.axis_size(axis))])


def shifted(value, axis, steps):
    count = lax.axis_size(axis)
    leading, last = (max(0, -steps), min(count, count - steps))
    return lax.ppermute(value, axis, [(source, source + steps) for source in range(leading, last)])


def apply_level(matrix, sibling, flipped):
    if flipped:
        return jnp.einsum("sr,asc->arc", matrix, sibling, precision=lax.Precision.HIGHEST)
    return jnp.einsum("rs,asc->arc", matrix, sibling, precision=lax.Precision.HIGHEST)


def expand(own_value, translations, flipped, rider=None, cover=None):
    depth_count = lax.axis_size("leaf").bit_length() - 1
    summed = jnp.zeros(own_value.shape, jnp.float32)
    node_value = own_value
    rows = own_value.shape[0] * own_value.shape[1]
    for height in range(depth_count):
        if rider is None:
            sibling = partner(node_value, "leaf", height)
        else:
            packed = jnp.concatenate(
                [node_value.reshape(rows, own_value.shape[2]), rider], axis=0
            )
            got = partner(packed, "leaf", height)
            if cover is not None and height < 1:
                got, cover = lax.optimization_barrier((got, cover))
            sibling = got[:rows].reshape(own_value.shape)
            rider = rider + got[rows:]
        summed = summed + apply_level(translations[height], sibling, flipped)
        node_value = node_value + sibling
    if cover is None:
        return summed, rider
    return summed, rider, cover


def near_fwd_kernel(cases, pairs, rows, ids_ref, kb_ref, ext_ref, out_ref):
    g = pl.program_id(0)
    for tb in range(TB):
        t = g * TB + tb
        lhs = jnp.concatenate([kb_ref[tb, k] for k in range(pairs)], axis=1)
        parts = []
        for k in range(pairs):
            start = pl.multiple_of(ids_ref[t * pairs + k] * rows, rows)
            parts.append(
                jnp.concatenate([ext_ref[c, pl.ds(start, rows), :] for c in range(cases)], axis=1)
            )
        rhs = jnp.concatenate(parts, axis=0)
        acc = jnp.dot(lhs, rhs, preferred_element_type=jnp.float32)
        width = acc.shape[1] // cases
        for c in range(cases):
            out_ref[c, pl.ds(tb * rows, rows), :] = acc[:, c * width : (c + 1) * width].astype(
                out_ref.dtype
            )


def near_forward(ids, kernel_blocks, extended):
    cases, span_points, width = extended.shape
    blocks_here, pairs, rows, _ = kernel_blocks.shape
    steps = blocks_here // TB
    flops = 2 * blocks_here * pairs * rows * rows * cases * width
    return pl.pallas_call(
        functools.partial(near_fwd_kernel, cases, pairs, rows),
        out_shape=jax.ShapeDtypeStruct((cases, blocks_here * rows, width), jnp.bfloat16),
        grid_spec=pltpu.PrefetchScalarGridSpec(
            num_scalar_prefetch=1,
            grid=(steps,),
            in_specs=[
                pl.BlockSpec((TB, pairs, rows, rows), lambda g, ids: (g, 0, 0, 0)),
                pl.BlockSpec((cases, span_points, width), lambda g, ids: (0, 0, 0)),
            ],
            out_specs=pl.BlockSpec((cases, TB * rows, width), lambda g, ids: (0, g, 0)),
        ),
        compiler_params=pltpu.CompilerParams(dimension_semantics=("arbitrary",)),
        cost_estimate=pl.CostEstimate(
            flops=flops,
            transcendentals=0,
            bytes_accessed=kernel_blocks.size * 2 + extended.size * 2 + cases * blocks_here * rows * width * 2,
        ),
    )(ids, kernel_blocks, extended)


def near_bwd_kernel(cases, pairs, rows, steps, ids_ref, kb_ref, back_ref, mid_ref, lo_ref, hi_ref, acc_ref):
    g = pl.program_id(0)

    @pl.when(g == 0)
    def _():
        acc_ref[...] = jnp.zeros(acc_ref.shape, acc_ref.dtype)

    width = back_ref.shape[2]
    for tb in range(TB):
        t = g * TB + tb
        lhs = jnp.concatenate([kb_ref[tb, k] for k in range(pairs)], axis=1)
        rhs = jnp.concatenate(
            [back_ref[c, pl.ds(tb * rows, rows), :] for c in range(cases)], axis=1
        )
        res = lax.dot_general(
            lhs, rhs, (((0,), (0,)), ((), ())), preferred_element_type=jnp.float32
        )
        for k in range(pairs):
            start = pl.multiple_of(ids_ref[t * pairs + k] * rows, rows)
            piece = res[k * rows : (k + 1) * rows]
            for c in range(cases):
                acc_ref[c, pl.ds(start, rows), :] += piece[:, c * width : (c + 1) * width]

    @pl.when(g == steps - 1)
    def _():
        halo_points = lo_ref.shape[1]
        mid_points = mid_ref.shape[1]
        lo_ref[...] = acc_ref[:, :halo_points, :].astype(lo_ref.dtype)
        mid_ref[...] = acc_ref[:, halo_points : halo_points + mid_points, :]
        hi_ref[...] = acc_ref[:, halo_points + mid_points :, :].astype(hi_ref.dtype)


def near_backward(ids, kernel_blocks, back_near, halo_points):
    cases, points_here, width = back_near.shape
    blocks_here, pairs, rows, _ = kernel_blocks.shape
    steps = blocks_here // TB
    span_points = points_here + 2 * halo_points
    flops = 2 * blocks_here * pairs * rows * rows * cases * width
    return pl.pallas_call(
        functools.partial(near_bwd_kernel, cases, pairs, rows, steps),
        out_shape=(
            jax.ShapeDtypeStruct((cases, points_here, width), jnp.float32),
            jax.ShapeDtypeStruct((cases, halo_points, width), jnp.bfloat16),
            jax.ShapeDtypeStruct((cases, halo_points, width), jnp.bfloat16),
        ),
        grid_spec=pltpu.PrefetchScalarGridSpec(
            num_scalar_prefetch=1,
            grid=(steps,),
            in_specs=[
                pl.BlockSpec((TB, pairs, rows, rows), lambda g, ids: (g, 0, 0, 0)),
                pl.BlockSpec((cases, TB * rows, width), lambda g, ids: (0, g, 0)),
            ],
            out_specs=[
                pl.BlockSpec((cases, points_here, width), lambda g, ids: (0, 0, 0)),
                pl.BlockSpec((cases, halo_points, width), lambda g, ids: (0, 0, 0)),
                pl.BlockSpec((cases, halo_points, width), lambda g, ids: (0, 0, 0)),
            ],
            scratch_shapes=[pltpu.VMEM((cases, span_points, width), jnp.float32)],
        ),
        compiler_params=pltpu.CompilerParams(
            dimension_semantics=("arbitrary",), vmem_limit_bytes=60 * 1024 * 1024
        ),
        cost_estimate=pl.CostEstimate(
            flops=flops,
            transcendentals=0,
            bytes_accessed=kernel_blocks.size * 2 + back_near.size * 2 + cases * span_points * width * 4,
        ),
    )(ids, kernel_blocks, back_near)


def on_device(
    features, cotangent, kernel_blocks, near_pairs, leaf_basis, w_near, w_far, translations
):
    cases_here, points_here, width = features.shape
    blocks_here, pair_count, block_rows = (
        kernel_blocks.shape[0],
        kernel_blocks.shape[1],
        kernel_blocks.shape[2],
    )
    halo_points = HALO * block_rows
    span_blocks = blocks_here + 2 * HALO
    position = lax.axis_index("leaf")

    head = features[:, :halo_points]
    tail = features[:, points_here - halo_points :]
    from_prev = shifted(tail, "leaf", 1)
    from_next = shifted(head, "leaf", -1)
    extended = jnp.concatenate([from_prev, features, from_next], axis=1)
    local_ids = jnp.clip(
        near_pairs - (position * blocks_here - HALO), 0, span_blocks - 1
    ).reshape(-1).astype(jnp.int32)

    near_bf = near_forward(local_ids, kernel_blocks, extended)

    summary = jnp.einsum("rp,apc->arc", leaf_basis, features, preferred_element_type=jnp.float32)
    expansion, _ = expand(summary, translations, False)
    exp_bf = expansion.astype(jnp.bfloat16)
    far_coeff = jnp.einsum("arc,cd->ard", exp_bf, w_far, preferred_element_type=jnp.float32).astype(
        jnp.bfloat16
    )
    far_field = jnp.einsum("rp,ard->apd", leaf_basis, far_coeff, preferred_element_type=jnp.float32)
    mixed = (
        jnp.einsum("apc,cd->apd", near_bf, w_near, preferred_element_type=jnp.float32) + far_field
    )
    output = jax.nn.gelu(mixed).astype(jnp.bfloat16)
    _, pullback = jax.vjp(jax.nn.gelu, mixed)
    slope = pullback(cotangent.astype(jnp.float32))[0].astype(jnp.bfloat16)
    projected = jnp.einsum(
        "rp,apc->arc", leaf_basis, slope, preferred_element_type=jnp.float32
    ).astype(jnp.bfloat16)
    back_near = jnp.einsum("apc,dc->apd", slope, w_near, preferred_element_type=jnp.float32).astype(
        jnp.bfloat16
    )

    mid, lo, hi = near_backward(local_ids, kernel_blocks, back_near, halo_points)

    scale = 1.0 / math.sqrt(
        cases_here * lax.axis_size("case") * points_here * lax.axis_size("leaf")
    )
    near_term = (
        jnp.einsum("apc,apd->cd", near_bf, slope, preferred_element_type=jnp.float32) * scale
    )
    far_term = (
        jnp.einsum("arc,ard->cd", exp_bf, projected, preferred_element_type=jnp.float32) * scale
    )
    grads = jnp.concatenate([near_term, far_term], axis=0)

    back_coeff = jnp.einsum("arc,dc->ard", projected, w_far, preferred_element_type=jnp.float32)
    back_exp, grads, (mid, lo, hi) = expand(
        back_coeff, translations, True, rider=grads, cover=(mid, lo, hi)
    )
    back_far = jnp.einsum(
        "rp,arc->apc", leaf_basis, back_exp.astype(jnp.bfloat16), preferred_element_type=jnp.float32
    )

    case_depth = lax.axis_size("case").bit_length() - 1
    for height in range(case_depth):
        grads = grads + partner(grads, "case", height)

    got_prev = shifted(hi, "leaf", 1).astype(jnp.float32)
    got_next = shifted(lo, "leaf", -1).astype(jnp.float32)
    near_back = jnp.concatenate(
        [
            mid[:, :halo_points] + got_prev,
            mid[:, halo_points : points_here - halo_points],
            mid[:, points_here - halo_points :] + got_next,
        ],
        axis=1,
    )
    grad_features = (near_back + back_far).astype(jnp.bfloat16)
    grad_near = grads[:width]
    grad_far = grads[width:]
    return (output, grad_features, grad_near, grad_far)


def solution(mesh):
    return jax.shard_map(
        on_device,
        mesh=mesh,
        in_specs=(
            P("case", "leaf", None),
            P("case", "leaf", None),
            P("leaf", None, None, None),
            P("leaf", None),
            P(None, "leaf"),
            P(),
            P(),
            P(),
        ),
        out_specs=(P("case", "leaf", None), P("case", "leaf", None), P(), P()),
        check_vma=False,
    )
```

```python
import functools
import math

import jax
import jax.numpy as jnp
from jax import lax
from jax.experimental import pallas as pl
from jax.experimental.pallas import tpu as pltpu
from jax.sharding import PartitionSpec as P

HALO = 8
TB = 4


def partner(shard, axis, apart):
    return lax.ppermute(shard, axis, [(i, i ^ 1 << apart) for i in range(lax.axis_size(axis))])


def shifted(value, axis, steps):
    count = lax.axis_size(axis)
    leading, last = (max(0, -steps), min(count, count - steps))
    return lax.ppermute(value, axis, [(source, source + steps) for source in range(leading, last)])


def apply_level(matrix, sibling, flipped):
    if flipped:
        return jnp.einsum("sr,asc->arc", matrix, sibling, precision=lax.Precision.HIGHEST)
    return jnp.einsum("rs,asc->arc", matrix, sibling, precision=lax.Precision.HIGHEST)


def expand(own_value, translations, flipped, rider=None, cover=None):
    depth_count = lax.axis_size("leaf").bit_length() - 1
    summed = jnp.zeros(own_value.shape, jnp.float32)
    node_value = own_value
    rows = own_value.shape[0] * own_value.shape[1]
    for height in range(depth_count):
        if rider is None:
            sibling = partner(node_value, "leaf", height)
        else:
            packed = jnp.concatenate(
                [node_value.reshape(rows, own_value.shape[2]), rider], axis=0
            )
            got = partner(packed, "leaf", height)
            if cover is not None and height < 2:
                got, cover = lax.optimization_barrier((got, cover))
            sibling = got[:rows].reshape(own_value.shape)
            rider = rider + got[rows:]
        summed = summed + apply_level(translations[height], sibling, flipped)
        node_value = node_value + sibling
    if cover is None:
        return summed, rider
    return summed, rider, cover


def near_fwd_kernel(cases, pairs, rows, ids_ref, kb_ref, ext_ref, out_ref):
    g = pl.program_id(0)
    for tb in range(TB):
        t = g * TB + tb
        lhs = jnp.concatenate([kb_ref[tb, k] for k in range(pairs)], axis=1)
        parts = []
        for k in range(pairs):
            start = pl.multiple_of(ids_ref[t * pairs + k] * rows, rows)
            parts.append(
                jnp.concatenate([ext_ref[c, pl.ds(start, rows), :] for c in range(cases)], axis=1)
            )
        rhs = jnp.concatenate(parts, axis=0)
        acc = jnp.dot(lhs, rhs, preferred_element_type=jnp.float32)
        width = acc.shape[1] // cases
        for c in range(cases):
            out_ref[c, pl.ds(tb * rows, rows), :] = acc[:, c * width : (c + 1) * width].astype(
                out_ref.dtype
            )


def near_forward(ids, kernel_blocks, extended):
    cases, span_points, width = extended.shape
    blocks_here, pairs, rows, _ = kernel_blocks.shape
    steps = blocks_here // TB
    flops = 2 * blocks_here * pairs * rows * rows * cases * width
    return pl.pallas_call(
        functools.partial(near_fwd_kernel, cases, pairs, rows),
        out_shape=jax.ShapeDtypeStruct((cases, blocks_here * rows, width), jnp.bfloat16),
        grid_spec=pltpu.PrefetchScalarGridSpec(
            num_scalar_prefetch=1,
            grid=(steps,),
            in_specs=[
                pl.BlockSpec((TB, pairs, rows, rows), lambda g, ids: (g, 0, 0, 0)),
                pl.BlockSpec((cases, span_points, width), lambda g, ids: (0, 0, 0)),
            ],
            out_specs=pl.BlockSpec((cases, TB * rows, width), lambda g, ids: (0, g, 0)),
        ),
        compiler_params=pltpu.CompilerParams(dimension_semantics=("arbitrary",)),
        cost_estimate=pl.CostEstimate(
            flops=flops,
            transcendentals=0,
            bytes_accessed=kernel_blocks.size * 2 + extended.size * 2 + cases * blocks_here * rows * width * 2,
        ),
    )(ids, kernel_blocks, extended)


def near_local_kernel(pairs, halo, own, ids_ref, kb_ref, feat_ref, out_ref, acc_ref):
    g = pl.program_id(0)
    tbs = kb_ref.shape[0]
    for tb in range(tbs):
        t = g * tbs + tb
        acc_ref[...] = jnp.zeros(acc_ref.shape, acc_ref.dtype)
        for k in range(pairs):
            idx = ids_ref[t * pairs + k] - halo

            @pl.when((idx >= 0) & (idx < own))
            def _():
                blk = feat_ref[jnp.clip(idx, 0, own - 1)]
                acc_ref[...] += jnp.dot(kb_ref[tb, k], blk, preferred_element_type=jnp.float32)

        out_ref[tb] = acc_ref[...]


def near_halo_kernel(pairs, halo, own, cases, ids_ref, kb_ref, halo_ref, part_ref, out_ref, acc_ref):
    g = pl.program_id(0)
    tbs = kb_ref.shape[0]
    rows = kb_ref.shape[2]
    for tb in range(tbs):
        t = g * tbs + tb
        acc_ref[...] = part_ref[tb]
        for k in range(pairs):
            idx = ids_ref[t * pairs + k]
            inside = (idx >= halo) & (idx < halo + own)
            hidx = jnp.where(idx < halo, idx, idx - own)

            @pl.when(jnp.logical_not(inside))
            def _():
                blk = halo_ref[jnp.clip(hidx, 0, 2 * halo - 1)]
                acc_ref[...] += jnp.dot(kb_ref[tb, k], blk, preferred_element_type=jnp.float32)

        width = acc_ref.shape[1] // cases
        for c in range(cases):
            out_ref[c, pl.ds(tb * rows, rows), :] = acc_ref[:, c * width : (c + 1) * width].astype(
                out_ref.dtype
            )


def case_minor(x, rows):
    cases, points, width = x.shape
    return x.reshape(cases, points // rows, rows, width).transpose(1, 2, 0, 3).reshape(
        points // rows, rows, cases * width
    )


def near_forward_split(ids, kernel_blocks, features, from_prev, from_next, halo):
    cases, points_here, width = features.shape
    blocks_here, pairs, rows, _ = kernel_blocks.shape
    steps = blocks_here // TB
    lanes = cases * width
    feat = case_minor(features, rows)
    flops = 2 * blocks_here * pairs * rows * rows * lanes
    partial = pl.pallas_call(
        functools.partial(near_local_kernel, pairs, halo, blocks_here),
        out_shape=jax.ShapeDtypeStruct((blocks_here, rows, lanes), jnp.float32),
        grid_spec=pltpu.PrefetchScalarGridSpec(
            num_scalar_prefetch=1,
            grid=(steps,),
            in_specs=[
                pl.BlockSpec((TB, pairs, rows, rows), lambda g, ids: (g, 0, 0, 0)),
                pl.BlockSpec((blocks_here, rows, lanes), lambda g, ids: (0, 0, 0)),
            ],
            out_specs=pl.BlockSpec((TB, rows, lanes), lambda g, ids: (g, 0, 0)),
            scratch_shapes=[pltpu.VMEM((rows, lanes), jnp.float32)],
        ),
        compiler_params=pltpu.CompilerParams(dimension_semantics=("arbitrary",)),
        cost_estimate=pl.CostEstimate(
            flops=flops // 2,
            transcendentals=0,
            bytes_accessed=kernel_blocks.size * 2 + features.size * 2 + blocks_here * rows * lanes * 4,
        ),
    )(ids, kernel_blocks, feat)
    halo_blocks = case_minor(jnp.concatenate([from_prev, from_next], axis=1), rows)
    return pl.pallas_call(
        functools.partial(near_halo_kernel, pairs, halo, blocks_here, cases),
        out_shape=jax.ShapeDtypeStruct((cases, points_here, width), jnp.bfloat16),
        grid_spec=pltpu.PrefetchScalarGridSpec(
            num_scalar_prefetch=1,
            grid=(steps,),
            in_specs=[
                pl.BlockSpec((TB, pairs, rows, rows), lambda g, ids: (g, 0, 0, 0)),
                pl.BlockSpec((2 * halo, rows, lanes), lambda g, ids: (0, 0, 0)),
                pl.BlockSpec((TB, rows, lanes), lambda g, ids: (g, 0, 0)),
            ],
            out_specs=pl.BlockSpec((cases, TB * rows, width), lambda g, ids: (0, g, 0)),
            scratch_shapes=[pltpu.VMEM((rows, lanes), jnp.float32)],
        ),
        compiler_params=pltpu.CompilerParams(dimension_semantics=("arbitrary",)),
        cost_estimate=pl.CostEstimate(
            flops=flops // 2,
            transcendentals=0,
            bytes_accessed=kernel_blocks.size * 2 + blocks_here * rows * lanes * 6,
        ),
    )(ids, kernel_blocks, halo_blocks, partial)


def near_bwd_kernel(cases, pairs, rows, steps, ids_ref, kb_ref, back_ref, mid_ref, lo_ref, hi_ref, acc_ref):
    g = pl.program_id(0)

    @pl.when(g == 0)
    def _():
        acc_ref[...] = jnp.zeros(acc_ref.shape, acc_ref.dtype)

    width = back_ref.shape[2]
    for tb in range(TB):
        t = g * TB + tb
        lhs = jnp.concatenate([kb_ref[tb, k] for k in range(pairs)], axis=1)
        rhs = jnp.concatenate(
            [back_ref[c, pl.ds(tb * rows, rows), :] for c in range(cases)], axis=1
        )
        res = lax.dot_general(
            lhs, rhs, (((0,), (0,)), ((), ())), preferred_element_type=jnp.float32
        )
        for k in range(pairs):
            start = pl.multiple_of(ids_ref[t * pairs + k] * rows, rows)
            piece = res[k * rows : (k + 1) * rows]
            for c in range(cases):
                acc_ref[c, pl.ds(start, rows), :] += piece[:, c * width : (c + 1) * width]

    @pl.when(g == steps - 1)
    def _():
        halo_points = lo_ref.shape[1]
        mid_points = mid_ref.shape[1]
        lo_ref[...] = acc_ref[:, :halo_points, :].astype(lo_ref.dtype)
        mid_ref[...] = acc_ref[:, halo_points : halo_points + mid_points, :]
        hi_ref[...] = acc_ref[:, halo_points + mid_points :, :].astype(hi_ref.dtype)


def near_backward(ids, kernel_blocks, back_near, halo_points):
    cases, points_here, width = back_near.shape
    blocks_here, pairs, rows, _ = kernel_blocks.shape
    steps = blocks_here // TB
    span_points = points_here + 2 * halo_points
    flops = 2 * blocks_here * pairs * rows * rows * cases * width
    return pl.pallas_call(
        functools.partial(near_bwd_kernel, cases, pairs, rows, steps),
        out_shape=(
            jax.ShapeDtypeStruct((cases, points_here, width), jnp.float32),
            jax.ShapeDtypeStruct((cases, halo_points, width), jnp.bfloat16),
            jax.ShapeDtypeStruct((cases, halo_points, width), jnp.bfloat16),
        ),
        grid_spec=pltpu.PrefetchScalarGridSpec(
            num_scalar_prefetch=1,
            grid=(steps,),
            in_specs=[
                pl.BlockSpec((TB, pairs, rows, rows), lambda g, ids: (g, 0, 0, 0)),
                pl.BlockSpec((cases, TB * rows, width), lambda g, ids: (0, g, 0)),
            ],
            out_specs=[
                pl.BlockSpec((cases, points_here, width), lambda g, ids: (0, 0, 0)),
                pl.BlockSpec((cases, halo_points, width), lambda g, ids: (0, 0, 0)),
                pl.BlockSpec((cases, halo_points, width), lambda g, ids: (0, 0, 0)),
            ],
            scratch_shapes=[pltpu.VMEM((cases, span_points, width), jnp.float32)],
        ),
        compiler_params=pltpu.CompilerParams(
            dimension_semantics=("arbitrary",), vmem_limit_bytes=60 * 1024 * 1024
        ),
        cost_estimate=pl.CostEstimate(
            flops=flops,
            transcendentals=0,
            bytes_accessed=kernel_blocks.size * 2 + back_near.size * 2 + cases * span_points * width * 4,
        ),
    )(ids, kernel_blocks, back_near)


def on_device(
    features, cotangent, kernel_blocks, near_pairs, leaf_basis, w_near, w_far, translations
):
    cases_here, points_here, width = features.shape
    blocks_here, pair_count, block_rows = (
        kernel_blocks.shape[0],
        kernel_blocks.shape[1],
        kernel_blocks.shape[2],
    )
    halo_points = HALO * block_rows
    span_blocks = blocks_here + 2 * HALO
    position = lax.axis_index("leaf")

    head = features[:, :halo_points]
    tail = features[:, points_here - halo_points :]
    from_prev = shifted(tail, "leaf", 1)
    from_next = shifted(head, "leaf", -1)

    local_ids = jnp.clip(
        near_pairs - (position * blocks_here - HALO), 0, span_blocks - 1
    ).reshape(-1).astype(jnp.int32)

    near_bf = near_forward_split(local_ids, kernel_blocks, features, from_prev, from_next, HALO)

    summary = jnp.einsum("rp,apc->arc", leaf_basis, features, preferred_element_type=jnp.float32)
    expansion, _ = expand(summary, translations, False)
    exp_bf = expansion.astype(jnp.bfloat16)
    far_coeff = jnp.einsum("arc,cd->ard", exp_bf, w_far, preferred_element_type=jnp.float32).astype(
        jnp.bfloat16
    )
    far_field = jnp.einsum("rp,ard->apd", leaf_basis, far_coeff, preferred_element_type=jnp.float32)
    mixed = (
        jnp.einsum("apc,cd->apd", near_bf, w_near, preferred_element_type=jnp.float32) + far_field
    )
    output = jax.nn.gelu(mixed).astype(jnp.bfloat16)
    _, pullback = jax.vjp(jax.nn.gelu, mixed)
    slope = pullback(cotangent.astype(jnp.float32))[0].astype(jnp.bfloat16)
    projected = jnp.einsum(
        "rp,apc->arc", leaf_basis, slope, preferred_element_type=jnp.float32
    ).astype(jnp.bfloat16)
    back_near = jnp.einsum("apc,dc->apd", slope, w_near, preferred_element_type=jnp.float32).astype(
        jnp.bfloat16
    )

    mid, lo, hi = near_backward(local_ids, kernel_blocks, back_near, halo_points)

    scale = 1.0 / math.sqrt(
        cases_here * lax.axis_size("case") * points_here * lax.axis_size("leaf")
    )
    near_term = (
        jnp.einsum("apc,apd->cd", near_bf, slope, preferred_element_type=jnp.float32) * scale
    )
    far_term = (
        jnp.einsum("arc,ard->cd", exp_bf, projected, preferred_element_type=jnp.float32) * scale
    )
    grads = jnp.concatenate([near_term, far_term], axis=0)

    back_coeff = jnp.einsum("arc,dc->ard", projected, w_far, preferred_element_type=jnp.float32)
    back_exp, grads, (mid, lo, hi) = expand(
        back_coeff, translations, True, rider=grads, cover=(mid, lo, hi)
    )
    back_far = jnp.einsum(
        "rp,arc->apc", leaf_basis, back_exp.astype(jnp.bfloat16), preferred_element_type=jnp.float32
    )

    case_depth = lax.axis_size("case").bit_length() - 1
    for height in range(case_depth):
        grads = grads + partner(grads, "case", height)

    got_prev = shifted(hi, "leaf", 1).astype(jnp.float32)
    got_next = shifted(lo, "leaf", -1).astype(jnp.float32)
    near_back = jnp.concatenate(
        [
            mid[:, :halo_points] + got_prev,
            mid[:, halo_points : points_here - halo_points],
            mid[:, points_here - halo_points :] + got_next,
        ],
        axis=1,
    )
    grad_features = (near_back + back_far).astype(jnp.bfloat16)
    grad_near = grads[:width]
    grad_far = grads[width:]
    return (output, grad_features, grad_near, grad_far)


def solution(mesh):
    return jax.shard_map(
        on_device,
        mesh=mesh,
        in_specs=(
            P("case", "leaf", None),
            P("case", "leaf", None),
            P("leaf", None, None, None),
            P("leaf", None),
            P(None, "leaf"),
            P(),
            P(),
            P(),
        ),
        out_specs=(P("case", "leaf", None), P("case", "leaf", None), P(), P()),
        check_vma=False,
    )
```

```python
import functools
import math

import jax
import jax.numpy as jnp
from jax import lax
from jax.experimental import pallas as pl
from jax.experimental.pallas import tpu as pltpu
from jax.sharding import PartitionSpec as P

HALO = 8
TB = 8
BWD_TB = 4


def partner(shard, axis, apart):
    return lax.ppermute(shard, axis, [(i, i ^ 1 << apart) for i in range(lax.axis_size(axis))])


def shifted(value, axis, steps):
    count = lax.axis_size(axis)
    leading, last = (max(0, -steps), min(count, count - steps))
    return lax.ppermute(value, axis, [(source, source + steps) for source in range(leading, last)])


def apply_level(matrix, sibling, flipped):
    if flipped:
        return jnp.einsum("sr,asc->arc", matrix, sibling, precision=lax.Precision.HIGHEST)
    return jnp.einsum("rs,asc->arc", matrix, sibling, precision=lax.Precision.HIGHEST)


def expand(own_value, translations, flipped, rider=None, stages=()):
    depth_count = lax.axis_size("leaf").bit_length() - 1
    summed = jnp.zeros(own_value.shape, jnp.float32)
    node_value = own_value
    rows = own_value.shape[0] * own_value.shape[1]
    staged = None
    for height in range(depth_count):
        if rider is None:
            sibling = partner(node_value, "leaf", height)
        else:
            packed = jnp.concatenate(
                [node_value.reshape(rows, own_value.shape[2]), rider], axis=0
            )
            got = partner(packed, "leaf", height)
            if height < len(stages):
                staged = stages[height](staged)
                got, staged = lax.optimization_barrier((got, staged))
            sibling = got[:rows].reshape(own_value.shape)
            rider = rider + got[rows:]
        summed = summed + apply_level(translations[height], sibling, flipped)
        node_value = node_value + sibling
    return summed, rider, staged


def near_fwd_kernel(cases, pairs, rows, ids_ref, kb_ref, ext_ref, out_ref):
    g = pl.program_id(0)
    for tb in range(TB):
        t = g * TB + tb
        lhs = jnp.concatenate([kb_ref[tb, k] for k in range(pairs)], axis=1)
        parts = []
        for k in range(pairs):
            start = pl.multiple_of(ids_ref[t * pairs + k] * rows, rows)
            parts.append(
                jnp.concatenate([ext_ref[c, pl.ds(start, rows), :] for c in range(cases)], axis=1)
            )
        rhs = jnp.concatenate(parts, axis=0)
        acc = jnp.dot(lhs, rhs, preferred_element_type=jnp.float32)
        width = acc.shape[1] // cases
        for c in range(cases):
            out_ref[c, pl.ds(tb * rows, rows), :] = acc[:, c * width : (c + 1) * width].astype(
                out_ref.dtype
            )


def near_forward(ids, kernel_blocks, extended):
    cases, span_points, width = extended.shape
    blocks_here, pairs, rows, _ = kernel_blocks.shape
    steps = blocks_here // TB
    flops = 2 * blocks_here * pairs * rows * rows * cases * width
    return pl.pallas_call(
        functools.partial(near_fwd_kernel, cases, pairs, rows),
        out_shape=jax.ShapeDtypeStruct((cases, blocks_here * rows, width), jnp.bfloat16),
        grid_spec=pltpu.PrefetchScalarGridSpec(
            num_scalar_prefetch=1,
            grid=(steps,),
            in_specs=[
                pl.BlockSpec((TB, pairs, rows, rows), lambda g, ids: (g, 0, 0, 0)),
                pl.BlockSpec((cases, span_points, width), lambda g, ids: (0, 0, 0)),
            ],
            out_specs=pl.BlockSpec((cases, TB * rows, width), lambda g, ids: (0, g, 0)),
        ),
        compiler_params=pltpu.CompilerParams(dimension_semantics=("arbitrary",)),
        cost_estimate=pl.CostEstimate(
            flops=flops,
            transcendentals=0,
            bytes_accessed=kernel_blocks.size * 2 + extended.size * 2 + cases * blocks_here * rows * width * 2,
        ),
    )(ids, kernel_blocks, extended)


def near_bwd_kernel(cases, pairs, rows, steps, first, carry, ids_ref, kb_ref, back_ref, *refs):
    if carry:
        lo_in, hi_in, mid_ref, lo_ref, hi_ref, acc_ref = refs
    else:
        mid_ref, lo_ref, hi_ref, acc_ref = refs
    g = pl.program_id(0)
    tbs = kb_ref.shape[0]

    @pl.when(g == 0)
    def _():
        acc_ref[...] = jnp.zeros(acc_ref.shape, acc_ref.dtype)

    width = back_ref.shape[2]
    for tb in range(tbs):
        t = first + g * tbs + tb
        lhs = jnp.concatenate([kb_ref[tb, k] for k in range(pairs)], axis=1)
        rhs = jnp.concatenate(
            [back_ref[c, pl.ds(tb * rows, rows), :] for c in range(cases)], axis=1
        )
        res = lax.dot_general(
            lhs, rhs, (((0,), (0,)), ((), ())), preferred_element_type=jnp.float32
        )
        for k in range(pairs):
            start = pl.multiple_of(ids_ref[t * pairs + k] * rows, rows)
            piece = res[k * rows : (k + 1) * rows]
            for c in range(cases):
                acc_ref[c, pl.ds(start, rows), :] += piece[:, c * width : (c + 1) * width]

    @pl.when(g == steps - 1)
    def _():
        halo_points = lo_ref.shape[1]
        mid_points = mid_ref.shape[1]
        lo = acc_ref[:, :halo_points, :]
        hi = acc_ref[:, halo_points + mid_points :, :]
        if carry:
            lo = lo + lo_in[...]
            hi = hi + hi_in[...]
        lo_ref[...] = lo.astype(lo_ref.dtype)
        mid_ref[...] = acc_ref[:, halo_points : halo_points + mid_points, :]
        hi_ref[...] = hi.astype(hi_ref.dtype)


def near_backward(ids, kernel_blocks, back_near, halo_points, first, count, carry=None):
    cases, points_here, width = back_near.shape
    blocks_here, pairs, rows, _ = kernel_blocks.shape
    tbs = BWD_TB
    steps = count // tbs
    offset = first // tbs
    span_points = points_here + 2 * halo_points
    flops = 2 * count * pairs * rows * rows * cases * width
    halo_type = jnp.float32 if carry is None else jnp.bfloat16
    halo_spec = pl.BlockSpec((cases, halo_points, width), lambda g, ids: (0, 0, 0))
    in_specs = [
        pl.BlockSpec((tbs, pairs, rows, rows), lambda g, ids: (g + offset, 0, 0, 0)),
        pl.BlockSpec((cases, tbs * rows, width), lambda g, ids: (0, g + offset, 0)),
    ]
    operands = [ids, kernel_blocks, back_near]
    if carry is not None:
        in_specs += [halo_spec, halo_spec]
        operands += list(carry)
    return pl.pallas_call(
        functools.partial(near_bwd_kernel, cases, pairs, rows, steps, first, carry is not None),
        out_shape=(
            jax.ShapeDtypeStruct((cases, points_here, width), jnp.float32),
            jax.ShapeDtypeStruct((cases, halo_points, width), halo_type),
            jax.ShapeDtypeStruct((cases, halo_points, width), halo_type),
        ),
        grid_spec=pltpu.PrefetchScalarGridSpec(
            num_scalar_prefetch=1,
            grid=(steps,),
            in_specs=in_specs,
            out_specs=[
                pl.BlockSpec((cases, points_here, width), lambda g, ids: (0, 0, 0)),
                halo_spec,
                halo_spec,
            ],
            scratch_shapes=[pltpu.VMEM((cases, span_points, width), jnp.float32)],
        ),
        compiler_params=pltpu.CompilerParams(
            dimension_semantics=("arbitrary",), vmem_limit_bytes=60 * 1024 * 1024
        ),
        cost_estimate=pl.CostEstimate(
            flops=flops,
            transcendentals=0,
            bytes_accessed=count * pairs * rows * rows * 2
            + count * rows * cases * width * 2
            + cases * span_points * width * 4,
        ),
    )(*operands)


def on_device(
    features, cotangent, kernel_blocks, near_pairs, leaf_basis, w_near, w_far, translations
):
    cases_here, points_here, width = features.shape
    blocks_here, pair_count, block_rows = (
        kernel_blocks.shape[0],
        kernel_blocks.shape[1],
        kernel_blocks.shape[2],
    )
    halo_points = HALO * block_rows
    span_blocks = blocks_here + 2 * HALO
    position = lax.axis_index("leaf")

    head = features[:, :halo_points]
    tail = features[:, points_here - halo_points :]
    from_prev = shifted(tail, "leaf", 1)
    from_next = shifted(head, "leaf", -1)
    extended = jnp.concatenate([from_prev, features, from_next], axis=1)
    local_ids = jnp.clip(
        near_pairs - (position * blocks_here - HALO), 0, span_blocks - 1
    ).reshape(-1).astype(jnp.int32)

    near_bf = near_forward(local_ids, kernel_blocks, extended)

    summary = jnp.einsum("rp,apc->arc", leaf_basis, features, preferred_element_type=jnp.float32)
    expansion, _, _ = expand(summary, translations, False)
    exp_bf = expansion.astype(jnp.bfloat16)
    far_coeff = jnp.einsum("arc,cd->ard", exp_bf, w_far, preferred_element_type=jnp.float32).astype(
        jnp.bfloat16
    )
    far_field = jnp.einsum("rp,ard->apd", leaf_basis, far_coeff, preferred_element_type=jnp.float32)
    mixed = (
        jnp.einsum("apc,cd->apd", near_bf, w_near, preferred_element_type=jnp.float32) + far_field
    )
    output = jax.nn.gelu(mixed).astype(jnp.bfloat16)
    _, pullback = jax.vjp(jax.nn.gelu, mixed)
    slope = pullback(cotangent.astype(jnp.float32))[0].astype(jnp.bfloat16)
    projected = jnp.einsum(
        "rp,apc->arc", leaf_basis, slope, preferred_element_type=jnp.float32
    ).astype(jnp.bfloat16)
    back_near = jnp.einsum("apc,dc->apd", slope, w_near, preferred_element_type=jnp.float32).astype(
        jnp.bfloat16
    )


    scale = 1.0 / math.sqrt(
        cases_here * lax.axis_size("case") * points_here * lax.axis_size("leaf")
    )
    near_term = (
        jnp.einsum("apc,apd->cd", near_bf, slope, preferred_element_type=jnp.float32) * scale
    )
    far_term = (
        jnp.einsum("arc,ard->cd", exp_bf, projected, preferred_element_type=jnp.float32) * scale
    )
    grads = jnp.concatenate([near_term, far_term], axis=0)

    back_coeff = jnp.einsum("arc,dc->ard", projected, w_far, preferred_element_type=jnp.float32)
    half = blocks_here // 2

    def first_half(_):
        return near_backward(local_ids, kernel_blocks, back_near, halo_points, 0, half)

    def second_half(prev):
        mid_first, lo_first, hi_first = prev
        mid_second, lo, hi = near_backward(
            local_ids, kernel_blocks, back_near, halo_points, half, blocks_here - half,
            carry=(lo_first, hi_first),
        )
        return mid_first + mid_second, lo, hi

    back_exp, grads, (mid, lo, hi) = expand(
        back_coeff, translations, True, rider=grads, stages=(first_half, second_half)
    )
    back_far = jnp.einsum(
        "rp,arc->apc", leaf_basis, back_exp.astype(jnp.bfloat16), preferred_element_type=jnp.float32
    )

    case_depth = lax.axis_size("case").bit_length() - 1
    for height in range(case_depth):
        grads = grads + partner(grads, "case", height)

    got_prev = shifted(hi, "leaf", 1).astype(jnp.float32)
    got_next = shifted(lo, "leaf", -1).astype(jnp.float32)
    near_back = jnp.concatenate(
        [
            mid[:, :halo_points] + got_prev,
            mid[:, halo_points : points_here - halo_points],
            mid[:, points_here - halo_points :] + got_next,
        ],
        axis=1,
    )
    grad_features = (near_back + back_far).astype(jnp.bfloat16)
    grad_near = grads[:width]
    grad_far = grads[width:]
    return (output, grad_features, grad_near, grad_far)


def solution(mesh):
    return jax.shard_map(
        on_device,
        mesh=mesh,
        in_specs=(
            P("case", "leaf", None),
            P("case", "leaf", None),
            P("leaf", None, None, None),
            P("leaf", None),
            P(None, "leaf"),
            P(),
            P(),
            P(),
        ),
        out_specs=(P("case", "leaf", None), P("case", "leaf", None), P(), P()),
        check_vma=False,
    )
```

```python
import functools
import math

import jax
import jax.numpy as jnp
from jax import lax
from jax.experimental import pallas as pl
from jax.experimental.pallas import tpu as pltpu
from jax.sharding import PartitionSpec as P

HALO = 8
TB = 8
BWD_TB = 4


def partner(shard, axis, apart):
    return lax.ppermute(shard, axis, [(i, i ^ 1 << apart) for i in range(lax.axis_size(axis))])


def shifted(value, axis, steps):
    count = lax.axis_size(axis)
    leading, last = (max(0, -steps), min(count, count - steps))
    return lax.ppermute(value, axis, [(source, source + steps) for source in range(leading, last)])


def apply_level(matrix, sibling, flipped):
    if flipped:
        return jnp.einsum("sr,asc->arc", matrix, sibling, precision=lax.Precision.HIGHEST)
    return jnp.einsum("rs,asc->arc", matrix, sibling, precision=lax.Precision.HIGHEST)


def expand(own_value, translations, flipped, rider=None, cover=None):
    depth_count = lax.axis_size("leaf").bit_length() - 1
    summed = jnp.zeros(own_value.shape, jnp.float32)
    node_value = own_value
    rows = own_value.shape[0] * own_value.shape[1]
    for height in range(depth_count):
        if rider is None:
            sibling = partner(node_value, "leaf", height)
        else:
            packed = jnp.concatenate(
                [node_value.reshape(rows, own_value.shape[2]), rider], axis=0
            )
            got = partner(packed, "leaf", height)
            if cover is not None and height < 2:
                got, cover = lax.optimization_barrier((got, cover))
            sibling = got[:rows].reshape(own_value.shape)
            rider = rider + got[rows:]
        summed = summed + apply_level(translations[height], sibling, flipped)
        node_value = node_value + sibling
    if cover is None:
        return summed, rider
    return summed, rider, cover


def near_fwd_kernel(cases, pairs, rows, ids_ref, kb_ref, prev_hbm, own_hbm, next_hbm, out_ref, ext_ref, sems):
    g = pl.program_id(0)
    halo_points = prev_hbm.shape[1]
    own_points = own_hbm.shape[1]

    @pl.when(g == 0)
    def _():
        copies = [
            pltpu.make_async_copy(prev_hbm, ext_ref.at[:, pl.ds(0, halo_points), :], sems.at[0]),
            pltpu.make_async_copy(own_hbm, ext_ref.at[:, pl.ds(halo_points, own_points), :], sems.at[1]),
            pltpu.make_async_copy(
                next_hbm, ext_ref.at[:, pl.ds(halo_points + own_points, halo_points), :], sems.at[2]
            ),
        ]
        for copy in copies:
            copy.start()
        for copy in copies:
            copy.wait()

    tbs = kb_ref.shape[0]
    for tb in range(tbs):
        t = g * tbs + tb
        lhs = jnp.concatenate([kb_ref[tb, k] for k in range(pairs)], axis=1)
        parts = []
        for k in range(pairs):
            start = pl.multiple_of(ids_ref[t * pairs + k] * rows, rows)
            parts.append(
                jnp.concatenate([ext_ref[c, pl.ds(start, rows), :] for c in range(cases)], axis=1)
            )
        rhs = jnp.concatenate(parts, axis=0)
        acc = jnp.dot(lhs, rhs, preferred_element_type=jnp.float32)
        width = acc.shape[1] // cases
        for c in range(cases):
            out_ref[c, pl.ds(tb * rows, rows), :] = acc[:, c * width : (c + 1) * width].astype(
                out_ref.dtype
            )


def near_forward(ids, kernel_blocks, from_prev, features, from_next):
    cases, points_here, width = features.shape
    span_points = points_here + from_prev.shape[1] + from_next.shape[1]
    blocks_here, pairs, rows, _ = kernel_blocks.shape
    steps = blocks_here // TB
    flops = 2 * blocks_here * pairs * rows * rows * cases * width
    hbm = pl.BlockSpec(memory_space=pl.ANY)
    return pl.pallas_call(
        functools.partial(near_fwd_kernel, cases, pairs, rows),
        out_shape=jax.ShapeDtypeStruct((cases, blocks_here * rows, width), jnp.bfloat16),
        grid_spec=pltpu.PrefetchScalarGridSpec(
            num_scalar_prefetch=1,
            grid=(steps,),
            in_specs=[
                pl.BlockSpec((TB, pairs, rows, rows), lambda g, ids: (g, 0, 0, 0)),
                hbm,
                hbm,
                hbm,
            ],
            out_specs=pl.BlockSpec((cases, TB * rows, width), lambda g, ids: (0, g, 0)),
            scratch_shapes=[
                pltpu.VMEM((cases, span_points, width), jnp.bfloat16),
                pltpu.SemaphoreType.DMA((3,)),
            ],
        ),
        compiler_params=pltpu.CompilerParams(dimension_semantics=("arbitrary",)),
        cost_estimate=pl.CostEstimate(
            flops=flops,
            transcendentals=0,
            bytes_accessed=kernel_blocks.size * 2 + cases * span_points * width * 2 + cases * blocks_here * rows * width * 2,
        ),
    )(ids, kernel_blocks, from_prev, features, from_next)


def near_bwd_kernel(cases, pairs, rows, steps, ids_ref, kb_ref, back_ref, mid_ref, lo_ref, hi_ref, acc_ref):
    g = pl.program_id(0)

    @pl.when(g == 0)
    def _():
        acc_ref[...] = jnp.zeros(acc_ref.shape, acc_ref.dtype)

    width = back_ref.shape[2]
    for tb in range(BWD_TB):
        t = g * BWD_TB + tb
        rhs = jnp.concatenate(
            [back_ref[c, pl.ds(tb * rows, rows), :] for c in range(cases)], axis=1
        )
        for k in range(pairs):
            start = pl.multiple_of(ids_ref[t * pairs + k] * rows, rows)
            piece = lax.dot_general(
                kb_ref[tb, k], rhs, (((0,), (0,)), ((), ())), preferred_element_type=jnp.float32
            )
            for c in range(cases):
                acc_ref[c, pl.ds(start, rows), :] += piece[:, c * width : (c + 1) * width]

    @pl.when(g == steps - 1)
    def _():
        halo_points = lo_ref.shape[1]
        mid_points = mid_ref.shape[1]
        lo_ref[...] = acc_ref[:, :halo_points, :].astype(lo_ref.dtype)
        mid_ref[...] = acc_ref[:, halo_points : halo_points + mid_points, :]
        hi_ref[...] = acc_ref[:, halo_points + mid_points :, :].astype(hi_ref.dtype)


def near_backward(ids, kernel_blocks, back_near, halo_points):
    cases, points_here, width = back_near.shape
    blocks_here, pairs, rows, _ = kernel_blocks.shape
    steps = blocks_here // BWD_TB
    span_points = points_here + 2 * halo_points
    flops = 2 * blocks_here * pairs * rows * rows * cases * width
    return pl.pallas_call(
        functools.partial(near_bwd_kernel, cases, pairs, rows, steps),
        out_shape=(
            jax.ShapeDtypeStruct((cases, points_here, width), jnp.float32),
            jax.ShapeDtypeStruct((cases, halo_points, width), jnp.bfloat16),
            jax.ShapeDtypeStruct((cases, halo_points, width), jnp.bfloat16),
        ),
        grid_spec=pltpu.PrefetchScalarGridSpec(
            num_scalar_prefetch=1,
            grid=(steps,),
            in_specs=[
                pl.BlockSpec((BWD_TB, pairs, rows, rows), lambda g, ids: (g, 0, 0, 0)),
                pl.BlockSpec((cases, BWD_TB * rows, width), lambda g, ids: (0, g, 0)),
            ],
            out_specs=[
                pl.BlockSpec((cases, points_here, width), lambda g, ids: (0, 0, 0)),
                pl.BlockSpec((cases, halo_points, width), lambda g, ids: (0, 0, 0)),
                pl.BlockSpec((cases, halo_points, width), lambda g, ids: (0, 0, 0)),
            ],
            scratch_shapes=[pltpu.VMEM((cases, span_points, width), jnp.float32)],
        ),
        compiler_params=pltpu.CompilerParams(
            dimension_semantics=("arbitrary",), vmem_limit_bytes=60 * 1024 * 1024
        ),
        cost_estimate=pl.CostEstimate(
            flops=flops,
            transcendentals=0,
            bytes_accessed=kernel_blocks.size * 2 + back_near.size * 2 + cases * span_points * width * 4,
        ),
    )(ids, kernel_blocks, back_near)


def on_device(
    features, cotangent, kernel_blocks, near_pairs, leaf_basis, w_near, w_far, translations
):
    cases_here, points_here, width = features.shape
    blocks_here, pair_count, block_rows = (
        kernel_blocks.shape[0],
        kernel_blocks.shape[1],
        kernel_blocks.shape[2],
    )
    halo_points = HALO * block_rows
    span_blocks = blocks_here + 2 * HALO
    position = lax.axis_index("leaf")

    head = features[:, :halo_points]
    tail = features[:, points_here - halo_points :]
    from_prev = shifted(tail, "leaf", 1)
    from_next = shifted(head, "leaf", -1)
    local_ids = jnp.clip(
        near_pairs - (position * blocks_here - HALO), 0, span_blocks - 1
    ).reshape(-1).astype(jnp.int32)

    near_bf = near_forward(local_ids, kernel_blocks, from_prev, features, from_next)

    summary = jnp.einsum("rp,apc->arc", leaf_basis, features, preferred_element_type=jnp.float32)
    expansion, _ = expand(summary, translations, False)
    exp_bf = expansion.astype(jnp.bfloat16)
    far_coeff = jnp.einsum("arc,cd->ard", exp_bf, w_far, preferred_element_type=jnp.float32).astype(
        jnp.bfloat16
    )
    far_field = jnp.einsum("rp,ard->apd", leaf_basis, far_coeff, preferred_element_type=jnp.float32)
    mixed = (
        jnp.einsum("apc,cd->apd", near_bf, w_near, preferred_element_type=jnp.float32) + far_field
    )
    output = jax.nn.gelu(mixed).astype(jnp.bfloat16)
    _, pullback = jax.vjp(jax.nn.gelu, mixed)
    slope = pullback(cotangent.astype(jnp.float32))[0].astype(jnp.bfloat16)
    projected = jnp.einsum(
        "rp,apc->arc", leaf_basis, slope, preferred_element_type=jnp.float32
    ).astype(jnp.bfloat16)
    back_near = jnp.einsum("apc,dc->apd", slope, w_near, preferred_element_type=jnp.float32).astype(
        jnp.bfloat16
    )

    mid, lo, hi = near_backward(local_ids, kernel_blocks, back_near, halo_points)

    scale = 1.0 / math.sqrt(
        cases_here * lax.axis_size("case") * points_here * lax.axis_size("leaf")
    )
    near_term = (
        jnp.einsum("apc,apd->cd", near_bf, slope, preferred_element_type=jnp.float32) * scale
    )
    far_term = (
        jnp.einsum("arc,ard->cd", exp_bf, projected, preferred_element_type=jnp.float32) * scale
    )
    grads = jnp.concatenate([near_term, far_term], axis=0)

    back_coeff = jnp.einsum("arc,dc->ard", projected, w_far, preferred_element_type=jnp.float32)
    back_exp, grads, (mid, lo, hi) = expand(
        back_coeff, translations, True, rider=grads, cover=(mid, lo, hi)
    )
    back_far = jnp.einsum(
        "rp,arc->apc", leaf_basis, back_exp.astype(jnp.bfloat16), preferred_element_type=jnp.float32
    )

    case_depth = lax.axis_size("case").bit_length() - 1
    for height in range(case_depth):
        grads = grads + partner(grads, "case", height)

    got_prev = shifted(hi, "leaf", 1).astype(jnp.float32)
    got_next = shifted(lo, "leaf", -1).astype(jnp.float32)
    near_back = jnp.concatenate(
        [
            mid[:, :halo_points] + got_prev,
            mid[:, halo_points : points_here - halo_points],
            mid[:, points_here - halo_points :] + got_next,
        ],
        axis=1,
    )
    grad_features = (near_back + back_far).astype(jnp.bfloat16)
    grad_near = grads[:width]
    grad_far = grads[width:]
    return (output, grad_features, grad_near, grad_far)


def solution(mesh):
    return jax.shard_map(
        on_device,
        mesh=mesh,
        in_specs=(
            P("case", "leaf", None),
            P("case", "leaf", None),
            P("leaf", None, None, None),
            P("leaf", None),
            P(None, "leaf"),
            P(),
            P(),
            P(),
        ),
        out_specs=(P("case", "leaf", None), P("case", "leaf", None), P(), P()),
        check_vma=False,
    )
```

```python
import functools
import math

import jax
import jax.numpy as jnp
from jax import lax
from jax.experimental import pallas as pl
from jax.experimental.pallas import tpu as pltpu
from jax.sharding import PartitionSpec as P

HALO = 8
TB = 8
BWD_TB = 4


def partner(shard, axis, apart):
    return lax.ppermute(shard, axis, [(i, i ^ 1 << apart) for i in range(lax.axis_size(axis))])


def shifted(value, axis, steps):
    count = lax.axis_size(axis)
    leading, last = (max(0, -steps), min(count, count - steps))
    return lax.ppermute(value, axis, [(source, source + steps) for source in range(leading, last)])


def apply_level(matrix, sibling, flipped):
    if flipped:
        return jnp.einsum("sr,asc->arc", matrix, sibling, precision=lax.Precision.HIGHEST)
    return jnp.einsum("rs,asc->arc", matrix, sibling, precision=lax.Precision.HIGHEST)


def expand(own_value, translations, flipped, rider=None, cover=None):
    depth_count = lax.axis_size("leaf").bit_length() - 1
    summed = jnp.zeros(own_value.shape, jnp.float32)
    node_value = own_value
    rows = own_value.shape[0] * own_value.shape[1]
    for height in range(depth_count):
        if rider is None:
            sibling = partner(node_value, "leaf", height)
        else:
            packed = jnp.concatenate(
                [node_value.reshape(rows, own_value.shape[2]), rider], axis=0
            )
            got = partner(packed, "leaf", height)
            if cover is not None and height < 2:
                got, cover = lax.optimization_barrier((got, cover))
            sibling = got[:rows].reshape(own_value.shape)
            rider = rider + got[rows:]
        summed = summed + apply_level(translations[height], sibling, flipped)
        node_value = node_value + sibling
    if cover is None:
        return summed, rider
    return summed, rider, cover


def near_fwd_kernel(
    cases, pairs, rows, ids_ref, kb_ref, prev_hbm, own_hbm, next_hbm, basis_ref, coeff_ref,
    w_ref, cot_ref, near_ref, out_ref, slope_ref, back_ref, ext_ref, sems,
):
    g = pl.program_id(0)
    halo_points = prev_hbm.shape[1]
    own_points = own_hbm.shape[1]

    @pl.when(g == 0)
    def _():
        copies = [
            pltpu.make_async_copy(prev_hbm, ext_ref.at[:, pl.ds(0, halo_points), :], sems.at[0]),
            pltpu.make_async_copy(own_hbm, ext_ref.at[:, pl.ds(halo_points, own_points), :], sems.at[1]),
            pltpu.make_async_copy(
                next_hbm, ext_ref.at[:, pl.ds(halo_points + own_points, halo_points), :], sems.at[2]
            ),
        ]
        for copy in copies:
            copy.start()
        for copy in copies:
            copy.wait()

    tbs = kb_ref.shape[0]
    w = w_ref[...]
    for tb in range(tbs):
        t = g * tbs + tb
        lhs = jnp.concatenate([kb_ref[tb, k] for k in range(pairs)], axis=1)
        parts = []
        for k in range(pairs):
            start = pl.multiple_of(ids_ref[t * pairs + k] * rows, rows)
            parts.append(
                jnp.concatenate([ext_ref[c, pl.ds(start, rows), :] for c in range(cases)], axis=1)
            )
        rhs = jnp.concatenate(parts, axis=0)
        acc = jnp.dot(lhs, rhs, preferred_element_type=jnp.float32)
        width = acc.shape[1] // cases
        basis = basis_ref[:, pl.ds(tb * rows, rows)]
        here = pl.ds(tb * rows, rows)
        for c in range(cases):
            near = acc[:, c * width : (c + 1) * width].astype(jnp.bfloat16)
            near_ref[c, here, :] = near
            far = lax.dot_general(
                basis, coeff_ref[c], (((0,), (0,)), ((), ())), preferred_element_type=jnp.float32
            )
            mixed = jnp.dot(near, w, preferred_element_type=jnp.float32) + far
            gelu_value, pullback = jax.vjp(jax.nn.gelu, mixed)
            out_ref[c, here, :] = gelu_value.astype(out_ref.dtype)
            slope = pullback(cot_ref[c, here, :].astype(jnp.float32))[0].astype(jnp.bfloat16)
            slope_ref[c, here, :] = slope
            back_ref[c, here, :] = lax.dot_general(
                slope, w, (((1,), (1,)), ((), ())), preferred_element_type=jnp.float32
            ).astype(back_ref.dtype)


def near_forward(ids, kernel_blocks, from_prev, features, from_next, leaf_basis, far_coeff, w_near, cotangent):
    cases, points_here, width = features.shape
    span_points = points_here + from_prev.shape[1] + from_next.shape[1]
    blocks_here, pairs, rows, _ = kernel_blocks.shape
    rank = leaf_basis.shape[0]
    steps = blocks_here // TB
    flops = 2 * blocks_here * pairs * rows * rows * cases * width
    hbm = pl.BlockSpec(memory_space=pl.ANY)
    block = pl.BlockSpec((cases, TB * rows, width), lambda g, ids: (0, g, 0))
    result = jax.ShapeDtypeStruct((cases, blocks_here * rows, width), jnp.bfloat16)
    return pl.pallas_call(
        functools.partial(near_fwd_kernel, cases, pairs, rows),
        out_shape=(result, result, result, result),
        grid_spec=pltpu.PrefetchScalarGridSpec(
            num_scalar_prefetch=1,
            grid=(steps,),
            in_specs=[
                pl.BlockSpec((TB, pairs, rows, rows), lambda g, ids: (g, 0, 0, 0)),
                hbm,
                hbm,
                hbm,
                pl.BlockSpec((rank, TB * rows), lambda g, ids: (0, g)),
                pl.BlockSpec((cases, rank, width), lambda g, ids: (0, 0, 0)),
                pl.BlockSpec((width, width), lambda g, ids: (0, 0)),
                block,
            ],
            out_specs=[block, block, block, block],
            scratch_shapes=[
                pltpu.VMEM((cases, span_points, width), jnp.bfloat16),
                pltpu.SemaphoreType.DMA((3,)),
            ],
        ),
        compiler_params=pltpu.CompilerParams(dimension_semantics=("arbitrary",)),
        cost_estimate=pl.CostEstimate(
            flops=flops + 6 * cases * points_here * width * width,
            transcendentals=cases * points_here * width,
            bytes_accessed=kernel_blocks.size * 2 + cases * span_points * width * 2 + 5 * cases * points_here * width * 2,
        ),
    )(ids, kernel_blocks, from_prev, features, from_next, leaf_basis, far_coeff, w_near, cotangent)


def near_bwd_kernel(cases, pairs, rows, steps, ids_ref, kb_ref, back_ref, mid_ref, lo_ref, hi_ref, acc_ref):
    g = pl.program_id(0)

    @pl.when(g == 0)
    def _():
        acc_ref[...] = jnp.zeros(acc_ref.shape, acc_ref.dtype)

    width = back_ref.shape[2]
    for tb in range(BWD_TB):
        t = g * BWD_TB + tb
        rhs = jnp.concatenate(
            [back_ref[c, pl.ds(tb * rows, rows), :] for c in range(cases)], axis=1
        )
        for k in range(pairs):
            start = pl.multiple_of(ids_ref[t * pairs + k] * rows, rows)
            piece = lax.dot_general(
                kb_ref[tb, k], rhs, (((0,), (0,)), ((), ())), preferred_element_type=jnp.float32
            )
            for c in range(cases):
                acc_ref[c, pl.ds(start, rows), :] += piece[:, c * width : (c + 1) * width]

    @pl.when(g == steps - 1)
    def _():
        halo_points = lo_ref.shape[1]
        mid_points = mid_ref.shape[1]
        lo_ref[...] = acc_ref[:, :halo_points, :].astype(lo_ref.dtype)
        mid_ref[...] = acc_ref[:, halo_points : halo_points + mid_points, :]
        hi_ref[...] = acc_ref[:, halo_points + mid_points :, :].astype(hi_ref.dtype)


def near_backward(ids, kernel_blocks, back_near, halo_points):
    cases, points_here, width = back_near.shape
    blocks_here, pairs, rows, _ = kernel_blocks.shape
    steps = blocks_here // BWD_TB
    span_points = points_here + 2 * halo_points
    flops = 2 * blocks_here * pairs * rows * rows * cases * width
    return pl.pallas_call(
        functools.partial(near_bwd_kernel, cases, pairs, rows, steps),
        out_shape=(
            jax.ShapeDtypeStruct((cases, points_here, width), jnp.float32),
            jax.ShapeDtypeStruct((cases, halo_points, width), jnp.bfloat16),
            jax.ShapeDtypeStruct((cases, halo_points, width), jnp.bfloat16),
        ),
        grid_spec=pltpu.PrefetchScalarGridSpec(
            num_scalar_prefetch=1,
            grid=(steps,),
            in_specs=[
                pl.BlockSpec((BWD_TB, pairs, rows, rows), lambda g, ids: (g, 0, 0, 0)),
                pl.BlockSpec((cases, BWD_TB * rows, width), lambda g, ids: (0, g, 0)),
            ],
            out_specs=[
                pl.BlockSpec((cases, points_here, width), lambda g, ids: (0, 0, 0)),
                pl.BlockSpec((cases, halo_points, width), lambda g, ids: (0, 0, 0)),
                pl.BlockSpec((cases, halo_points, width), lambda g, ids: (0, 0, 0)),
            ],
            scratch_shapes=[pltpu.VMEM((cases, span_points, width), jnp.float32)],
        ),
        compiler_params=pltpu.CompilerParams(
            dimension_semantics=("arbitrary",), vmem_limit_bytes=60 * 1024 * 1024
        ),
        cost_estimate=pl.CostEstimate(
            flops=flops,
            transcendentals=0,
            bytes_accessed=kernel_blocks.size * 2 + back_near.size * 2 + cases * span_points * width * 4,
        ),
    )(ids, kernel_blocks, back_near)


def on_device(
    features, cotangent, kernel_blocks, near_pairs, leaf_basis, w_near, w_far, translations
):
    cases_here, points_here, width = features.shape
    blocks_here, pair_count, block_rows = (
        kernel_blocks.shape[0],
        kernel_blocks.shape[1],
        kernel_blocks.shape[2],
    )
    halo_points = HALO * block_rows
    span_blocks = blocks_here + 2 * HALO
    position = lax.axis_index("leaf")

    head = features[:, :halo_points]
    tail = features[:, points_here - halo_points :]
    from_prev = shifted(tail, "leaf", 1)
    from_next = shifted(head, "leaf", -1)
    local_ids = jnp.clip(
        near_pairs - (position * blocks_here - HALO), 0, span_blocks - 1
    ).reshape(-1).astype(jnp.int32)

    summary = jnp.einsum("rp,apc->arc", leaf_basis, features, preferred_element_type=jnp.float32)
    expansion, _ = expand(summary, translations, False)
    exp_bf = expansion.astype(jnp.bfloat16)
    far_coeff = jnp.einsum("arc,cd->ard", exp_bf, w_far, preferred_element_type=jnp.float32).astype(
        jnp.bfloat16
    )
    near_bf, output, slope, back_near = near_forward(
        local_ids, kernel_blocks, from_prev, features, from_next, leaf_basis, far_coeff, w_near,
        cotangent,
    )
    projected = jnp.einsum(
        "rp,apc->arc", leaf_basis, slope, preferred_element_type=jnp.float32
    ).astype(jnp.bfloat16)
    mid, lo, hi = near_backward(local_ids, kernel_blocks, back_near, halo_points)

    scale = 1.0 / math.sqrt(
        cases_here * lax.axis_size("case") * points_here * lax.axis_size("leaf")
    )
    near_term = (
        jnp.einsum("apc,apd->cd", near_bf, slope, preferred_element_type=jnp.float32) * scale
    )
    far_term = (
        jnp.einsum("arc,ard->cd", exp_bf, projected, preferred_element_type=jnp.float32) * scale
    )
    grads = jnp.concatenate([near_term, far_term], axis=0)

    back_coeff = jnp.einsum("arc,dc->ard", projected, w_far, preferred_element_type=jnp.float32)
    back_exp, grads, (mid, lo, hi) = expand(
        back_coeff, translations, True, rider=grads, cover=(mid, lo, hi)
    )
    back_far = jnp.einsum(
        "rp,arc->apc", leaf_basis, back_exp.astype(jnp.bfloat16), preferred_element_type=jnp.float32
    )

    case_depth = lax.axis_size("case").bit_length() - 1
    for height in range(case_depth):
        grads = grads + partner(grads, "case", height)

    got_prev = shifted(hi, "leaf", 1).astype(jnp.float32)
    got_next = shifted(lo, "leaf", -1).astype(jnp.float32)
    near_back = jnp.concatenate(
        [
            mid[:, :halo_points] + got_prev,
            mid[:, halo_points : points_here - halo_points],
            mid[:, points_here - halo_points :] + got_next,
        ],
        axis=1,
    )
    grad_features = (near_back + back_far).astype(jnp.bfloat16)
    grad_near = grads[:width]
    grad_far = grads[width:]
    return (output, grad_features, grad_near, grad_far)


def solution(mesh):
    return jax.shard_map(
        on_device,
        mesh=mesh,
        in_specs=(
            P("case", "leaf", None),
            P("case", "leaf", None),
            P("leaf", None, None, None),
            P("leaf", None),
            P(None, "leaf"),
            P(),
            P(),
            P(),
        ),
        out_specs=(P("case", "leaf", None), P("case", "leaf", None), P(), P()),
        check_vma=False,
    )
```

```python
import functools
import math

import jax
import jax.numpy as jnp
from jax import lax
from jax.experimental import pallas as pl
from jax.experimental.pallas import tpu as pltpu
from jax.sharding import PartitionSpec as P

HALO = 8
TB = 8
BWD_TB = 4


def partner(shard, axis, apart):
    return lax.ppermute(shard, axis, [(i, i ^ 1 << apart) for i in range(lax.axis_size(axis))])


def shifted(value, axis, steps):
    count = lax.axis_size(axis)
    leading, last = (max(0, -steps), min(count, count - steps))
    return lax.ppermute(value, axis, [(source, source + steps) for source in range(leading, last)])


def apply_level(matrix, sibling, flipped):
    if flipped:
        return jnp.einsum("sr,asc->arc", matrix, sibling, precision=lax.Precision.HIGHEST)
    return jnp.einsum("rs,asc->arc", matrix, sibling, precision=lax.Precision.HIGHEST)


def expand(own_value, translations, flipped, rider=None, cover=None):
    depth_count = lax.axis_size("leaf").bit_length() - 1
    summed = jnp.zeros(own_value.shape, jnp.float32)
    node_value = own_value
    rows = own_value.shape[0] * own_value.shape[1]
    for height in range(depth_count):
        if rider is None:
            sibling = partner(node_value, "leaf", height)
        else:
            packed = jnp.concatenate(
                [node_value.reshape(rows, own_value.shape[2]), rider], axis=0
            )
            got = partner(packed, "leaf", height)
            if cover is not None and height < 2:
                got, cover = lax.optimization_barrier((got, cover))
            sibling = got[:rows].reshape(own_value.shape)
            rider = rider + got[rows:]
        summed = summed + apply_level(translations[height], sibling, flipped)
        node_value = node_value + sibling
    if cover is None:
        return summed, rider
    return summed, rider, cover


def near_fwd_kernel(cases, pairs, rows, ids_ref, kb_ref, prev_hbm, own_hbm, next_hbm, out_ref, ext_ref, sems):
    g = pl.program_id(0)
    halo_points = prev_hbm.shape[1]
    own_points = own_hbm.shape[1]

    @pl.when(g == 0)
    def _():
        copies = [
            pltpu.make_async_copy(prev_hbm, ext_ref.at[:, pl.ds(0, halo_points), :], sems.at[0]),
            pltpu.make_async_copy(own_hbm, ext_ref.at[:, pl.ds(halo_points, own_points), :], sems.at[1]),
            pltpu.make_async_copy(
                next_hbm, ext_ref.at[:, pl.ds(halo_points + own_points, halo_points), :], sems.at[2]
            ),
        ]
        for copy in copies:
            copy.start()
        for copy in copies:
            copy.wait()

    tbs = kb_ref.shape[0]
    for tb in range(tbs):
        t = g * tbs + tb
        lhs = jnp.concatenate([kb_ref[tb, k] for k in range(pairs)], axis=1)
        parts = []
        for k in range(pairs):
            start = pl.multiple_of(ids_ref[t * pairs + k] * rows, rows)
            parts.append(
                jnp.concatenate([ext_ref[c, pl.ds(start, rows), :] for c in range(cases)], axis=1)
            )
        rhs = jnp.concatenate(parts, axis=0)
        acc = jnp.dot(lhs, rhs, preferred_element_type=jnp.float32)
        width = acc.shape[1] // cases
        for c in range(cases):
            out_ref[c, pl.ds(tb * rows, rows), :] = acc[:, c * width : (c + 1) * width].astype(
                out_ref.dtype
            )


def near_forward(ids, kernel_blocks, from_prev, features, from_next):
    cases, points_here, width = features.shape
    span_points = points_here + from_prev.shape[1] + from_next.shape[1]
    blocks_here, pairs, rows, _ = kernel_blocks.shape
    steps = blocks_here // TB
    flops = 2 * blocks_here * pairs * rows * rows * cases * width
    hbm = pl.BlockSpec(memory_space=pl.ANY)
    return pl.pallas_call(
        functools.partial(near_fwd_kernel, cases, pairs, rows),
        out_shape=jax.ShapeDtypeStruct((cases, blocks_here * rows, width), jnp.bfloat16),
        grid_spec=pltpu.PrefetchScalarGridSpec(
            num_scalar_prefetch=1,
            grid=(steps,),
            in_specs=[
                pl.BlockSpec((TB, pairs, rows, rows), lambda g, ids: (g, 0, 0, 0)),
                hbm,
                hbm,
                hbm,
            ],
            out_specs=pl.BlockSpec((cases, TB * rows, width), lambda g, ids: (0, g, 0)),
            scratch_shapes=[
                pltpu.VMEM((cases, span_points, width), jnp.bfloat16),
                pltpu.SemaphoreType.DMA((3,)),
            ],
        ),
        compiler_params=pltpu.CompilerParams(dimension_semantics=("arbitrary",)),
        cost_estimate=pl.CostEstimate(
            flops=flops,
            transcendentals=0,
            bytes_accessed=kernel_blocks.size * 2 + cases * span_points * width * 2 + cases * blocks_here * rows * width * 2,
        ),
    )(ids, kernel_blocks, from_prev, features, from_next)


def near_bwd_kernel(cases, pairs, rows, steps, ids_ref, kb_ref, back_ref, mid_ref, lo_ref, hi_ref, acc_ref):
    g = pl.program_id(0)

    @pl.when(g == 0)
    def _():
        acc_ref[...] = jnp.zeros(acc_ref.shape, acc_ref.dtype)

    width = back_ref.shape[2]
    for tb in range(BWD_TB):
        t = g * BWD_TB + tb
        rhs = jnp.concatenate(
            [back_ref[c, pl.ds(tb * rows, rows), :] for c in range(cases)], axis=1
        )
        for k in range(pairs):
            start = pl.multiple_of(ids_ref[t * pairs + k] * rows, rows)
            piece = lax.dot_general(
                kb_ref[tb, k], rhs, (((0,), (0,)), ((), ())), preferred_element_type=jnp.float32
            )
            for c in range(cases):
                acc_ref[c, pl.ds(start, rows), :] += piece[:, c * width : (c + 1) * width]

    @pl.when(g == steps - 1)
    def _():
        halo_points = lo_ref.shape[1]
        mid_points = mid_ref.shape[1]
        lo_ref[...] = acc_ref[:, :halo_points, :].astype(lo_ref.dtype)
        mid_ref[...] = acc_ref[:, halo_points : halo_points + mid_points, :]
        hi_ref[...] = acc_ref[:, halo_points + mid_points :, :].astype(hi_ref.dtype)


def near_backward(ids, kernel_blocks, back_near, halo_points):
    cases, points_here, width = back_near.shape
    blocks_here, pairs, rows, _ = kernel_blocks.shape
    steps = blocks_here // BWD_TB
    span_points = points_here + 2 * halo_points
    flops = 2 * blocks_here * pairs * rows * rows * cases * width
    return pl.pallas_call(
        functools.partial(near_bwd_kernel, cases, pairs, rows, steps),
        out_shape=(
            jax.ShapeDtypeStruct((cases, points_here, width), jnp.float32),
            jax.ShapeDtypeStruct((cases, halo_points, width), jnp.bfloat16),
            jax.ShapeDtypeStruct((cases, halo_points, width), jnp.bfloat16),
        ),
        grid_spec=pltpu.PrefetchScalarGridSpec(
            num_scalar_prefetch=1,
            grid=(steps,),
            in_specs=[
                pl.BlockSpec((BWD_TB, pairs, rows, rows), lambda g, ids: (g, 0, 0, 0)),
                pl.BlockSpec((cases, BWD_TB * rows, width), lambda g, ids: (0, g, 0)),
            ],
            out_specs=[
                pl.BlockSpec((cases, points_here, width), lambda g, ids: (0, 0, 0)),
                pl.BlockSpec((cases, halo_points, width), lambda g, ids: (0, 0, 0)),
                pl.BlockSpec((cases, halo_points, width), lambda g, ids: (0, 0, 0)),
            ],
            scratch_shapes=[pltpu.VMEM((cases, span_points, width), jnp.float32)],
        ),
        compiler_params=pltpu.CompilerParams(
            dimension_semantics=("arbitrary",), vmem_limit_bytes=60 * 1024 * 1024
        ),
        cost_estimate=pl.CostEstimate(
            flops=flops,
            transcendentals=0,
            bytes_accessed=kernel_blocks.size * 2 + back_near.size * 2 + cases * span_points * width * 4,
        ),
    )(ids, kernel_blocks, back_near)


def on_device(
    features, cotangent, kernel_blocks, near_pairs, leaf_basis, w_near, w_far, translations
):
    cases_here, points_here, width = features.shape
    blocks_here, pair_count, block_rows = (
        kernel_blocks.shape[0],
        kernel_blocks.shape[1],
        kernel_blocks.shape[2],
    )
    halo_points = HALO * block_rows
    span_blocks = blocks_here + 2 * HALO
    position = lax.axis_index("leaf")

    local_ids = jnp.clip(
        near_pairs - (position * blocks_here - HALO), 0, span_blocks - 1
    ).reshape(-1).astype(jnp.int32)

    halos = []
    waited = ()
    for c in range(cases_here):
        head = features[c : c + 1, :halo_points]
        tail = features[c : c + 1, points_here - halo_points :]
        if waited:
            head, tail, _ = lax.optimization_barrier((head, tail, waited))
        from_prev = shifted(tail, "leaf", 1)
        from_next = shifted(head, "leaf", -1)
        halos.append((from_prev, from_next))
        waited = (from_prev, from_next)

    summary = jnp.einsum("rp,apc->arc", leaf_basis, features, preferred_element_type=jnp.float32)
    expansion, _ = expand(summary, translations, False)
    exp_bf = expansion.astype(jnp.bfloat16)
    far_coeff = jnp.einsum("arc,cd->ard", exp_bf, w_far, preferred_element_type=jnp.float32).astype(
        jnp.bfloat16
    )
    far_field = jnp.einsum("rp,ard->apd", leaf_basis, far_coeff, preferred_element_type=jnp.float32)

    near_parts, output_parts, slope_parts, scattered = [], [], [], []
    for c in range(cases_here):
        from_prev, from_next = halos[c]
        near_c = near_forward(local_ids, kernel_blocks, from_prev, features[c : c + 1], from_next)
        mixed = (
            jnp.einsum("apc,cd->apd", near_c, w_near, preferred_element_type=jnp.float32)
            + far_field[c : c + 1]
        )
        output_parts.append(jax.nn.gelu(mixed).astype(jnp.bfloat16))
        _, pullback = jax.vjp(jax.nn.gelu, mixed)
        slope_c = pullback(cotangent[c : c + 1].astype(jnp.float32))[0].astype(jnp.bfloat16)
        back_c = jnp.einsum(
            "apc,dc->apd", slope_c, w_near, preferred_element_type=jnp.float32
        ).astype(jnp.bfloat16)
        mid_c, lo_c, hi_c = near_backward(local_ids, kernel_blocks, back_c, halo_points)
        got_prev = shifted(hi_c, "leaf", 1).astype(jnp.float32)
        got_next = shifted(lo_c, "leaf", -1).astype(jnp.float32)
        scattered.append(
            jnp.concatenate(
                [
                    mid_c[:, :halo_points] + got_prev,
                    mid_c[:, halo_points : points_here - halo_points],
                    mid_c[:, points_here - halo_points :] + got_next,
                ],
                axis=1,
            )
        )
        near_parts.append(near_c)
        slope_parts.append(slope_c)
    near_bf = jnp.concatenate(near_parts, axis=0)
    slope = jnp.concatenate(slope_parts, axis=0)
    output = jnp.concatenate(output_parts, axis=0)

    projected = jnp.einsum(
        "rp,apc->arc", leaf_basis, slope, preferred_element_type=jnp.float32
    ).astype(jnp.bfloat16)
    scale = 1.0 / math.sqrt(
        cases_here * lax.axis_size("case") * points_here * lax.axis_size("leaf")
    )
    near_term = (
        jnp.einsum("apc,apd->cd", near_bf, slope, preferred_element_type=jnp.float32) * scale
    )
    far_term = (
        jnp.einsum("arc,ard->cd", exp_bf, projected, preferred_element_type=jnp.float32) * scale
    )
    grads = jnp.concatenate([near_term, far_term], axis=0)

    back_coeff = jnp.einsum("arc,dc->ard", projected, w_far, preferred_element_type=jnp.float32)
    back_exp, grads = expand(back_coeff, translations, True, rider=grads)
    back_far = jnp.einsum(
        "rp,arc->apc", leaf_basis, back_exp.astype(jnp.bfloat16), preferred_element_type=jnp.float32
    )

    case_depth = lax.axis_size("case").bit_length() - 1
    for height in range(case_depth):
        grads = grads + partner(grads, "case", height)

    near_back = jnp.concatenate(scattered, axis=0)
    grad_features = (near_back + back_far).astype(jnp.bfloat16)
    grad_near = grads[:width]
    grad_far = grads[width:]
    return (output, grad_features, grad_near, grad_far)


def solution(mesh):
    return jax.shard_map(
        on_device,
        mesh=mesh,
        in_specs=(
            P("case", "leaf", None),
            P("case", "leaf", None),
            P("leaf", None, None, None),
            P("leaf", None),
            P(None, "leaf"),
            P(),
            P(),
            P(),
        ),
        out_specs=(P("case", "leaf", None), P("case", "leaf", None), P(), P()),
        check_vma=False,
    )
```

```python
import functools
import math

import jax
import jax.numpy as jnp
from jax import lax
from jax.experimental import pallas as pl
from jax.experimental.pallas import tpu as pltpu
from jax.sharding import PartitionSpec as P

HALO = 8
TB = 8
BWD_TB = 4


def partner(shard, axis, apart):
    return lax.ppermute(shard, axis, [(i, i ^ 1 << apart) for i in range(lax.axis_size(axis))])


def shifted(value, axis, steps):
    count = lax.axis_size(axis)
    leading, last = (max(0, -steps), min(count, count - steps))
    return lax.ppermute(value, axis, [(source, source + steps) for source in range(leading, last)])


def apply_level(matrix, sibling, flipped):
    if flipped:
        return jnp.einsum("sr,asc->arc", matrix, sibling, precision=lax.Precision.HIGHEST)
    return jnp.einsum("rs,asc->arc", matrix, sibling, precision=lax.Precision.HIGHEST)


def expand(own_value, translations, flipped, rider=None, stages=()):
    depth_count = lax.axis_size("leaf").bit_length() - 1
    summed = jnp.zeros(own_value.shape, jnp.float32)
    node_value = own_value
    rows = own_value.shape[0] * own_value.shape[1]
    staged = None
    for height in range(depth_count):
        if rider is None:
            sibling = partner(node_value, "leaf", height)
        else:
            packed = jnp.concatenate(
                [node_value.reshape(rows, own_value.shape[2]), rider], axis=0
            )
            got = partner(packed, "leaf", height)
            if height < len(stages):
                staged = stages[height](staged)
                got, staged = lax.optimization_barrier((got, staged))
            sibling = got[:rows].reshape(own_value.shape)
            rider = rider + got[rows:]
        summed = summed + apply_level(translations[height], sibling, flipped)
        node_value = node_value + sibling
    if not stages:
        return summed, rider
    return summed, rider, staged


def near_fwd_kernel(cases, pairs, rows, ids_ref, kb_ref, prev_hbm, own_hbm, next_hbm, out_ref, ext_ref, sems):
    g = pl.program_id(0)
    halo_points = prev_hbm.shape[1]
    own_points = own_hbm.shape[1]

    @pl.when(g == 0)
    def _():
        copies = [
            pltpu.make_async_copy(prev_hbm, ext_ref.at[:, pl.ds(0, halo_points), :], sems.at[0]),
            pltpu.make_async_copy(own_hbm, ext_ref.at[:, pl.ds(halo_points, own_points), :], sems.at[1]),
            pltpu.make_async_copy(
                next_hbm, ext_ref.at[:, pl.ds(halo_points + own_points, halo_points), :], sems.at[2]
            ),
        ]
        for copy in copies:
            copy.start()
        for copy in copies:
            copy.wait()

    tbs = kb_ref.shape[0]
    for tb in range(tbs):
        t = g * tbs + tb
        lhs = jnp.concatenate([kb_ref[tb, k] for k in range(pairs)], axis=1)
        parts = []
        for k in range(pairs):
            start = pl.multiple_of(ids_ref[t * pairs + k] * rows, rows)
            parts.append(
                jnp.concatenate([ext_ref[c, pl.ds(start, rows), :] for c in range(cases)], axis=1)
            )
        rhs = jnp.concatenate(parts, axis=0)
        acc = jnp.dot(lhs, rhs, preferred_element_type=jnp.float32)
        width = acc.shape[1] // cases
        for c in range(cases):
            out_ref[c, pl.ds(tb * rows, rows), :] = acc[:, c * width : (c + 1) * width].astype(
                out_ref.dtype
            )


def near_forward(ids, kernel_blocks, from_prev, features, from_next):
    cases, points_here, width = features.shape
    span_points = points_here + from_prev.shape[1] + from_next.shape[1]
    blocks_here, pairs, rows, _ = kernel_blocks.shape
    steps = blocks_here // TB
    flops = 2 * blocks_here * pairs * rows * rows * cases * width
    hbm = pl.BlockSpec(memory_space=pl.ANY)
    return pl.pallas_call(
        functools.partial(near_fwd_kernel, cases, pairs, rows),
        out_shape=jax.ShapeDtypeStruct((cases, blocks_here * rows, width), jnp.bfloat16),
        grid_spec=pltpu.PrefetchScalarGridSpec(
            num_scalar_prefetch=1,
            grid=(steps,),
            in_specs=[
                pl.BlockSpec((TB, pairs, rows, rows), lambda g, ids: (g, 0, 0, 0)),
                hbm,
                hbm,
                hbm,
            ],
            out_specs=pl.BlockSpec((cases, TB * rows, width), lambda g, ids: (0, g, 0)),
            scratch_shapes=[
                pltpu.VMEM((cases, span_points, width), jnp.bfloat16),
                pltpu.SemaphoreType.DMA((3,)),
            ],
        ),
        compiler_params=pltpu.CompilerParams(dimension_semantics=("arbitrary",)),
        cost_estimate=pl.CostEstimate(
            flops=flops,
            transcendentals=0,
            bytes_accessed=kernel_blocks.size * 2 + cases * span_points * width * 2 + cases * blocks_here * rows * width * 2,
        ),
    )(ids, kernel_blocks, from_prev, features, from_next)


def near_bwd_kernel(cases, pairs, rows, steps, ids_ref, kb_ref, back_ref, mid_ref, lo_ref, hi_ref, acc_ref):
    g = pl.program_id(0)

    @pl.when(g == 0)
    def _():
        acc_ref[...] = jnp.zeros(acc_ref.shape, acc_ref.dtype)

    width = back_ref.shape[2]
    for tb in range(BWD_TB):
        t = g * BWD_TB + tb
        rhs = jnp.concatenate(
            [back_ref[c, pl.ds(tb * rows, rows), :] for c in range(cases)], axis=1
        )
        for k in range(pairs):
            start = pl.multiple_of(ids_ref[t * pairs + k] * rows, rows)
            piece = lax.dot_general(
                kb_ref[tb, k], rhs, (((0,), (0,)), ((), ())), preferred_element_type=jnp.float32
            )
            for c in range(cases):
                acc_ref[c, pl.ds(start, rows), :] += piece[:, c * width : (c + 1) * width]

    @pl.when(g == steps - 1)
    def _():
        halo_points = lo_ref.shape[1]
        mid_points = mid_ref.shape[1]
        lo_ref[...] = acc_ref[:, :halo_points, :].astype(lo_ref.dtype)
        mid_ref[...] = acc_ref[:, halo_points : halo_points + mid_points, :]
        hi_ref[...] = acc_ref[:, halo_points + mid_points :, :].astype(hi_ref.dtype)


def near_backward(ids, kernel_blocks, back_near, halo_points):
    cases, points_here, width = back_near.shape
    blocks_here, pairs, rows, _ = kernel_blocks.shape
    steps = blocks_here // BWD_TB
    span_points = points_here + 2 * halo_points
    flops = 2 * blocks_here * pairs * rows * rows * cases * width
    return pl.pallas_call(
        functools.partial(near_bwd_kernel, cases, pairs, rows, steps),
        out_shape=(
            jax.ShapeDtypeStruct((cases, points_here, width), jnp.float32),
            jax.ShapeDtypeStruct((cases, halo_points, width), jnp.bfloat16),
            jax.ShapeDtypeStruct((cases, halo_points, width), jnp.bfloat16),
        ),
        grid_spec=pltpu.PrefetchScalarGridSpec(
            num_scalar_prefetch=1,
            grid=(steps,),
            in_specs=[
                pl.BlockSpec((BWD_TB, pairs, rows, rows), lambda g, ids: (g, 0, 0, 0)),
                pl.BlockSpec((cases, BWD_TB * rows, width), lambda g, ids: (0, g, 0)),
            ],
            out_specs=[
                pl.BlockSpec((cases, points_here, width), lambda g, ids: (0, 0, 0)),
                pl.BlockSpec((cases, halo_points, width), lambda g, ids: (0, 0, 0)),
                pl.BlockSpec((cases, halo_points, width), lambda g, ids: (0, 0, 0)),
            ],
            scratch_shapes=[pltpu.VMEM((cases, span_points, width), jnp.float32)],
        ),
        compiler_params=pltpu.CompilerParams(
            dimension_semantics=("arbitrary",), vmem_limit_bytes=60 * 1024 * 1024
        ),
        cost_estimate=pl.CostEstimate(
            flops=flops,
            transcendentals=0,
            bytes_accessed=kernel_blocks.size * 2 + back_near.size * 2 + cases * span_points * width * 4,
        ),
    )(ids, kernel_blocks, back_near)


def on_device(
    features, cotangent, kernel_blocks, near_pairs, leaf_basis, w_near, w_far, translations
):
    cases_here, points_here, width = features.shape
    blocks_here, pair_count, block_rows = (
        kernel_blocks.shape[0],
        kernel_blocks.shape[1],
        kernel_blocks.shape[2],
    )
    halo_points = HALO * block_rows
    span_blocks = blocks_here + 2 * HALO
    position = lax.axis_index("leaf")

    head = features[:, :halo_points]
    tail = features[:, points_here - halo_points :]
    from_prev = shifted(tail, "leaf", 1)
    from_next = shifted(head, "leaf", -1)
    local_ids = jnp.clip(
        near_pairs - (position * blocks_here - HALO), 0, span_blocks - 1
    ).reshape(-1).astype(jnp.int32)

    near_bf = near_forward(local_ids, kernel_blocks, from_prev, features, from_next)

    summary = jnp.einsum("rp,apc->arc", leaf_basis, features, preferred_element_type=jnp.float32)
    expansion, _ = expand(summary, translations, False)
    exp_bf = expansion.astype(jnp.bfloat16)
    far_coeff = jnp.einsum("arc,cd->ard", exp_bf, w_far, preferred_element_type=jnp.float32).astype(
        jnp.bfloat16
    )
    far_field = jnp.einsum("rp,ard->apd", leaf_basis, far_coeff, preferred_element_type=jnp.float32)
    mixed = (
        jnp.einsum("apc,cd->apd", near_bf, w_near, preferred_element_type=jnp.float32) + far_field
    )
    output = jax.nn.gelu(mixed).astype(jnp.bfloat16)
    _, pullback = jax.vjp(jax.nn.gelu, mixed)
    slope = pullback(cotangent.astype(jnp.float32))[0].astype(jnp.bfloat16)
    projected = jnp.einsum(
        "rp,apc->arc", leaf_basis, slope, preferred_element_type=jnp.float32
    ).astype(jnp.bfloat16)
    back_near = jnp.einsum("apc,dc->apd", slope, w_near, preferred_element_type=jnp.float32).astype(
        jnp.bfloat16
    )


    scale = 1.0 / math.sqrt(
        cases_here * lax.axis_size("case") * points_here * lax.axis_size("leaf")
    )
    near_term = (
        jnp.einsum("apc,apd->cd", near_bf, slope, preferred_element_type=jnp.float32) * scale
    )
    far_term = (
        jnp.einsum("arc,ard->cd", exp_bf, projected, preferred_element_type=jnp.float32) * scale
    )
    grads = jnp.concatenate([near_term, far_term], axis=0)

    back_coeff = jnp.einsum("arc,dc->ard", projected, w_far, preferred_element_type=jnp.float32)
    back_exp, grads, (mid, lo, hi) = expand(
        back_coeff,
        translations,
        True,
        rider=grads,
        stages=(
            lambda _: back_near,
            lambda ready: near_backward(local_ids, kernel_blocks, ready, halo_points),
        ),
    )
    back_far = jnp.einsum(
        "rp,arc->apc", leaf_basis, back_exp.astype(jnp.bfloat16), preferred_element_type=jnp.float32
    )

    case_depth = lax.axis_size("case").bit_length() - 1
    for height in range(case_depth):
        grads = grads + partner(grads, "case", height)

    got_prev = shifted(hi, "leaf", 1).astype(jnp.float32)
    got_next = shifted(lo, "leaf", -1).astype(jnp.float32)
    near_back = jnp.concatenate(
        [
            mid[:, :halo_points] + got_prev,
            mid[:, halo_points : points_here - halo_points],
            mid[:, points_here - halo_points :] + got_next,
        ],
        axis=1,
    )
    grad_features = (near_back + back_far).astype(jnp.bfloat16)
    grad_near = grads[:width]
    grad_far = grads[width:]
    return (output, grad_features, grad_near, grad_far)


def solution(mesh):
    return jax.shard_map(
        on_device,
        mesh=mesh,
        in_specs=(
            P("case", "leaf", None),
            P("case", "leaf", None),
            P("leaf", None, None, None),
            P("leaf", None),
            P(None, "leaf"),
            P(),
            P(),
            P(),
        ),
        out_specs=(P("case", "leaf", None), P("case", "leaf", None), P(), P()),
        check_vma=False,
    )
```

```python
import functools
import math

import jax
import jax.numpy as jnp
from jax import lax
from jax.experimental import pallas as pl
from jax.experimental.pallas import tpu as pltpu
from jax.sharding import PartitionSpec as P

HALO = 8
TB = 8
BWD_TB = 4


def partner(shard, axis, apart):
    return lax.ppermute(shard, axis, [(i, i ^ 1 << apart) for i in range(lax.axis_size(axis))])


def shifted(value, axis, steps):
    count = lax.axis_size(axis)
    leading, last = (max(0, -steps), min(count, count - steps))
    return lax.ppermute(value, axis, [(source, source + steps) for source in range(leading, last)])


def apply_level(matrix, sibling, flipped):
    if flipped:
        return jnp.einsum("sr,asc->arc", matrix, sibling, precision=lax.Precision.HIGHEST)
    return jnp.einsum("rs,asc->arc", matrix, sibling, precision=lax.Precision.HIGHEST)


def expand(own_value, translations, flipped, rider=None, stages=()):
    depth_count = lax.axis_size("leaf").bit_length() - 1
    summed = jnp.zeros(own_value.shape, jnp.float32)
    node_value = own_value
    rows = own_value.shape[0] * own_value.shape[1]
    staged = None
    for height in range(depth_count):
        if rider is None:
            sibling = partner(node_value, "leaf", height)
        else:
            packed = jnp.concatenate(
                [node_value.reshape(rows, own_value.shape[2]), rider], axis=0
            )
            got = partner(packed, "leaf", height)
            if height < len(stages):
                staged = stages[height](staged)
                got, staged = lax.optimization_barrier((got, staged))
            sibling = got[:rows].reshape(own_value.shape)
            rider = rider + got[rows:]
        summed = summed + apply_level(translations[height], sibling, flipped)
        node_value = node_value + sibling
    if not stages:
        return summed, rider
    return summed, rider, staged


def near_fwd_kernel(cases, pairs, rows, ids_ref, kb_ref, prev_hbm, own_hbm, next_hbm, out_ref, ext_ref, sems):
    g = pl.program_id(0)
    halo_points = prev_hbm.shape[1]
    own_points = own_hbm.shape[1]

    @pl.when(g == 0)
    def _():
        copies = [
            pltpu.make_async_copy(prev_hbm, ext_ref.at[:, pl.ds(0, halo_points), :], sems.at[0]),
            pltpu.make_async_copy(own_hbm, ext_ref.at[:, pl.ds(halo_points, own_points), :], sems.at[1]),
            pltpu.make_async_copy(
                next_hbm, ext_ref.at[:, pl.ds(halo_points + own_points, halo_points), :], sems.at[2]
            ),
        ]
        for copy in copies:
            copy.start()
        for copy in copies:
            copy.wait()

    tbs = kb_ref.shape[0]
    for tb in range(tbs):
        t = g * tbs + tb
        lhs = jnp.concatenate([kb_ref[tb, k] for k in range(pairs)], axis=1)
        parts = []
        for k in range(pairs):
            start = pl.multiple_of(ids_ref[t * pairs + k] * rows, rows)
            parts.append(
                jnp.concatenate([ext_ref[c, pl.ds(start, rows), :] for c in range(cases)], axis=1)
            )
        rhs = jnp.concatenate(parts, axis=0)
        acc = jnp.dot(lhs, rhs, preferred_element_type=jnp.float32)
        width = acc.shape[1] // cases
        for c in range(cases):
            out_ref[c, pl.ds(tb * rows, rows), :] = acc[:, c * width : (c + 1) * width].astype(
                out_ref.dtype
            )


def near_forward(ids, kernel_blocks, from_prev, features, from_next):
    cases, points_here, width = features.shape
    span_points = points_here + from_prev.shape[1] + from_next.shape[1]
    blocks_here, pairs, rows, _ = kernel_blocks.shape
    steps = blocks_here // TB
    flops = 2 * blocks_here * pairs * rows * rows * cases * width
    hbm = pl.BlockSpec(memory_space=pl.ANY)
    return pl.pallas_call(
        functools.partial(near_fwd_kernel, cases, pairs, rows),
        out_shape=jax.ShapeDtypeStruct((cases, blocks_here * rows, width), jnp.bfloat16),
        grid_spec=pltpu.PrefetchScalarGridSpec(
            num_scalar_prefetch=1,
            grid=(steps,),
            in_specs=[
                pl.BlockSpec((TB, pairs, rows, rows), lambda g, ids: (g, 0, 0, 0)),
                hbm,
                hbm,
                hbm,
            ],
            out_specs=pl.BlockSpec((cases, TB * rows, width), lambda g, ids: (0, g, 0)),
            scratch_shapes=[
                pltpu.VMEM((cases, span_points, width), jnp.bfloat16),
                pltpu.SemaphoreType.DMA((3,)),
            ],
        ),
        compiler_params=pltpu.CompilerParams(dimension_semantics=("arbitrary",)),
        cost_estimate=pl.CostEstimate(
            flops=flops,
            transcendentals=0,
            bytes_accessed=kernel_blocks.size * 2 + cases * span_points * width * 2 + cases * blocks_here * rows * width * 2,
        ),
    )(ids, kernel_blocks, from_prev, features, from_next)


def near_bwd_kernel(cases, pairs, rows, steps, ids_ref, kb_ref, back_ref, mid_ref, lo_ref, hi_ref, acc_ref):
    g = pl.program_id(0)

    @pl.when(g == 0)
    def _():
        acc_ref[...] = jnp.zeros(acc_ref.shape, acc_ref.dtype)

    width = back_ref.shape[2]
    for tb in range(BWD_TB):
        t = g * BWD_TB + tb
        rhs = jnp.concatenate(
            [back_ref[c, pl.ds(tb * rows, rows), :] for c in range(cases)], axis=1
        )
        for k in range(pairs):
            start = pl.multiple_of(ids_ref[t * pairs + k] * rows, rows)
            piece = lax.dot_general(
                kb_ref[tb, k], rhs, (((0,), (0,)), ((), ())), preferred_element_type=jnp.float32
            )
            for c in range(cases):
                acc_ref[c, pl.ds(start, rows), :] += piece[:, c * width : (c + 1) * width]

    @pl.when(g == steps - 1)
    def _():
        halo_points = lo_ref.shape[1]
        mid_points = mid_ref.shape[1]
        lo_ref[...] = acc_ref[:, :halo_points, :].astype(lo_ref.dtype)
        mid_ref[...] = acc_ref[:, halo_points : halo_points + mid_points, :]
        hi_ref[...] = acc_ref[:, halo_points + mid_points :, :].astype(hi_ref.dtype)


def near_backward(ids, kernel_blocks, back_near, halo_points):
    cases, points_here, width = back_near.shape
    blocks_here, pairs, rows, _ = kernel_blocks.shape
    steps = blocks_here // BWD_TB
    span_points = points_here + 2 * halo_points
    flops = 2 * blocks_here * pairs * rows * rows * cases * width
    return pl.pallas_call(
        functools.partial(near_bwd_kernel, cases, pairs, rows, steps),
        out_shape=(
            jax.ShapeDtypeStruct((cases, points_here, width), jnp.float32),
            jax.ShapeDtypeStruct((cases, halo_points, width), jnp.bfloat16),
            jax.ShapeDtypeStruct((cases, halo_points, width), jnp.bfloat16),
        ),
        grid_spec=pltpu.PrefetchScalarGridSpec(
            num_scalar_prefetch=1,
            grid=(steps,),
            in_specs=[
                pl.BlockSpec((BWD_TB, pairs, rows, rows), lambda g, ids: (g, 0, 0, 0)),
                pl.BlockSpec((cases, BWD_TB * rows, width), lambda g, ids: (0, g, 0)),
            ],
            out_specs=[
                pl.BlockSpec((cases, points_here, width), lambda g, ids: (0, 0, 0)),
                pl.BlockSpec((cases, halo_points, width), lambda g, ids: (0, 0, 0)),
                pl.BlockSpec((cases, halo_points, width), lambda g, ids: (0, 0, 0)),
            ],
            scratch_shapes=[pltpu.VMEM((cases, span_points, width), jnp.float32)],
        ),
        compiler_params=pltpu.CompilerParams(
            dimension_semantics=("arbitrary",), vmem_limit_bytes=60 * 1024 * 1024
        ),
        cost_estimate=pl.CostEstimate(
            flops=flops,
            transcendentals=0,
            bytes_accessed=kernel_blocks.size * 2 + back_near.size * 2 + cases * span_points * width * 4,
        ),
    )(ids, kernel_blocks, back_near)


def on_device(
    features, cotangent, kernel_blocks, near_pairs, leaf_basis, w_near, w_far, translations
):
    cases_here, points_here, width = features.shape
    blocks_here, pair_count, block_rows = (
        kernel_blocks.shape[0],
        kernel_blocks.shape[1],
        kernel_blocks.shape[2],
    )
    halo_points = HALO * block_rows
    span_blocks = blocks_here + 2 * HALO
    position = lax.axis_index("leaf")

    head = features[:, :halo_points]
    tail = features[:, points_here - halo_points :]
    from_prev = shifted(tail, "leaf", 1)
    head, from_prev = lax.optimization_barrier((head, from_prev))
    from_next = shifted(head, "leaf", -1)
    local_ids = jnp.clip(
        near_pairs - (position * blocks_here - HALO), 0, span_blocks - 1
    ).reshape(-1).astype(jnp.int32)

    near_bf = near_forward(local_ids, kernel_blocks, from_prev, features, from_next)

    summary = jnp.einsum("rp,apc->arc", leaf_basis, features, preferred_element_type=jnp.float32)
    expansion, _ = expand(summary, translations, False)
    exp_bf = expansion.astype(jnp.bfloat16)
    far_coeff = jnp.einsum("arc,cd->ard", exp_bf, w_far, preferred_element_type=jnp.float32).astype(
        jnp.bfloat16
    )
    far_field = jnp.einsum("rp,ard->apd", leaf_basis, far_coeff, preferred_element_type=jnp.float32)
    mixed = (
        jnp.einsum("apc,cd->apd", near_bf, w_near, preferred_element_type=jnp.float32) + far_field
    )
    output = jax.nn.gelu(mixed).astype(jnp.bfloat16)
    _, pullback = jax.vjp(jax.nn.gelu, mixed)
    slope = pullback(cotangent.astype(jnp.float32))[0].astype(jnp.bfloat16)
    projected = jnp.einsum(
        "rp,apc->arc", leaf_basis, slope, preferred_element_type=jnp.float32
    ).astype(jnp.bfloat16)
    back_near = jnp.einsum("apc,dc->apd", slope, w_near, preferred_element_type=jnp.float32).astype(
        jnp.bfloat16
    )


    scale = 1.0 / math.sqrt(
        cases_here * lax.axis_size("case") * points_here * lax.axis_size("leaf")
    )
    near_term = (
        jnp.einsum("apc,apd->cd", near_bf, slope, preferred_element_type=jnp.float32) * scale
    )
    far_term = (
        jnp.einsum("arc,ard->cd", exp_bf, projected, preferred_element_type=jnp.float32) * scale
    )
    grads = jnp.concatenate([near_term, far_term], axis=0)

    back_coeff = jnp.einsum("arc,dc->ard", projected, w_far, preferred_element_type=jnp.float32)
    back_exp, grads, (mid, lo, hi) = expand(
        back_coeff,
        translations,
        True,
        rider=grads,
        stages=(
            lambda _: back_near,
            lambda ready: near_backward(local_ids, kernel_blocks, ready, halo_points),
        ),
    )
    back_far = jnp.einsum(
        "rp,arc->apc", leaf_basis, back_exp.astype(jnp.bfloat16), preferred_element_type=jnp.float32
    )

    case_depth = lax.axis_size("case").bit_length() - 1
    for height in range(case_depth):
        grads = grads + partner(grads, "case", height)

    got_prev = shifted(hi, "leaf", 1)
    lo, got_prev = lax.optimization_barrier((lo, got_prev))
    got_next = shifted(lo, "leaf", -1).astype(jnp.float32)
    got_prev = got_prev.astype(jnp.float32)
    near_back = jnp.concatenate(
        [
            mid[:, :halo_points] + got_prev,
            mid[:, halo_points : points_here - halo_points],
            mid[:, points_here - halo_points :] + got_next,
        ],
        axis=1,
    )
    grad_features = (near_back + back_far).astype(jnp.bfloat16)
    grad_near = grads[:width]
    grad_far = grads[width:]
    return (output, grad_features, grad_near, grad_far)


def solution(mesh):
    return jax.shard_map(
        on_device,
        mesh=mesh,
        in_specs=(
            P("case", "leaf", None),
            P("case", "leaf", None),
            P("leaf", None, None, None),
            P("leaf", None),
            P(None, "leaf"),
            P(),
            P(),
            P(),
        ),
        out_specs=(P("case", "leaf", None), P("case", "leaf", None), P(), P()),
        check_vma=False,
    )
```

```python
import functools
import math

import jax
import jax.numpy as jnp
from jax import lax
from jax.experimental import pallas as pl
from jax.experimental.pallas import tpu as pltpu
from jax.sharding import PartitionSpec as P

HALO = 8
TB = 8
BWD_TB = 4


def partner(shard, axis, apart):
    return lax.ppermute(shard, axis, [(i, i ^ 1 << apart) for i in range(lax.axis_size(axis))])


def shifted(value, axis, steps):
    count = lax.axis_size(axis)
    leading, last = (max(0, -steps), min(count, count - steps))
    return lax.ppermute(value, axis, [(source, source + steps) for source in range(leading, last)])


def case_sum(value):
    for height in range(lax.axis_size("case").bit_length() - 1):
        value = value + partner(value, "case", height)
    return value


def apply_level(matrix, sibling, flipped):
    if flipped:
        return jnp.einsum("sr,asc->arc", matrix, sibling, precision=lax.Precision.HIGHEST)
    return jnp.einsum("rs,asc->arc", matrix, sibling, precision=lax.Precision.HIGHEST)


def expand(own_value, translations, flipped, rider=None, stages=(), last_hook=None):
    depth_count = lax.axis_size("leaf").bit_length() - 1
    summed = jnp.zeros(own_value.shape, jnp.float32)
    node_value = own_value
    rows = own_value.shape[0] * own_value.shape[1]
    staged = None
    for height in range(depth_count):
        if rider is None:
            sibling = partner(node_value, "leaf", height)
        else:
            if last_hook is not None and height == depth_count - 1:
                rider = last_hook(rider)
            packed = jnp.concatenate(
                [node_value.reshape(rows, own_value.shape[2]), rider], axis=0
            )
            got = partner(packed, "leaf", height)
            if height < len(stages):
                staged = stages[height](staged)
                got, staged = lax.optimization_barrier((got, staged))
            sibling = got[:rows].reshape(own_value.shape)
            rider = rider + got[rows:]
        summed = summed + apply_level(translations[height], sibling, flipped)
        node_value = node_value + sibling
    if not stages:
        return summed, rider
    return summed, rider, staged


def near_fwd_kernel(cases, pairs, rows, ids_ref, kb_ref, prev_hbm, own_hbm, next_hbm, out_ref, ext_ref, sems):
    g = pl.program_id(0)
    halo_points = prev_hbm.shape[1]
    own_points = own_hbm.shape[1]

    @pl.when(g == 0)
    def _():
        copies = [
            pltpu.make_async_copy(prev_hbm, ext_ref.at[:, pl.ds(0, halo_points), :], sems.at[0]),
            pltpu.make_async_copy(own_hbm, ext_ref.at[:, pl.ds(halo_points, own_points), :], sems.at[1]),
            pltpu.make_async_copy(
                next_hbm, ext_ref.at[:, pl.ds(halo_points + own_points, halo_points), :], sems.at[2]
            ),
        ]
        for copy in copies:
            copy.start()
        for copy in copies:
            copy.wait()

    tbs = kb_ref.shape[0]
    for tb in range(tbs):
        t = g * tbs + tb
        lhs = jnp.concatenate([kb_ref[tb, k] for k in range(pairs)], axis=1)
        parts = []
        for k in range(pairs):
            start = pl.multiple_of(ids_ref[t * pairs + k] * rows, rows)
            parts.append(
                jnp.concatenate([ext_ref[c, pl.ds(start, rows), :] for c in range(cases)], axis=1)
            )
        rhs = jnp.concatenate(parts, axis=0)
        acc = jnp.dot(lhs, rhs, preferred_element_type=jnp.float32)
        width = acc.shape[1] // cases
        for c in range(cases):
            out_ref[c, pl.ds(tb * rows, rows), :] = acc[:, c * width : (c + 1) * width].astype(
                out_ref.dtype
            )


def near_forward(ids, kernel_blocks, from_prev, features, from_next):
    cases, points_here, width = features.shape
    span_points = points_here + from_prev.shape[1] + from_next.shape[1]
    blocks_here, pairs, rows, _ = kernel_blocks.shape
    steps = blocks_here // TB
    flops = 2 * blocks_here * pairs * rows * rows * cases * width
    hbm = pl.BlockSpec(memory_space=pl.ANY)
    return pl.pallas_call(
        functools.partial(near_fwd_kernel, cases, pairs, rows),
        out_shape=jax.ShapeDtypeStruct((cases, blocks_here * rows, width), jnp.bfloat16),
        grid_spec=pltpu.PrefetchScalarGridSpec(
            num_scalar_prefetch=1,
            grid=(steps,),
            in_specs=[
                pl.BlockSpec((TB, pairs, rows, rows), lambda g, ids: (g, 0, 0, 0)),
                hbm,
                hbm,
                hbm,
            ],
            out_specs=pl.BlockSpec((cases, TB * rows, width), lambda g, ids: (0, g, 0)),
            scratch_shapes=[
                pltpu.VMEM((cases, span_points, width), jnp.bfloat16),
                pltpu.SemaphoreType.DMA((3,)),
            ],
        ),
        compiler_params=pltpu.CompilerParams(dimension_semantics=("arbitrary",)),
        cost_estimate=pl.CostEstimate(
            flops=flops,
            transcendentals=0,
            bytes_accessed=kernel_blocks.size * 2 + cases * span_points * width * 2 + cases * blocks_here * rows * width * 2,
        ),
    )(ids, kernel_blocks, from_prev, features, from_next)


def near_bwd_kernel(cases, pairs, rows, steps, ids_ref, kb_ref, back_ref, mid_ref, lo_ref, hi_ref, acc_ref):
    g = pl.program_id(0)

    @pl.when(g == 0)
    def _():
        acc_ref[...] = jnp.zeros(acc_ref.shape, acc_ref.dtype)

    width = back_ref.shape[2]
    for tb in range(BWD_TB):
        t = g * BWD_TB + tb
        rhs = jnp.concatenate(
            [back_ref[c, pl.ds(tb * rows, rows), :] for c in range(cases)], axis=1
        )
        for k in range(pairs):
            start = pl.multiple_of(ids_ref[t * pairs + k] * rows, rows)
            piece = lax.dot_general(
                kb_ref[tb, k], rhs, (((0,), (0,)), ((), ())), preferred_element_type=jnp.float32
            )
            for c in range(cases):
                acc_ref[c, pl.ds(start, rows), :] += piece[:, c * width : (c + 1) * width]

    @pl.when(g == steps - 1)
    def _():
        halo_points = lo_ref.shape[1]
        mid_points = mid_ref.shape[1]
        lo_ref[...] = acc_ref[:, :halo_points, :].astype(lo_ref.dtype)
        mid_ref[...] = acc_ref[:, halo_points : halo_points + mid_points, :]
        hi_ref[...] = acc_ref[:, halo_points + mid_points :, :].astype(hi_ref.dtype)


def near_backward(ids, kernel_blocks, back_near, halo_points):
    cases, points_here, width = back_near.shape
    blocks_here, pairs, rows, _ = kernel_blocks.shape
    steps = blocks_here // BWD_TB
    span_points = points_here + 2 * halo_points
    flops = 2 * blocks_here * pairs * rows * rows * cases * width
    return pl.pallas_call(
        functools.partial(near_bwd_kernel, cases, pairs, rows, steps),
        out_shape=(
            jax.ShapeDtypeStruct((cases, points_here, width), jnp.float32),
            jax.ShapeDtypeStruct((cases, halo_points, width), jnp.bfloat16),
            jax.ShapeDtypeStruct((cases, halo_points, width), jnp.bfloat16),
        ),
        grid_spec=pltpu.PrefetchScalarGridSpec(
            num_scalar_prefetch=1,
            grid=(steps,),
            in_specs=[
                pl.BlockSpec((BWD_TB, pairs, rows, rows), lambda g, ids: (g, 0, 0, 0)),
                pl.BlockSpec((cases, BWD_TB * rows, width), lambda g, ids: (0, g, 0)),
            ],
            out_specs=[
                pl.BlockSpec((cases, points_here, width), lambda g, ids: (0, 0, 0)),
                pl.BlockSpec((cases, halo_points, width), lambda g, ids: (0, 0, 0)),
                pl.BlockSpec((cases, halo_points, width), lambda g, ids: (0, 0, 0)),
            ],
            scratch_shapes=[pltpu.VMEM((cases, span_points, width), jnp.float32)],
        ),
        compiler_params=pltpu.CompilerParams(
            dimension_semantics=("arbitrary",), vmem_limit_bytes=60 * 1024 * 1024
        ),
        cost_estimate=pl.CostEstimate(
            flops=flops,
            transcendentals=0,
            bytes_accessed=kernel_blocks.size * 2 + back_near.size * 2 + cases * span_points * width * 4,
        ),
    )(ids, kernel_blocks, back_near)


def on_device(
    features, cotangent, kernel_blocks, near_pairs, leaf_basis, w_near, w_far, translations
):
    cases_here, points_here, width = features.shape
    blocks_here, pair_count, block_rows = (
        kernel_blocks.shape[0],
        kernel_blocks.shape[1],
        kernel_blocks.shape[2],
    )
    halo_points = HALO * block_rows
    span_blocks = blocks_here + 2 * HALO
    position = lax.axis_index("leaf")

    head = features[:, :halo_points]
    tail = features[:, points_here - halo_points :]
    from_prev = shifted(tail, "leaf", 1)
    from_next = shifted(head, "leaf", -1)
    local_ids = jnp.clip(
        near_pairs - (position * blocks_here - HALO), 0, span_blocks - 1
    ).reshape(-1).astype(jnp.int32)

    near_bf = near_forward(local_ids, kernel_blocks, from_prev, features, from_next)

    summary = jnp.einsum("rp,apc->arc", leaf_basis, features, preferred_element_type=jnp.float32)
    expansion, _ = expand(summary, translations, False)
    exp_bf = expansion.astype(jnp.bfloat16)
    far_coeff = jnp.einsum("arc,cd->ard", exp_bf, w_far, preferred_element_type=jnp.float32).astype(
        jnp.bfloat16
    )
    far_field = jnp.einsum("rp,ard->apd", leaf_basis, far_coeff, preferred_element_type=jnp.float32)
    mixed = (
        jnp.einsum("apc,cd->apd", near_bf, w_near, preferred_element_type=jnp.float32) + far_field
    )
    output = jax.nn.gelu(mixed).astype(jnp.bfloat16)
    _, pullback = jax.vjp(jax.nn.gelu, mixed)
    slope = pullback(cotangent.astype(jnp.float32))[0].astype(jnp.bfloat16)
    projected = jnp.einsum(
        "rp,apc->arc", leaf_basis, slope, preferred_element_type=jnp.float32
    ).astype(jnp.bfloat16)
    back_near = jnp.einsum("apc,dc->apd", slope, w_near, preferred_element_type=jnp.float32).astype(
        jnp.bfloat16
    )


    scale = 1.0 / math.sqrt(
        cases_here * lax.axis_size("case") * points_here * lax.axis_size("leaf")
    )
    near_term = (
        jnp.einsum("apc,apd->cd", near_bf, slope, preferred_element_type=jnp.float32) * scale
    )
    far_term = (
        jnp.einsum("arc,ard->cd", exp_bf, projected, preferred_element_type=jnp.float32) * scale
    )
    grads = jnp.concatenate([near_term, far_term], axis=0)

    back_coeff = jnp.einsum("arc,dc->ard", projected, w_far, preferred_element_type=jnp.float32)
    back_exp, grads, (mid, lo, hi) = expand(
        back_coeff,
        translations,
        True,
        rider=grads,
        stages=(
            lambda _: back_near,
            lambda ready: near_backward(local_ids, kernel_blocks, ready, halo_points),
        ),
        last_hook=case_sum,
    )
    back_far = jnp.einsum(
        "rp,arc->apc", leaf_basis, back_exp.astype(jnp.bfloat16), preferred_element_type=jnp.float32
    )


    got_prev = shifted(hi, "leaf", 1).astype(jnp.float32)
    got_next = shifted(lo, "leaf", -1).astype(jnp.float32)
    near_back = jnp.concatenate(
        [
            mid[:, :halo_points] + got_prev,
            mid[:, halo_points : points_here - halo_points],
            mid[:, points_here - halo_points :] + got_next,
        ],
        axis=1,
    )
    grad_features = (near_back + back_far).astype(jnp.bfloat16)
    grad_near = grads[:width]
    grad_far = grads[width:]
    return (output, grad_features, grad_near, grad_far)


def solution(mesh):
    return jax.shard_map(
        on_device,
        mesh=mesh,
        in_specs=(
            P("case", "leaf", None),
            P("case", "leaf", None),
            P("leaf", None, None, None),
            P("leaf", None),
            P(None, "leaf"),
            P(),
            P(),
            P(),
        ),
        out_specs=(P("case", "leaf", None), P("case", "leaf", None), P(), P()),
        check_vma=False,
    )
```

```python
import functools
import math

import jax
import jax.numpy as jnp
from jax import lax
from jax.experimental import pallas as pl
from jax.experimental.pallas import tpu as pltpu
from jax.sharding import PartitionSpec as P

HALO = 8
TB = 8
BWD_TB = 4


def partner(shard, axis, apart):
    return lax.ppermute(shard, axis, [(i, i ^ 1 << apart) for i in range(lax.axis_size(axis))])


def shifted(value, axis, steps):
    count = lax.axis_size(axis)
    leading, last = (max(0, -steps), min(count, count - steps))
    return lax.ppermute(value, axis, [(source, source + steps) for source in range(leading, last)])


def apply_level(matrix, sibling, flipped):
    if flipped:
        return jnp.einsum("sr,asc->arc", matrix, sibling, precision=lax.Precision.HIGHEST)
    return jnp.einsum("rs,asc->arc", matrix, sibling, precision=lax.Precision.HIGHEST)


def expand(own_value, translations, flipped, rider=None, stages=()):
    depth_count = lax.axis_size("leaf").bit_length() - 1
    summed = jnp.zeros(own_value.shape, jnp.float32)
    node_value = own_value
    rows = own_value.shape[0] * own_value.shape[1]
    staged = None
    for height in range(depth_count):
        if rider is None:
            sibling = partner(node_value, "leaf", height)
        else:
            packed = jnp.concatenate(
                [node_value.reshape(rows, own_value.shape[2]), rider], axis=0
            )
            got = partner(packed, "leaf", height)
            if height < len(stages):
                staged = stages[height](staged)
                got, staged = lax.optimization_barrier((got, staged))
            sibling = got[:rows].reshape(own_value.shape)
            rider = rider + got[rows:]
        summed = summed + apply_level(translations[height], sibling, flipped)
        node_value = node_value + sibling
    if not stages:
        return summed, rider
    return summed, rider, staged


def near_fwd_kernel(cases, pairs, rows, ids_ref, kb_ref, prev_hbm, own_hbm, next_hbm, out_ref, ext_ref, sems):
    g = pl.program_id(0)
    halo_points = prev_hbm.shape[1]
    own_points = own_hbm.shape[1]

    @pl.when(g == 0)
    def _():
        copies = [
            pltpu.make_async_copy(prev_hbm, ext_ref.at[:, pl.ds(0, halo_points), :], sems.at[0]),
            pltpu.make_async_copy(own_hbm, ext_ref.at[:, pl.ds(halo_points, own_points), :], sems.at[1]),
            pltpu.make_async_copy(
                next_hbm, ext_ref.at[:, pl.ds(halo_points + own_points, halo_points), :], sems.at[2]
            ),
        ]
        for copy in copies:
            copy.start()
        for copy in copies:
            copy.wait()

    tbs = kb_ref.shape[0]
    for tb in range(tbs):
        t = g * tbs + tb
        lhs = jnp.concatenate([kb_ref[tb, k] for k in range(pairs)], axis=1)
        parts = []
        for k in range(pairs):
            start = pl.multiple_of(ids_ref[t * pairs + k] * rows, rows)
            parts.append(
                jnp.concatenate([ext_ref[c, pl.ds(start, rows), :] for c in range(cases)], axis=1)
            )
        rhs = jnp.concatenate(parts, axis=0)
        acc = jnp.dot(lhs, rhs, preferred_element_type=jnp.float32)
        width = acc.shape[1] // cases
        for c in range(cases):
            out_ref[c, pl.ds(tb * rows, rows), :] = acc[:, c * width : (c + 1) * width].astype(
                out_ref.dtype
            )


def near_forward(ids, kernel_blocks, from_prev, features, from_next):
    cases, points_here, width = features.shape
    span_points = points_here + from_prev.shape[1] + from_next.shape[1]
    blocks_here, pairs, rows, _ = kernel_blocks.shape
    steps = blocks_here // TB
    flops = 2 * blocks_here * pairs * rows * rows * cases * width
    hbm = pl.BlockSpec(memory_space=pl.ANY)
    return pl.pallas_call(
        functools.partial(near_fwd_kernel, cases, pairs, rows),
        out_shape=jax.ShapeDtypeStruct((cases, blocks_here * rows, width), jnp.bfloat16),
        grid_spec=pltpu.PrefetchScalarGridSpec(
            num_scalar_prefetch=1,
            grid=(steps,),
            in_specs=[
                pl.BlockSpec((TB, pairs, rows, rows), lambda g, ids: (g, 0, 0, 0)),
                hbm,
                hbm,
                hbm,
            ],
            out_specs=pl.BlockSpec((cases, TB * rows, width), lambda g, ids: (0, g, 0)),
            scratch_shapes=[
                pltpu.VMEM((cases, span_points, width), jnp.bfloat16),
                pltpu.SemaphoreType.DMA((3,)),
            ],
        ),
        compiler_params=pltpu.CompilerParams(dimension_semantics=("arbitrary",)),
        cost_estimate=pl.CostEstimate(
            flops=flops,
            transcendentals=0,
            bytes_accessed=kernel_blocks.size * 2 + cases * span_points * width * 2 + cases * blocks_here * rows * width * 2,
        ),
    )(ids, kernel_blocks, from_prev, features, from_next)


def near_bwd_kernel(cases, pairs, rows, steps, ids_ref, kb_ref, back_ref, mid_ref, lo_ref, hi_ref, acc_ref):
    g = pl.program_id(0)

    @pl.when(g == 0)
    def _():
        acc_ref[...] = jnp.zeros(acc_ref.shape, acc_ref.dtype)

    width = back_ref.shape[2]
    for tb in range(BWD_TB):
        t = g * BWD_TB + tb
        rhs = jnp.concatenate(
            [back_ref[c, pl.ds(tb * rows, rows), :] for c in range(cases)], axis=1
        )
        for k in range(pairs):
            start = pl.multiple_of(ids_ref[t * pairs + k] * rows, rows)
            piece = lax.dot_general(
                kb_ref[tb, k], rhs, (((0,), (0,)), ((), ())), preferred_element_type=jnp.float32
            )
            for c in range(cases):
                acc_ref[c, pl.ds(start, rows), :] += piece[:, c * width : (c + 1) * width]

    @pl.when(g == steps - 1)
    def _():
        halo_points = lo_ref.shape[1]
        mid_points = mid_ref.shape[1]
        lo_ref[...] = acc_ref[:, :halo_points, :].astype(lo_ref.dtype)
        mid_ref[...] = acc_ref[:, halo_points : halo_points + mid_points, :]
        hi_ref[...] = acc_ref[:, halo_points + mid_points :, :].astype(hi_ref.dtype)


def near_backward(ids, kernel_blocks, back_near, halo_points):
    cases, points_here, width = back_near.shape
    blocks_here, pairs, rows, _ = kernel_blocks.shape
    steps = blocks_here // BWD_TB
    span_points = points_here + 2 * halo_points
    flops = 2 * blocks_here * pairs * rows * rows * cases * width
    return pl.pallas_call(
        functools.partial(near_bwd_kernel, cases, pairs, rows, steps),
        out_shape=(
            jax.ShapeDtypeStruct((cases, points_here, width), jnp.float32),
            jax.ShapeDtypeStruct((cases, halo_points, width), jnp.bfloat16),
            jax.ShapeDtypeStruct((cases, halo_points, width), jnp.bfloat16),
        ),
        grid_spec=pltpu.PrefetchScalarGridSpec(
            num_scalar_prefetch=1,
            grid=(steps,),
            in_specs=[
                pl.BlockSpec((BWD_TB, pairs, rows, rows), lambda g, ids: (g, 0, 0, 0)),
                pl.BlockSpec((cases, BWD_TB * rows, width), lambda g, ids: (0, g, 0)),
            ],
            out_specs=[
                pl.BlockSpec((cases, points_here, width), lambda g, ids: (0, 0, 0)),
                pl.BlockSpec((cases, halo_points, width), lambda g, ids: (0, 0, 0)),
                pl.BlockSpec((cases, halo_points, width), lambda g, ids: (0, 0, 0)),
            ],
            scratch_shapes=[pltpu.VMEM((cases, span_points, width), jnp.float32)],
        ),
        compiler_params=pltpu.CompilerParams(
            dimension_semantics=("arbitrary",), vmem_limit_bytes=60 * 1024 * 1024
        ),
        cost_estimate=pl.CostEstimate(
            flops=flops,
            transcendentals=0,
            bytes_accessed=kernel_blocks.size * 2 + back_near.size * 2 + cases * span_points * width * 4,
        ),
    )(ids, kernel_blocks, back_near)


def on_device(
    features, cotangent, kernel_blocks, near_pairs, leaf_basis, w_near, w_far, translations
):
    cases_here, points_here, width = features.shape
    blocks_here, pair_count, block_rows = (
        kernel_blocks.shape[0],
        kernel_blocks.shape[1],
        kernel_blocks.shape[2],
    )
    halo_points = HALO * block_rows
    span_blocks = blocks_here + 2 * HALO
    position = lax.axis_index("leaf")

    head = features[:, :halo_points]
    tail = features[:, points_here - halo_points :]
    from_prev = shifted(tail, "leaf", 1)
    from_next = shifted(head, "leaf", -1)
    local_ids = jnp.clip(
        near_pairs - (position * blocks_here - HALO), 0, span_blocks - 1
    ).reshape(-1).astype(jnp.int32)

    near_bf = near_forward(local_ids, kernel_blocks, from_prev, features, from_next)

    summary = jnp.einsum("rp,apc->arc", leaf_basis, features, preferred_element_type=jnp.float32)
    expansion, _ = expand(summary, translations, False)
    exp_bf = expansion.astype(jnp.bfloat16)
    far_coeff = jnp.einsum("arc,cd->ard", exp_bf, w_far, preferred_element_type=jnp.float32).astype(
        jnp.bfloat16
    )
    far_field = jnp.einsum("rp,ard->apd", leaf_basis, far_coeff, preferred_element_type=jnp.float32)
    mixed = (
        jnp.einsum("apc,cd->apd", near_bf, w_near, preferred_element_type=jnp.float32) + far_field
    )
    output = jax.nn.gelu(mixed).astype(jnp.bfloat16)
    _, pullback = jax.vjp(jax.nn.gelu, mixed)
    slope = pullback(cotangent.astype(jnp.float32))[0].astype(jnp.bfloat16)
    projected = jnp.einsum(
        "rp,apc->arc", leaf_basis, slope, preferred_element_type=jnp.float32
    ).astype(jnp.bfloat16)
    back_near = jnp.einsum("apc,dc->apd", slope, w_near, preferred_element_type=jnp.float32).astype(
        jnp.bfloat16
    )


    scale = 1.0 / math.sqrt(
        cases_here * lax.axis_size("case") * points_here * lax.axis_size("leaf")
    )
    near_term = (
        jnp.einsum("apc,apd->cd", near_bf, slope, preferred_element_type=jnp.float32) * scale
    )
    far_term = (
        jnp.einsum("arc,ard->cd", exp_bf, projected, preferred_element_type=jnp.float32) * scale
    )
    grads = jnp.concatenate([near_term, far_term], axis=0)

    back_coeff = jnp.einsum("arc,dc->ard", projected, w_far, preferred_element_type=jnp.float32)
    back_exp, grads, (mid, lo, hi) = expand(
        back_coeff,
        translations,
        True,
        rider=grads,
        stages=(
            lambda _: back_near,
            lambda ready: near_backward(local_ids, kernel_blocks, ready, halo_points),
        ),
    )
    back_far = jnp.einsum(
        "rp,arc->apc", leaf_basis, back_exp.astype(jnp.bfloat16), preferred_element_type=jnp.float32
    )

    case_depth = lax.axis_size("case").bit_length() - 1
    for height in range(case_depth):
        grads = grads + partner(grads, "case", height)

    got_prev = shifted(hi, "leaf", 1).astype(jnp.float32)
    got_next = shifted(lo, "leaf", -1).astype(jnp.float32)
    base = lax.optimization_barrier(mid + back_far)
    near_back = jnp.concatenate(
        [
            base[:, :halo_points] + got_prev,
            base[:, halo_points : points_here - halo_points],
            base[:, points_here - halo_points :] + got_next,
        ],
        axis=1,
    )
    grad_features = near_back.astype(jnp.bfloat16)
    grad_near = grads[:width]
    grad_far = grads[width:]
    return (output, grad_features, grad_near, grad_far)


def solution(mesh):
    return jax.shard_map(
        on_device,
        mesh=mesh,
        in_specs=(
            P("case", "leaf", None),
            P("case", "leaf", None),
            P("leaf", None, None, None),
            P("leaf", None),
            P(None, "leaf"),
            P(),
            P(),
            P(),
        ),
        out_specs=(P("case", "leaf", None), P("case", "leaf", None), P(), P()),
        check_vma=False,
    )
```

```python
import functools
import math

import jax
import jax.numpy as jnp
from jax import lax
from jax.experimental import pallas as pl
from jax.experimental.pallas import tpu as pltpu
from jax.sharding import PartitionSpec as P

HALO = 8
TB = 8
BWD_TB = 4


def partner(shard, axis, apart):
    return lax.ppermute(shard, axis, [(i, i ^ 1 << apart) for i in range(lax.axis_size(axis))])


def shifted(value, axis, steps):
    count = lax.axis_size(axis)
    leading, last = (max(0, -steps), min(count, count - steps))
    return lax.ppermute(value, axis, [(source, source + steps) for source in range(leading, last)])


def apply_level(matrix, sibling, flipped):
    if flipped:
        return jnp.einsum("sr,asc->arc", matrix, sibling, precision=lax.Precision.HIGHEST)
    return jnp.einsum("rs,asc->arc", matrix, sibling, precision=lax.Precision.HIGHEST)


def expand(own_value, translations, flipped, rider=None, stages=()):
    depth_count = lax.axis_size("leaf").bit_length() - 1
    summed = jnp.zeros(own_value.shape, jnp.float32)
    node_value = own_value
    rows = own_value.shape[0] * own_value.shape[1]
    staged = None
    for height in range(depth_count):
        if rider is None:
            sibling = partner(node_value, "leaf", height)
        else:
            packed = jnp.concatenate(
                [node_value.reshape(rows, own_value.shape[2]), rider], axis=0
            )
            got = partner(packed, "leaf", height)
            if height < len(stages):
                staged = stages[height](staged)
                got, staged = lax.optimization_barrier((got, staged))
            sibling = got[:rows].reshape(own_value.shape)
            rider = rider + got[rows:]
        summed = summed + apply_level(translations[height], sibling, flipped)
        node_value = node_value + sibling
    if not stages:
        return summed, rider
    return summed, rider, staged


def near_fwd_kernel(cases, pairs, rows, ids_ref, kb_ref, prev_hbm, own_hbm, next_hbm, out_ref, ext_ref, sems):
    g = pl.program_id(0)
    halo_points = prev_hbm.shape[1]
    own_points = own_hbm.shape[1]

    @pl.when(g == 0)
    def _():
        copies = [
            pltpu.make_async_copy(prev_hbm, ext_ref.at[:, pl.ds(0, halo_points), :], sems.at[0]),
            pltpu.make_async_copy(own_hbm, ext_ref.at[:, pl.ds(halo_points, own_points), :], sems.at[1]),
            pltpu.make_async_copy(
                next_hbm, ext_ref.at[:, pl.ds(halo_points + own_points, halo_points), :], sems.at[2]
            ),
        ]
        for copy in copies:
            copy.start()
        for copy in copies:
            copy.wait()

    tbs = kb_ref.shape[0]
    for tb in range(tbs):
        t = g * tbs + tb
        lhs = jnp.concatenate([kb_ref[tb, k] for k in range(pairs)], axis=1)
        parts = []
        for k in range(pairs):
            start = pl.multiple_of(ids_ref[t * pairs + k] * rows, rows)
            parts.append(
                jnp.concatenate([ext_ref[c, pl.ds(start, rows), :] for c in range(cases)], axis=1)
            )
        rhs = jnp.concatenate(parts, axis=0)
        acc = jnp.dot(lhs, rhs, preferred_element_type=jnp.float32)
        width = acc.shape[1] // cases
        for c in range(cases):
            out_ref[c, pl.ds(tb * rows, rows), :] = acc[:, c * width : (c + 1) * width].astype(
                out_ref.dtype
            )


def near_forward(ids, kernel_blocks, from_prev, features, from_next):
    cases, points_here, width = features.shape
    span_points = points_here + from_prev.shape[1] + from_next.shape[1]
    blocks_here, pairs, rows, _ = kernel_blocks.shape
    steps = blocks_here // TB
    flops = 2 * blocks_here * pairs * rows * rows * cases * width
    hbm = pl.BlockSpec(memory_space=pl.ANY)
    return pl.pallas_call(
        functools.partial(near_fwd_kernel, cases, pairs, rows),
        out_shape=jax.ShapeDtypeStruct((cases, blocks_here * rows, width), jnp.bfloat16),
        grid_spec=pltpu.PrefetchScalarGridSpec(
            num_scalar_prefetch=1,
            grid=(steps,),
            in_specs=[
                pl.BlockSpec((TB, pairs, rows, rows), lambda g, ids: (g, 0, 0, 0)),
                hbm,
                pl.BlockSpec((cases, points_here, width), lambda g, ids: (0, 0, 0)),
                hbm,
            ],
            out_specs=pl.BlockSpec((cases, TB * rows, width), lambda g, ids: (0, g, 0)),
            scratch_shapes=[
                pltpu.VMEM((cases, span_points, width), jnp.bfloat16),
                pltpu.SemaphoreType.DMA((3,)),
            ],
        ),
        compiler_params=pltpu.CompilerParams(dimension_semantics=("arbitrary",)),
        cost_estimate=pl.CostEstimate(
            flops=flops,
            transcendentals=0,
            bytes_accessed=kernel_blocks.size * 2 + cases * span_points * width * 2 + cases * blocks_here * rows * width * 2,
        ),
    )(ids, kernel_blocks, from_prev, features, from_next)


def near_bwd_kernel(cases, pairs, rows, steps, ids_ref, kb_ref, back_ref, mid_ref, lo_ref, hi_ref, acc_ref):
    g = pl.program_id(0)

    @pl.when(g == 0)
    def _():
        acc_ref[...] = jnp.zeros(acc_ref.shape, acc_ref.dtype)

    width = back_ref.shape[2]
    for tb in range(BWD_TB):
        t = g * BWD_TB + tb
        rhs = jnp.concatenate(
            [back_ref[c, pl.ds(tb * rows, rows), :] for c in range(cases)], axis=1
        )
        for k in range(pairs):
            start = pl.multiple_of(ids_ref[t * pairs + k] * rows, rows)
            piece = lax.dot_general(
                kb_ref[tb, k], rhs, (((0,), (0,)), ((), ())), preferred_element_type=jnp.float32
            )
            for c in range(cases):
                acc_ref[c, pl.ds(start, rows), :] += piece[:, c * width : (c + 1) * width]

    @pl.when(g == steps - 1)
    def _():
        halo_points = lo_ref.shape[1]
        mid_points = mid_ref.shape[1]
        lo_ref[...] = acc_ref[:, :halo_points, :].astype(lo_ref.dtype)
        mid_ref[...] = acc_ref[:, halo_points : halo_points + mid_points, :]
        hi_ref[...] = acc_ref[:, halo_points + mid_points :, :].astype(hi_ref.dtype)


def near_backward(ids, kernel_blocks, back_near, halo_points):
    cases, points_here, width = back_near.shape
    blocks_here, pairs, rows, _ = kernel_blocks.shape
    steps = blocks_here // BWD_TB
    span_points = points_here + 2 * halo_points
    flops = 2 * blocks_here * pairs * rows * rows * cases * width
    return pl.pallas_call(
        functools.partial(near_bwd_kernel, cases, pairs, rows, steps),
        out_shape=(
            jax.ShapeDtypeStruct((cases, points_here, width), jnp.float32),
            jax.ShapeDtypeStruct((cases, halo_points, width), jnp.bfloat16),
            jax.ShapeDtypeStruct((cases, halo_points, width), jnp.bfloat16),
        ),
        grid_spec=pltpu.PrefetchScalarGridSpec(
            num_scalar_prefetch=1,
            grid=(steps,),
            in_specs=[
                pl.BlockSpec((BWD_TB, pairs, rows, rows), lambda g, ids: (g, 0, 0, 0)),
                pl.BlockSpec((cases, BWD_TB * rows, width), lambda g, ids: (0, g, 0)),
            ],
            out_specs=[
                pl.BlockSpec((cases, points_here, width), lambda g, ids: (0, 0, 0)),
                pl.BlockSpec((cases, halo_points, width), lambda g, ids: (0, 0, 0)),
                pl.BlockSpec((cases, halo_points, width), lambda g, ids: (0, 0, 0)),
            ],
            scratch_shapes=[pltpu.VMEM((cases, span_points, width), jnp.float32)],
        ),
        compiler_params=pltpu.CompilerParams(
            dimension_semantics=("arbitrary",), vmem_limit_bytes=60 * 1024 * 1024
        ),
        cost_estimate=pl.CostEstimate(
            flops=flops,
            transcendentals=0,
            bytes_accessed=kernel_blocks.size * 2 + back_near.size * 2 + cases * span_points * width * 4,
        ),
    )(ids, kernel_blocks, back_near)


def on_device(
    features, cotangent, kernel_blocks, near_pairs, leaf_basis, w_near, w_far, translations
):
    cases_here, points_here, width = features.shape
    blocks_here, pair_count, block_rows = (
        kernel_blocks.shape[0],
        kernel_blocks.shape[1],
        kernel_blocks.shape[2],
    )
    halo_points = HALO * block_rows
    span_blocks = blocks_here + 2 * HALO
    position = lax.axis_index("leaf")

    head = features[:, :halo_points]
    tail = features[:, points_here - halo_points :]
    from_prev = shifted(tail, "leaf", 1)
    from_next = shifted(head, "leaf", -1)
    local_ids = jnp.clip(
        near_pairs - (position * blocks_here - HALO), 0, span_blocks - 1
    ).reshape(-1).astype(jnp.int32)

    near_bf = near_forward(local_ids, kernel_blocks, from_prev, features, from_next)

    summary = jnp.einsum("rp,apc->arc", leaf_basis, features, preferred_element_type=jnp.float32)
    expansion, _ = expand(summary, translations, False)
    exp_bf = expansion.astype(jnp.bfloat16)
    far_coeff = jnp.einsum("arc,cd->ard", exp_bf, w_far, preferred_element_type=jnp.float32).astype(
        jnp.bfloat16
    )
    far_field = jnp.einsum("rp,ard->apd", leaf_basis, far_coeff, preferred_element_type=jnp.float32)
    mixed = (
        jnp.einsum("apc,cd->apd", near_bf, w_near, preferred_element_type=jnp.float32) + far_field
    )
    output = jax.nn.gelu(mixed).astype(jnp.bfloat16)
    _, pullback = jax.vjp(jax.nn.gelu, mixed)
    slope = pullback(cotangent.astype(jnp.float32))[0].astype(jnp.bfloat16)
    projected = jnp.einsum(
        "rp,apc->arc", leaf_basis, slope, preferred_element_type=jnp.float32
    ).astype(jnp.bfloat16)
    back_near = jnp.einsum("apc,dc->apd", slope, w_near, preferred_element_type=jnp.float32).astype(
        jnp.bfloat16
    )


    scale = 1.0 / math.sqrt(
        cases_here * lax.axis_size("case") * points_here * lax.axis_size("leaf")
    )
    near_term = (
        jnp.einsum("apc,apd->cd", near_bf, slope, preferred_element_type=jnp.float32) * scale
    )
    far_term = (
        jnp.einsum("arc,ard->cd", exp_bf, projected, preferred_element_type=jnp.float32) * scale
    )
    grads = jnp.concatenate([near_term, far_term], axis=0)

    back_coeff = jnp.einsum("arc,dc->ard", projected, w_far, preferred_element_type=jnp.float32)
    back_exp, grads, (mid, lo, hi) = expand(
        back_coeff,
        translations,
        True,
        rider=grads,
        stages=(
            lambda _: back_near,
            lambda ready: near_backward(local_ids, kernel_blocks, ready, halo_points),
        ),
    )
    back_far = jnp.einsum(
        "rp,arc->apc", leaf_basis, back_exp.astype(jnp.bfloat16), preferred_element_type=jnp.float32
    )

    case_depth = lax.axis_size("case").bit_length() - 1
    for height in range(case_depth):
        grads = grads + partner(grads, "case", height)

    got_prev = shifted(hi, "leaf", 1).astype(jnp.float32)
    got_next = shifted(lo, "leaf", -1).astype(jnp.float32)
    base = lax.optimization_barrier(mid + back_far)
    near_back = jnp.concatenate(
        [
            base[:, :halo_points] + got_prev,
            base[:, halo_points : points_here - halo_points],
            base[:, points_here - halo_points :] + got_next,
        ],
        axis=1,
    )
    grad_features = near_back.astype(jnp.bfloat16)
    grad_near = grads[:width]
    grad_far = grads[width:]
    return (output, grad_features, grad_near, grad_far)


def solution(mesh):
    return jax.shard_map(
        on_device,
        mesh=mesh,
        in_specs=(
            P("case", "leaf", None),
            P("case", "leaf", None),
            P("leaf", None, None, None),
            P("leaf", None),
            P(None, "leaf"),
            P(),
            P(),
            P(),
        ),
        out_specs=(P("case", "leaf", None), P("case", "leaf", None), P(), P()),
        check_vma=False,
    )
```

```python
import functools
import math

import jax
import jax.numpy as jnp
from jax import lax
from jax.experimental import pallas as pl
from jax.experimental.pallas import tpu as pltpu
from jax.sharding import PartitionSpec as P

HALO = 8
TB = 8
BWD_TB = 8


def partner(shard, axis, apart):
    return lax.ppermute(shard, axis, [(i, i ^ 1 << apart) for i in range(lax.axis_size(axis))])


def shifted(value, axis, steps):
    count = lax.axis_size(axis)
    leading, last = (max(0, -steps), min(count, count - steps))
    return lax.ppermute(value, axis, [(source, source + steps) for source in range(leading, last)])


def apply_level(matrix, sibling, flipped):
    if flipped:
        return jnp.einsum("sr,asc->arc", matrix, sibling, precision=lax.Precision.HIGHEST)
    return jnp.einsum("rs,asc->arc", matrix, sibling, precision=lax.Precision.HIGHEST)


def expand(own_value, translations, flipped, rider=None, stages=()):
    depth_count = lax.axis_size("leaf").bit_length() - 1
    summed = jnp.zeros(own_value.shape, jnp.float32)
    node_value = own_value
    rows = own_value.shape[0] * own_value.shape[1]
    staged = None
    for height in range(depth_count):
        if rider is None:
            sibling = partner(node_value, "leaf", height)
        else:
            packed = jnp.concatenate(
                [node_value.reshape(rows, own_value.shape[2]), rider], axis=0
            )
            got = partner(packed, "leaf", height)
            if height < len(stages):
                staged = stages[height](staged)
                got, staged = lax.optimization_barrier((got, staged))
            sibling = got[:rows].reshape(own_value.shape)
            rider = rider + got[rows:]
        summed = summed + apply_level(translations[height], sibling, flipped)
        node_value = node_value + sibling
    if not stages:
        return summed, rider
    return summed, rider, staged


def near_fwd_kernel(cases, pairs, rows, ids_ref, kb_ref, prev_hbm, own_hbm, next_hbm, out_ref, ext_ref, sems):
    g = pl.program_id(0)
    halo_points = prev_hbm.shape[1]
    own_points = own_hbm.shape[1]

    @pl.when(g == 0)
    def _():
        copies = [
            pltpu.make_async_copy(prev_hbm, ext_ref.at[:, pl.ds(0, halo_points), :], sems.at[0]),
            pltpu.make_async_copy(own_hbm, ext_ref.at[:, pl.ds(halo_points, own_points), :], sems.at[1]),
            pltpu.make_async_copy(
                next_hbm, ext_ref.at[:, pl.ds(halo_points + own_points, halo_points), :], sems.at[2]
            ),
        ]
        for copy in copies:
            copy.start()
        for copy in copies:
            copy.wait()

    tbs = kb_ref.shape[0]
    for tb in range(tbs):
        t = g * tbs + tb
        lhs = jnp.concatenate([kb_ref[tb, k] for k in range(pairs)], axis=1)
        parts = []
        for k in range(pairs):
            start = pl.multiple_of(ids_ref[t * pairs + k] * rows, rows)
            parts.append(
                jnp.concatenate([ext_ref[c, pl.ds(start, rows), :] for c in range(cases)], axis=1)
            )
        rhs = jnp.concatenate(parts, axis=0)
        acc = jnp.dot(lhs, rhs, preferred_element_type=jnp.float32)
        width = acc.shape[1] // cases
        for c in range(cases):
            out_ref[c, pl.ds(tb * rows, rows), :] = acc[:, c * width : (c + 1) * width].astype(
                out_ref.dtype
            )


def near_forward(ids, kernel_blocks, from_prev, features, from_next):
    cases, points_here, width = features.shape
    span_points = points_here + from_prev.shape[1] + from_next.shape[1]
    blocks_here, pairs, rows, _ = kernel_blocks.shape
    steps = blocks_here // TB
    flops = 2 * blocks_here * pairs * rows * rows * cases * width
    hbm = pl.BlockSpec(memory_space=pl.ANY)
    return pl.pallas_call(
        functools.partial(near_fwd_kernel, cases, pairs, rows),
        out_shape=jax.ShapeDtypeStruct((cases, blocks_here * rows, width), jnp.bfloat16),
        grid_spec=pltpu.PrefetchScalarGridSpec(
            num_scalar_prefetch=1,
            grid=(steps,),
            in_specs=[
                pl.BlockSpec((TB, pairs, rows, rows), lambda g, ids: (g, 0, 0, 0)),
                hbm,
                hbm,
                hbm,
            ],
            out_specs=pl.BlockSpec((cases, TB * rows, width), lambda g, ids: (0, g, 0)),
            scratch_shapes=[
                pltpu.VMEM((cases, span_points, width), jnp.bfloat16),
                pltpu.SemaphoreType.DMA((3,)),
            ],
        ),
        compiler_params=pltpu.CompilerParams(dimension_semantics=("arbitrary",)),
        cost_estimate=pl.CostEstimate(
            flops=flops,
            transcendentals=0,
            bytes_accessed=kernel_blocks.size * 2 + cases * span_points * width * 2 + cases * blocks_here * rows * width * 2,
        ),
    )(ids, kernel_blocks, from_prev, features, from_next)


def near_bwd_kernel(cases, pairs, rows, steps, ids_ref, kb_ref, back_ref, mid_ref, lo_ref, hi_ref, acc_ref):
    g = pl.program_id(0)

    @pl.when(g == 0)
    def _():
        acc_ref[...] = jnp.zeros(acc_ref.shape, acc_ref.dtype)

    width = back_ref.shape[2]
    for tb in range(BWD_TB):
        t = g * BWD_TB + tb
        rhs = jnp.concatenate(
            [back_ref[c, pl.ds(tb * rows, rows), :] for c in range(cases)], axis=1
        )
        for k in range(pairs):
            start = pl.multiple_of(ids_ref[t * pairs + k] * rows, rows)
            piece = lax.dot_general(
                kb_ref[tb, k], rhs, (((0,), (0,)), ((), ())), preferred_element_type=jnp.float32
            )
            for c in range(cases):
                acc_ref[c, pl.ds(start, rows), :] += piece[:, c * width : (c + 1) * width]

    @pl.when(g == steps - 1)
    def _():
        halo_points = lo_ref.shape[1]
        mid_points = mid_ref.shape[1]
        lo_ref[...] = acc_ref[:, :halo_points, :].astype(lo_ref.dtype)
        mid_ref[...] = acc_ref[:, halo_points : halo_points + mid_points, :]
        hi_ref[...] = acc_ref[:, halo_points + mid_points :, :].astype(hi_ref.dtype)


def near_backward(ids, kernel_blocks, back_near, halo_points):
    cases, points_here, width = back_near.shape
    blocks_here, pairs, rows, _ = kernel_blocks.shape
    steps = blocks_here // BWD_TB
    span_points = points_here + 2 * halo_points
    flops = 2 * blocks_here * pairs * rows * rows * cases * width
    return pl.pallas_call(
        functools.partial(near_bwd_kernel, cases, pairs, rows, steps),
        out_shape=(
            jax.ShapeDtypeStruct((cases, points_here, width), jnp.float32),
            jax.ShapeDtypeStruct((cases, halo_points, width), jnp.bfloat16),
            jax.ShapeDtypeStruct((cases, halo_points, width), jnp.bfloat16),
        ),
        grid_spec=pltpu.PrefetchScalarGridSpec(
            num_scalar_prefetch=1,
            grid=(steps,),
            in_specs=[
                pl.BlockSpec((BWD_TB, pairs, rows, rows), lambda g, ids: (g, 0, 0, 0)),
                pl.BlockSpec((cases, BWD_TB * rows, width), lambda g, ids: (0, g, 0)),
            ],
            out_specs=[
                pl.BlockSpec((cases, points_here, width), lambda g, ids: (0, 0, 0)),
                pl.BlockSpec((cases, halo_points, width), lambda g, ids: (0, 0, 0)),
                pl.BlockSpec((cases, halo_points, width), lambda g, ids: (0, 0, 0)),
            ],
            scratch_shapes=[pltpu.VMEM((cases, span_points, width), jnp.float32)],
        ),
        compiler_params=pltpu.CompilerParams(
            dimension_semantics=("arbitrary",), vmem_limit_bytes=60 * 1024 * 1024
        ),
        cost_estimate=pl.CostEstimate(
            flops=flops,
            transcendentals=0,
            bytes_accessed=kernel_blocks.size * 2 + back_near.size * 2 + cases * span_points * width * 4,
        ),
    )(ids, kernel_blocks, back_near)


def on_device(
    features, cotangent, kernel_blocks, near_pairs, leaf_basis, w_near, w_far, translations
):
    cases_here, points_here, width = features.shape
    blocks_here, pair_count, block_rows = (
        kernel_blocks.shape[0],
        kernel_blocks.shape[1],
        kernel_blocks.shape[2],
    )
    halo_points = HALO * block_rows
    span_blocks = blocks_here + 2 * HALO
    position = lax.axis_index("leaf")

    head = features[:, :halo_points]
    tail = features[:, points_here - halo_points :]
    from_prev = shifted(tail, "leaf", 1)
    from_next = shifted(head, "leaf", -1)
    local_ids = jnp.clip(
        near_pairs - (position * blocks_here - HALO), 0, span_blocks - 1
    ).reshape(-1).astype(jnp.int32)

    near_bf = near_forward(local_ids, kernel_blocks, from_prev, features, from_next)

    summary = jnp.einsum("rp,apc->arc", leaf_basis, features, preferred_element_type=jnp.float32)
    expansion, _ = expand(summary, translations, False)
    exp_bf = expansion.astype(jnp.bfloat16)
    far_coeff = jnp.einsum("arc,cd->ard", exp_bf, w_far, preferred_element_type=jnp.float32).astype(
        jnp.bfloat16
    )
    far_field = jnp.einsum("rp,ard->apd", leaf_basis, far_coeff, preferred_element_type=jnp.float32)
    mixed = (
        jnp.einsum("apc,cd->apd", near_bf, w_near, preferred_element_type=jnp.float32) + far_field
    )
    output = jax.nn.gelu(mixed).astype(jnp.bfloat16)
    _, pullback = jax.vjp(jax.nn.gelu, mixed)
    slope = pullback(cotangent.astype(jnp.float32))[0].astype(jnp.bfloat16)
    projected = jnp.einsum(
        "rp,apc->arc", leaf_basis, slope, preferred_element_type=jnp.float32
    ).astype(jnp.bfloat16)
    back_near = jnp.einsum("apc,dc->apd", slope, w_near, preferred_element_type=jnp.float32).astype(
        jnp.bfloat16
    )


    scale = 1.0 / math.sqrt(
        cases_here * lax.axis_size("case") * points_here * lax.axis_size("leaf")
    )
    near_term = (
        jnp.einsum("apc,apd->cd", near_bf, slope, preferred_element_type=jnp.float32) * scale
    )
    far_term = (
        jnp.einsum("arc,ard->cd", exp_bf, projected, preferred_element_type=jnp.float32) * scale
    )
    grads = jnp.concatenate([near_term, far_term], axis=0)

    back_coeff = jnp.einsum("arc,dc->ard", projected, w_far, preferred_element_type=jnp.float32)
    back_exp, grads, (mid, lo, hi) = expand(
        back_coeff,
        translations,
        True,
        rider=grads,
        stages=(
            lambda _: back_near,
            lambda ready: near_backward(local_ids, kernel_blocks, ready, halo_points),
        ),
    )
    back_far = jnp.einsum(
        "rp,arc->apc", leaf_basis, back_exp.astype(jnp.bfloat16), preferred_element_type=jnp.float32
    )

    case_depth = lax.axis_size("case").bit_length() - 1
    for height in range(case_depth):
        grads = grads + partner(grads, "case", height)

    got_prev = shifted(hi, "leaf", 1).astype(jnp.float32)
    got_next = shifted(lo, "leaf", -1).astype(jnp.float32)
    base = lax.optimization_barrier(mid + back_far)
    near_back = jnp.concatenate(
        [
            base[:, :halo_points] + got_prev,
            base[:, halo_points : points_here - halo_points],
            base[:, points_here - halo_points :] + got_next,
        ],
        axis=1,
    )
    grad_features = near_back.astype(jnp.bfloat16)
    grad_near = grads[:width]
    grad_far = grads[width:]
    return (output, grad_features, grad_near, grad_far)


def solution(mesh):
    return jax.shard_map(
        on_device,
        mesh=mesh,
        in_specs=(
            P("case", "leaf", None),
            P("case", "leaf", None),
            P("leaf", None, None, None),
            P("leaf", None),
            P(None, "leaf"),
            P(),
            P(),
            P(),
        ),
        out_specs=(P("case", "leaf", None), P("case", "leaf", None), P(), P()),
        check_vma=False,
    )
```
